256 devices in a mesh: req: 32 (over x_hi, z, core), mlp: 8 (over x_lo, y).
Axes of the slice: x: 4 (x_hi: 2, x_lo: 2; x = x_hi * 2 + x_lo), y: 4, z: 8, core: 2. Of those that a mesh axis runs over, the one named last changes fastest.
Arguments:
- tokens: bfloat16 [768, 1536], P('req')
- lengths: int32 [768], replicated, may hold values from 1 to 16384, as said below
- leaving: int32 [32, 13], replicated, may hold values from 0 to 23, as said below
- owner: int32 [32, 13], replicated, may hold values from 0 to 31, as said below
- cache: bfloat16 [768, 1024, 256], P('req', 'mlp'), as said below
- conv_state: bfloat16 [768, 3, 2048], P('req', None, 'mlp'), may hold values from -6 to 6
- lru_state: bfloat16 [768, 2048], P('req', 'mlp'), may hold values from -6 to 6
- gain_rec: float32 [1536], replicated, may hold values from 0.25 to 1.75
- w_input: bfloat16 [1536, 2048], P(None, 'mlp'), may hold values from -0.15625 to 0.15625
- w_branch: bfloat16 [1536, 2048], P(None, 'mlp'), may hold values from -0.15625 to 0.15625
- conv_weight: float32 [4, 2048], P(None, 'mlp'), may hold values from -3 to 3
- conv_bias: float32 [2048], P('mlp'), may hold values from -3 to 3
- gate_weight: bfloat16 [2, 16, 128, 128], P(None, 'mlp'), may hold values from -0.5 to 0.5
- gate_bias: float32 [2, 2048], P(None, 'mlp'), may hold values from -4 to 4
- decay_param: float32 [2048], P('mlp'), may hold values from 1 to 6
- w_rec_out: bfloat16 [2048, 1536], P('mlp'), may hold values from -0.125 to 0.125
- gain_att: float32 [1536], replicated, may hold values from 0.25 to 1.75
- w_query: bfloat16 [1536, 1536], P('mlp'), may hold values from -0.15625 to 0.15625
- w_keyval: bfloat16 [1536, 256], replicated, may hold values from -0.15625 to 0.15625
- w_attn_out: bfloat16 [1536, 1536], P('mlp'), may hold values from -0.25 to 0.25
- gain_mlp: float32 [1536], replicated, may hold values from 0.25 to 1.75
- w_gate: bfloat16 [1536, 4608], P(None, 'mlp'), may hold values from -0.15625 to 0.15625
- w_up: bfloat16 [1536, 4608], P(None, 'mlp'), may hold values from -0.15625 to 0.15625
- w_down: bfloat16 [4608, 1536], P('mlp'), may hold values from -0.09375 to 0.09375
Outputs:
- hidden_out: bfloat16 [768, 1536], P('req', 'mlp')
- cache_out: bfloat16 [768, 1024, 256], P('req', 'mlp')
- conv_out: bfloat16 [768, 3, 2048], P('req', None, 'mlp')
- lru_out: bfloat16 [768, 2048], P('req', 'mlp')
The draws below stay inside these ranges and needn't reach their ends.
Inputs may be any that keep to these rules, and one draw needn't show every extreme that they name: lengths[0] is 16384 and lengths[1] is 1. `leaving`: row d holds 13 different slot numbers within req index d. `owner`: each row holds 13 different req indices, none equal to the row's own index, and each column holds every req index once. `cache`: keys are stored already rotated for the positions they hold.
All inputs are finite; a program needn't handle non-finite values.
Results may differ from the reference program's by a relative error of at most 0.03.
Values may be sent and summed in bfloat16 or wider, within the bound.
No kernel may reach another device: no remote copies, remote signals or barrier semaphores. Data moves between devices by JAX's collectives and lax.ppermute only.
A program may use at most 128 MiB of HBM per device.

```python
import math
import jax
import jax.numpy as jnp
from jax import lax

D = 1536
R = 2048
FF = 4608
HD = 128
HEADS = 12
BLOCK = 128
CONV = 4
WINDOW = 1024
MAXLEN = 16384
REQ_DEV = 24
MOVE = 13
SLOTS = 768
N_REQ = 32


def draw_tokens(key, part):
    key_vals, key_rows, key_cols = jax.random.split(jax.random.fold_in(key, 11), 3)
    base_vals = jax.random.normal(key_vals, (SLOTS, D), jnp.float32)
    row_scale = jnp.exp(jax.random.uniform(key_rows, (SLOTS, 1), jnp.float32, -1.15, 1.15))
    col_scale = jnp.exp(jax.random.uniform(key_cols, (1, D), jnp.float32, -1.15, 1.15))
    return (base_vals * row_scale * col_scale).astype(jnp.bfloat16)


def draw_lengths(key, part):
    key_first, key_second, key_third = jax.random.split(jax.random.fold_in(key, 23), 3)
    first_draw = jax.random.randint(key_first, (SLOTS,), 0, MAXLEN)
    second_draw = jax.random.randint(key_second, (SLOTS,), 0, MAXLEN)
    third_draw = jax.random.randint(key_third, (SLOTS,), 0, MAXLEN)
    product = first_draw * second_draw // MAXLEN
    product = product * third_draw // MAXLEN
    lengths_all = 1 + product
    lengths_all = lengths_all.at[0].set(MAXLEN).at[1].set(1)
    return lengths_all.astype(jnp.int32)


def draw_leaving(key, part):
    groups = SLOTS // REQ_DEV
    tickets = jax.random.randint(jax.random.fold_in(key, 37), (groups, REQ_DEV), 0, 1 << 20) * REQ_DEV + jnp.arange(REQ_DEV)[None, :]
    return jnp.argsort(tickets, axis=1)[:, :MOVE].astype(jnp.int32)


def draw_owner(key, part):
    groups = SLOTS // REQ_DEV
    key_perm, key_shift = jax.random.split(jax.random.fold_in(key, 53))
    tickets = jax.random.randint(key_perm, (groups,), 0, 1 << 20) * groups + jnp.arange(groups)
    ordering = jnp.argsort(tickets)
    inverse = jnp.argsort(ordering)
    shift_tickets = jax.random.randint(key_shift, (groups - 1,), 0, 1 << 20) * (groups - 1) + jnp.arange(groups - 1)
    shifts = 1 + jnp.argsort(shift_tickets)[:MOVE]
    return ordering[(inverse[:, None] + shifts[None, :]) % groups].astype(jnp.int32)


def draw_cache(key, part):
    key_keys = jax.random.fold_in(jax.random.fold_in(key, 71), 0)
    key_vals = jax.random.fold_in(jax.random.fold_in(key, 71), 2)
    key_common = jax.random.fold_in(jax.random.fold_in(key, 71), 4)
    along = jnp.arange(WINDOW, dtype=jnp.float32)[None, :, None] / (WINDOW - 1)
    keys_part = 2.0 * jax.random.normal(key_keys, (SLOTS, WINDOW, HD), jnp.float32)
    common = jax.random.normal(key_common, (SLOTS, 1, HD), jnp.float32)
    rising = 0.3 * jnp.exp(along * 2.3026)
    values_part = (jax.random.normal(key_vals, (SLOTS, WINDOW, HD), jnp.float32) + common) * rising
    return jnp.concatenate([keys_part, values_part], axis=-1).astype(jnp.bfloat16)


def steps_of(stream_key, shape, shards, smallest, top_value):
    gain, own = 1.0, jax.random.fold_in(stream_key, 6)
    for axis_at, shards_of in shards:
        heights = jnp.exp(jax.random.uniform(jax.random.fold_in(own, axis_at), (shards_of,), jnp.float32, smallest / len(shards), top_value / len(shards)))
        gain = gain * jnp.repeat(heights, shape[axis_at] // shards_of).reshape([-1 if axis == axis_at else 1 for axis in range(len(shape))])
    return gain


def noise(stream_key, dims, spread, limit, pieces=(), kind=jnp.bfloat16):
    values = spread * jax.random.normal(stream_key, dims, jnp.float32)
    if pieces:
        values = values * steps_of(stream_key, dims, pieces, -0.22, 0.18)
    return jnp.clip(values, -limit, limit).astype(kind)


def setup_inputs(seed: int = 0) -> dict:
    key_of = jax.random.split(jax.random.key(seed), 25)
    tokens = draw_tokens(jax.random.fold_in(key_of[24], 71), 0)
    lengths = draw_lengths(jax.random.fold_in(key_of[24], 71), 0)
    leaving = draw_leaving(jax.random.fold_in(key_of[24], 71), 0)
    owner = draw_owner(jax.random.fold_in(key_of[24], 71), 0)
    cache = draw_cache(jax.random.fold_in(key_of[24], 71), 0)
    conv_state = noise(key_of[5], (SLOTS, CONV - 1, R), 1.0, 6.0, ((0, 32), (2, 8)))
    lru_state = noise(key_of[6], (SLOTS, R), 1.0, 6.0, ((0, 32), (1, 8)))
    gain_rec = jnp.clip(1.0 + 0.15 * jax.random.normal(key_of[7], (D,), jnp.float32), 0.25, 1.75)
    w_input = noise(key_of[8], (D, R), D ** -0.5, 0.15625, ((1, 8),))
    w_branch = noise(key_of[9], (D, R), D ** -0.5, 0.15625, ((1, 8),))
    conv_weight = noise(key_of[10], (CONV, R), CONV ** -0.5, 3.0, ((1, 8),), jnp.float32)
    conv_bias = noise(key_of[11], (R,), 0.5, 3.0, ((0, 8),), jnp.float32)
    gate_weight = noise(key_of[12], (2, R // BLOCK, BLOCK, BLOCK), BLOCK ** -0.5, 0.5, ((1, 8),))
    gate_bias = noise(key_of[13], (2, R), 1.0, 4.0, ((1, 8),), jnp.float32)
    decay_param = jnp.clip(1.0 + 5.0 * jax.random.uniform(key_of[14], (R,), jnp.float32) ** steps_of(key_of[14], (R,), ((0, 8),), -0.2, 0.2), 1.0, 6.0)
    w_rec_out = noise(key_of[15], (R, D), R ** -0.5, 0.125, ((0, 8),))
    gain_att = jnp.clip(1.0 + 0.15 * jax.random.normal(key_of[16], (D,), jnp.float32), 0.25, 1.75)
    w_query = noise(key_of[17], (D, D), D ** -0.5, 0.15625, ((0, 8),))
    w_keyval = noise(key_of[18], (D, 2 * HD), D ** -0.5, 0.15625)
    w_attn_out = noise(key_of[19], (D, D), (4 * HD) ** -0.5, 0.25, ((0, 8),))
    gain_mlp = jnp.clip(1.0 + 0.15 * jax.random.normal(key_of[20], (D,), jnp.float32), 0.25, 1.75)
    w_gate = noise(key_of[21], (D, FF), D ** -0.5, 0.15625, ((1, 8),))
    w_up = noise(key_of[22], (D, FF), D ** -0.5, 0.15625, ((1, 8),))
    w_down = noise(key_of[23], (FF, D), FF ** -0.5, 0.09375, ((0, 8),))
    return dict(tokens=tokens, lengths=lengths, leaving=leaving, owner=owner, cache=cache, conv_state=conv_state, lru_state=lru_state, gain_rec=gain_rec, w_input=w_input, w_branch=w_branch, conv_weight=conv_weight, conv_bias=conv_bias, gate_weight=gate_weight, gate_bias=gate_bias, decay_param=decay_param, w_rec_out=w_rec_out, gain_att=gain_att, w_query=w_query, w_keyval=w_keyval, w_attn_out=w_attn_out, gain_mlp=gain_mlp, w_gate=w_gate, w_up=w_up, w_down=w_down)


epsilon = 1e-06

def rms_norm(values, gain_vec):
    mean_square = lax.optimization_barrier(jnp.mean(values * values, axis=-1, keepdims=True))
    return (values * lax.rsqrt(mean_square + epsilon) * gain_vec).astype(jnp.bfloat16)

def rotate(vectors, positions):
    half_size = vectors.shape[-1] // 2
    frequency = 10000.0 ** (-2.0 * jnp.arange(half_size, dtype=jnp.float32) / vectors.shape[-1])
    angles = positions[:, None] * frequency[None, :]
    cos_part = jnp.cos(angles)[:, None, :]
    sin_part = jnp.sin(angles)[:, None, :]
    first_half = vectors[..., :half_size]
    second = vectors[..., half_size:]
    return jnp.concatenate([first_half * cos_part - second * sin_part, second * cos_part + first_half * sin_part], axis=-1)

def reference(tokens, lengths, leaving, owner, cache, conv_state, lru_state, gain_rec, w_input, w_branch, conv_weight, conv_bias, gate_weight, gate_bias, decay_param, w_rec_out, gain_att, w_query, w_keyval, w_attn_out, gain_mlp, w_gate, w_up, w_down):
    groups = N_REQ
    rank_ids = jnp.arange(MOVE, dtype=jnp.int32)
    source_slots = (jnp.arange(groups, dtype=jnp.int32)[:, None] * REQ_DEV + leaving).reshape(-1).astype(jnp.int32)
    target_slots = (owner * REQ_DEV + leaving[owner, rank_ids[None, :]]).reshape(-1).astype(jnp.int32)
    source_of = jnp.arange(SLOTS, dtype=jnp.int32).at[target_slots].set(source_slots)
    moved_cache = cache[source_of]
    moved_conv = conv_state[source_of]
    moved_lru = lru_state[source_of]
    position = lengths[source_of]
    inputs = tokens.astype(jnp.float32)
    normed = rms_norm(inputs, gain_rec)
    branch_in = jnp.dot(normed, w_input, preferred_element_type=jnp.float32).astype(jnp.bfloat16)
    branch = jax.nn.gelu(jnp.dot(normed, w_branch, preferred_element_type=jnp.float32), approximate=True)
    history = moved_conv.astype(jnp.float32)
    conv_in = lax.optimization_barrier(jnp.sum(conv_weight[:-1][None] * history, axis=1)) + conv_weight[-1] * branch_in.astype(jnp.float32) + conv_bias
    blocks = R // BLOCK
    gate_pre = jnp.einsum('snb,gnbc->gsnc', conv_in.reshape(SLOTS, blocks, BLOCK), gate_weight.astype(jnp.float32)).reshape(2, SLOTS, R) + gate_bias[:, None, :]
    rate_gate = jax.nn.sigmoid(gate_pre[0])
    admit_gate = jax.nn.sigmoid(gate_pre[1])
    log_decay = -8.0 * rate_gate * jax.nn.softplus(-decay_param)
    new_state = jnp.exp(log_decay) * moved_lru.astype(jnp.float32) + jnp.sqrt(-jnp.expm1(2.0 * log_decay)) * admit_gate * conv_in
    lru_out = new_state.astype(jnp.bfloat16)
    conv_out = jnp.concatenate([moved_conv[:, 1:], branch_in[:, None, :]], axis=1)
    gated_rec = (new_state * branch).astype(jnp.bfloat16)
    resid_one = inputs + jnp.dot(gated_rec, w_rec_out, preferred_element_type=jnp.float32)
    normed_att = rms_norm(resid_one, gain_att)
    where_pos = position.astype(jnp.float32)
    queries = rotate(jnp.dot(normed_att, w_query, preferred_element_type=jnp.float32).reshape(SLOTS, HEADS, HD), where_pos).astype(jnp.bfloat16)
    key_value = jnp.dot(normed_att, w_keyval, preferred_element_type=jnp.float32)
    key_new = rotate(key_value[:, None, :HD], where_pos)[:, 0].astype(jnp.bfloat16)
    value_new = key_value[:, HD:].astype(jnp.bfloat16)
    score_scale = 1.0 / math.sqrt(HD)
    query_wide = queries.astype(jnp.float32)
    scores = jnp.einsum('shd,swd->shw', query_wide, moved_cache[..., :HD].astype(jnp.float32)) * score_scale
    own_score = lax.optimization_barrier(jnp.sum(query_wide * key_new.astype(jnp.float32)[:, None, :], axis=-1)) * score_scale
    slot_ids = jnp.arange(WINDOW, dtype=jnp.int32)[None, :]
    current = position[:, None]
    held_pos = current - 1 - jnp.mod(current - 1 - slot_ids, WINDOW)
    usable = ((held_pos >= 0) & (held_pos != current - WINDOW))[:, None, :]
    top_score = jnp.maximum(lax.optimization_barrier(jnp.max(jnp.where(usable, scores, -1e+30), axis=-1)), own_score)
    weights = jnp.where(usable, jnp.exp(scores - top_score[..., None]), 0.0)
    own_weight = jnp.exp(own_score - top_score)
    denominator = lax.optimization_barrier(jnp.sum(weights, axis=-1)) + own_weight
    rounded = lax.optimization_barrier(weights.astype(jnp.bfloat16)).astype(jnp.float32)
    own_rounded = lax.optimization_barrier(own_weight.astype(jnp.bfloat16)).astype(jnp.float32)
    numerator = jnp.einsum('shw,swd->shd', rounded, moved_cache[..., HD:].astype(jnp.float32)) + own_rounded[..., None] * value_new.astype(jnp.float32)[:, None, :]
    attended = (numerator / denominator[..., None]).reshape(SLOTS, D).astype(jnp.bfloat16)
    resid_two = resid_one + jnp.dot(attended, w_attn_out, preferred_element_type=jnp.float32)
    normed_mlp = rms_norm(resid_two, gain_mlp)
    gate_act = jax.nn.gelu(jnp.dot(normed_mlp, w_gate, preferred_element_type=jnp.float32), approximate=True)
    hidden = (gate_act * jnp.dot(normed_mlp, w_up, preferred_element_type=jnp.float32)).astype(jnp.bfloat16)
    hidden_out = (resid_two + jnp.dot(hidden, w_down, preferred_element_type=jnp.float32)).astype(jnp.bfloat16)
    write_row = jnp.concatenate([key_new, value_new], axis=-1)
    row_hit = slot_ids == jnp.mod(current, WINDOW)
    cache_out = jnp.where(row_hit[:, :, None], write_row[:, None, :], moved_cache)
    return (hidden_out, cache_out, conv_out, lru_out)
```

```python
import math

import jax
import jax.numpy as jnp
from jax import lax
from jax.sharding import PartitionSpec as P

epsilon = 1e-06


def partner_swap(value, axis, bit):
    size = lax.axis_size(axis)
    pairs = [(j, j ^ bit) for j in range(size)]
    return jax.tree.map(lambda part: lax.ppermute(part, axis, pairs), value)


def axis_bits(axis):
    size = lax.axis_size(axis)
    assert size & (size - 1) == 0
    bits = []
    bit = 1
    while bit < size:
        bits.append(bit)
        bit *= 2
    return bits


def joined(value, axis, join):
    for bit in axis_bits(axis):
        value = join(value, partner_swap(value, axis, bit))
    return value


def scatter_sum(value, axis):
    size = lax.axis_size(axis)
    rows, cols = value.shape
    me = lax.axis_index(axis)
    held = value.reshape(rows, size, cols // size)
    for bit in reversed(axis_bits(axis)):
        half = held.shape[1] // 2
        lower, upper = held[:, :half], held[:, half:]
        mine_upper = (me & bit) != 0
        keep = jnp.where(mine_upper, upper, lower)
        send = jnp.where(mine_upper, lower, upper)
        held = keep + partner_swap(send, axis, bit)
    return held.reshape(rows, cols // size)


def rms_norm(values, gain_vec):
    mean_square = jnp.mean(values * values, axis=-1, keepdims=True)
    return (values * lax.rsqrt(mean_square + epsilon) * gain_vec).astype(jnp.bfloat16)


def rotate(vectors, positions):
    half_size = vectors.shape[-1] // 2
    frequency = 10000.0 ** (-2.0 * jnp.arange(half_size, dtype=jnp.float32) / vectors.shape[-1])
    angles = positions[:, None] * frequency[None, :]
    cos_part = jnp.cos(angles)[:, None, :]
    sin_part = jnp.sin(angles)[:, None, :]
    first_half = vectors[..., :half_size]
    second = vectors[..., half_size:]
    return jnp.concatenate(
        [first_half * cos_part - second * sin_part, second * cos_part + first_half * sin_part],
        axis=-1,
    )


def combine_parts(first_part, second_part):
    first_top, first_sum, first_acc = first_part
    second_top, second_sum, second_acc = second_part
    larger = jnp.maximum(first_top, second_top)
    first_factor = jnp.exp(first_top - larger)
    second_factor = jnp.exp(second_top - larger)
    return (
        larger,
        first_sum * first_factor + second_sum * second_factor,
        first_acc * first_factor[..., None] + second_acc * second_factor[..., None],
    )


def across_mlp(partial_value):
    return joined(partial_value, "mlp", lambda first, second: first + second)


def per_device(
    tokens,
    lengths,
    leaving,
    owner,
    cache,
    conv_state,
    lru_state,
    gain_rec,
    w_input,
    w_branch,
    conv_weight,
    conv_bias,
    gate_weight,
    gate_bias,
    decay_param,
    w_rec_out,
    gain_att,
    w_query,
    w_keyval,
    w_attn_out,
    gain_mlp,
    w_gate,
    w_up,
    w_down,
):
    req_rows = tokens.shape[0]
    width = tokens.shape[1]
    leavers = leaving.shape[1]
    groups = lax.axis_size("req")
    own_group = lax.axis_index("req")
    mlp_id = lax.axis_index("mlp")
    rank_ids = jnp.arange(leavers, dtype=jnp.int32)
    group_ids = jnp.arange(groups, dtype=jnp.int32)
    my_leave = leaving[own_group]
    anchor = jnp.sum(jnp.where(owner == own_group, group_ids[:, None], 0), axis=0)
    page_rows = cache.shape[1]
    conv_rows = conv_state.shape[1]
    combined = jnp.concatenate([cache, conv_state, lru_state[:, None, :]], axis=1)
    to_group = owner[own_group][None, :] == group_ids[:, None]
    send_slot = jnp.sum(jnp.where(to_group, my_leave[None, :], 0), axis=1)
    send = jnp.take(combined, send_slot, axis=0)
    got = lax.all_to_all(send, "req", 0, 0, tiled=True)
    local_ids = jnp.arange(req_rows, dtype=jnp.int32)
    match_slot = my_leave[None, :] == local_ids[:, None]
    arrive_rank = jnp.sum(jnp.where(match_slot, rank_ids[None, :], 0), axis=1)
    arriving = jnp.any(match_slot, axis=1)
    arrived = jnp.take(got, anchor[arrive_rank], axis=0)
    moved = jnp.where(arriving[:, None, None], arrived, combined)
    moved_cache = moved[:, :page_rows]
    moved_conv = moved[:, page_rows : page_rows + conv_rows]
    moved_lru = moved[:, page_rows + conv_rows]
    arrive_anchor = anchor[arrive_rank]
    anchor_slot = arrive_anchor * req_rows + leaving[arrive_anchor, arrive_rank]
    source_slot = jnp.where(arriving, anchor_slot, own_group * req_rows + local_ids)
    position = lengths[source_slot]
    inputs = tokens.astype(jnp.float32)
    normed = rms_norm(inputs, gain_rec)
    branch_in = jnp.dot(normed, w_input, preferred_element_type=jnp.float32).astype(jnp.bfloat16)
    branch = jax.nn.gelu(
        jnp.dot(normed, w_branch, preferred_element_type=jnp.float32), approximate=True
    )
    history = moved_conv.astype(jnp.float32)
    conv_in = (
        jnp.sum(conv_weight[:-1][None] * history, axis=1)
        + conv_weight[-1] * branch_in.astype(jnp.float32)
        + conv_bias
    )
    channels = conv_in.shape[1]
    block_size = gate_weight.shape[2]
    blocks = channels // block_size
    gate_pre = (
        jnp.einsum(
            "snb,gnbc->gsnc",
            conv_in.reshape(req_rows, blocks, block_size),
            gate_weight.astype(jnp.float32),
        ).reshape(2, req_rows, channels)
        + gate_bias[:, None, :]
    )
    rate_gate = jax.nn.sigmoid(gate_pre[0])
    admit_gate = jax.nn.sigmoid(gate_pre[1])
    log_decay = -8.0 * rate_gate * jax.nn.softplus(-decay_param)
    new_state = (
        jnp.exp(log_decay) * moved_lru.astype(jnp.float32)
        + jnp.sqrt(-jnp.expm1(2.0 * log_decay)) * admit_gate * conv_in
    )
    lru_out = new_state.astype(jnp.bfloat16)
    conv_out = jnp.concatenate([moved_conv[:, 1:], branch_in[:, None, :]], axis=1)
    gated_rec = (new_state * branch).astype(jnp.bfloat16)
    resid_one = inputs + across_mlp(
        jnp.dot(gated_rec, w_rec_out, preferred_element_type=jnp.float32)
    )
    head_size = w_keyval.shape[1] // 2
    heads = width // head_size
    slice_rows = w_query.shape[0]
    normed_att = rms_norm(resid_one, gain_att)
    query_part = jnp.dot(
        lax.dynamic_slice_in_dim(normed_att, mlp_id * slice_rows, slice_rows, 1),
        w_query,
        preferred_element_type=jnp.float32,
    )
    query_full = across_mlp(query_part)
    where_pos = position.astype(jnp.float32)
    queries = rotate(query_full.reshape(req_rows, heads, head_size), where_pos).astype(jnp.bfloat16)
    key_value = jnp.dot(normed_att, w_keyval, preferred_element_type=jnp.float32)
    key_new = rotate(key_value[:, None, :head_size], where_pos)[:, 0].astype(jnp.bfloat16)
    value_new = key_value[:, head_size:].astype(jnp.bfloat16)
    window = page_rows * lax.axis_size("mlp")
    score_scale = 1.0 / math.sqrt(head_size)
    scores = (
        jnp.einsum(
            "shd,swd->shw",
            queries,
            moved_cache[..., :head_size],
            preferred_element_type=jnp.float32,
        )
        * score_scale
    )
    slot_ids = mlp_id * page_rows + jnp.arange(page_rows, dtype=jnp.int32)[None, :]
    current = position[:, None]
    held_pos = current - 1 - jnp.mod(current - 1 - slot_ids, window)
    usable = ((held_pos >= 0) & (held_pos != current - window))[:, None, :]
    local_top = jnp.max(jnp.where(usable, scores, -1e30), axis=-1)
    weights = jnp.where(usable, jnp.exp(scores - local_top[..., None]), 0.0)
    local_sum = jnp.sum(weights, axis=-1)
    local_acc = jnp.einsum(
        "shw,swd->shd",
        weights.astype(jnp.bfloat16),
        moved_cache[..., head_size:],
        preferred_element_type=jnp.float32,
    )
    merged_top, merged_sum, merged_acc = joined(
        (local_top, local_sum, local_acc), "mlp", combine_parts
    )
    own_score = (
        jnp.sum(queries.astype(jnp.float32) * key_new.astype(jnp.float32)[:, None, :], axis=-1)
        * score_scale
    )
    top_score = jnp.maximum(merged_top, own_score)
    rescale = jnp.exp(merged_top - top_score)
    own_weight = jnp.exp(own_score - top_score)
    own_rounded = lax.optimization_barrier(own_weight.astype(jnp.bfloat16)).astype(jnp.float32)
    denominator = merged_sum * rescale + own_weight
    numerator = (
        merged_acc * rescale[..., None]
        + own_rounded[..., None] * value_new.astype(jnp.float32)[:, None, :]
    )
    attended = (numerator / denominator[..., None]).reshape(req_rows, width).astype(jnp.bfloat16)
    attn_part = jnp.dot(
        lax.dynamic_slice_in_dim(attended, mlp_id * slice_rows, slice_rows, 1),
        w_attn_out,
        preferred_element_type=jnp.float32,
    )
    resid_two = resid_one + across_mlp(attn_part)
    normed_mlp = rms_norm(resid_two, gain_mlp)
    gate_act = jax.nn.gelu(
        jnp.dot(normed_mlp, w_gate, preferred_element_type=jnp.float32), approximate=True
    )
    hidden = (gate_act * jnp.dot(normed_mlp, w_up, preferred_element_type=jnp.float32)).astype(
        jnp.bfloat16
    )
    down_part = jnp.dot(hidden, w_down, preferred_element_type=jnp.float32)
    share = scatter_sum(down_part, "mlp")
    share_cols = share.shape[1]
    hidden_out = (
        lax.dynamic_slice_in_dim(resid_two, mlp_id * share_cols, share_cols, 1) + share
    ).astype(jnp.bfloat16)
    write_row = jnp.concatenate([key_new, value_new], axis=-1)
    row_hit = slot_ids == jnp.mod(current, window)
    cache_out = jnp.where(row_hit[:, :, None], write_row[:, None, :], moved_cache)
    return (hidden_out, cache_out, conv_out, lru_out)


def solution(mesh):
    placed = (
        P("req", None),
        P(),
        P(),
        P(),
        P("req", "mlp", None),
        P("req", None, "mlp"),
        P("req", "mlp"),
        P(),
        P(None, "mlp"),
        P(None, "mlp"),
        P(None, "mlp"),
        P("mlp"),
        P(None, "mlp", None, None),
        P(None, "mlp"),
        P("mlp"),
        P("mlp", None),
        P(),
        P("mlp", None),
        P(),
        P("mlp", None),
        P(),
        P(None, "mlp"),
        P(None, "mlp"),
        P("mlp", None),
    )
    return jax.shard_map(
        per_device,
        mesh=mesh,
        in_specs=placed,
        out_specs=(P("req", "mlp"), P("req", "mlp", None), P("req", None, "mlp"), P("req", "mlp")),
        check_vma=False,
    )
```

```python
import math

import jax
import jax.numpy as jnp
from jax import lax
from jax.sharding import PartitionSpec as P

epsilon = 1e-06


def partner_swap(value, axis, bit):
    size = lax.axis_size(axis)
    pairs = [(j, j ^ bit) for j in range(size)]
    return jax.tree.map(lambda part: lax.ppermute(part, axis, pairs), value)


def axis_bits(axis):
    size = lax.axis_size(axis)
    assert size & (size - 1) == 0
    bits = []
    bit = 1
    while bit < size:
        bits.append(bit)
        bit *= 2
    return bits


def joined(value, axis, join):
    for bit in axis_bits(axis):
        value = join(value, partner_swap(value, axis, bit))
    return value


def scatter_sum(value, axis):
    size = lax.axis_size(axis)
    rows, cols = value.shape
    me = lax.axis_index(axis)
    held = value.reshape(rows, size, cols // size)
    for bit in reversed(axis_bits(axis)):
        half = held.shape[1] // 2
        lower, upper = held[:, :half], held[:, half:]
        mine_upper = (me & bit) != 0
        keep = jnp.where(mine_upper, upper, lower)
        send = jnp.where(mine_upper, lower, upper)
        held = keep + partner_swap(send, axis, bit)
    return held.reshape(rows, cols // size)


def rms_norm(values, gain_vec):
    mean_square = jnp.mean(values * values, axis=-1, keepdims=True)
    return (values * lax.rsqrt(mean_square + epsilon) * gain_vec).astype(jnp.bfloat16)


def rotate(vectors, positions):
    half_size = vectors.shape[-1] // 2
    frequency = 10000.0 ** (-2.0 * jnp.arange(half_size, dtype=jnp.float32) / vectors.shape[-1])
    angles = positions[:, None] * frequency[None, :]
    cos_part = jnp.cos(angles)[:, None, :]
    sin_part = jnp.sin(angles)[:, None, :]
    first_half = vectors[..., :half_size]
    second = vectors[..., half_size:]
    return jnp.concatenate(
        [first_half * cos_part - second * sin_part, second * cos_part + first_half * sin_part],
        axis=-1,
    )


def combine_parts(first_part, second_part):
    first_top, first_sum, first_acc = first_part
    second_top, second_sum, second_acc = second_part
    larger = jnp.maximum(first_top, second_top)
    first_factor = jnp.exp(first_top - larger)
    second_factor = jnp.exp(second_top - larger)
    return (
        larger,
        first_sum * first_factor + second_sum * second_factor,
        first_acc * first_factor[..., None] + second_acc * second_factor[..., None],
    )


def across_mlp(partial_value):
    return joined(partial_value, "mlp", lambda first, second: first + second)


def per_device(
    tokens,
    lengths,
    leaving,
    owner,
    cache,
    conv_state,
    lru_state,
    gain_rec,
    w_input,
    w_branch,
    conv_weight,
    conv_bias,
    gate_weight,
    gate_bias,
    decay_param,
    w_rec_out,
    gain_att,
    w_query,
    w_keyval,
    w_attn_out,
    gain_mlp,
    w_gate,
    w_up,
    w_down,
):
    req_rows = tokens.shape[0]
    width = tokens.shape[1]
    leavers = leaving.shape[1]
    groups = lax.axis_size("req")
    own_group = lax.axis_index("req")
    mlp_id = lax.axis_index("mlp")
    rank_ids = jnp.arange(leavers, dtype=jnp.int32)
    group_ids = jnp.arange(groups, dtype=jnp.int32)
    my_leave = leaving[own_group]
    anchor = jnp.sum(jnp.where(owner == own_group, group_ids[:, None], 0), axis=0)
    page_rows = cache.shape[1]
    conv_rows = conv_state.shape[1]
    states = jnp.concatenate([conv_state, lru_state[:, None, :]], axis=1)
    to_group = owner[own_group][None, :] == group_ids[:, None]
    send_slot = jnp.sum(jnp.where(to_group, my_leave[None, :], 0), axis=1)
    got_states = lax.all_to_all(jnp.take(states, send_slot, axis=0), "req", 0, 0, tiled=True)
    got_cache = lax.all_to_all(jnp.take(cache, send_slot, axis=0), "req", 0, 0, tiled=True)
    local_ids = jnp.arange(req_rows, dtype=jnp.int32)
    match_slot = my_leave[None, :] == local_ids[:, None]
    arrive_rank = jnp.sum(jnp.where(match_slot, rank_ids[None, :], 0), axis=1)
    arriving = jnp.any(match_slot, axis=1)
    arrive_from = anchor[arrive_rank]
    moved_states = jnp.where(
        arriving[:, None, None], jnp.take(got_states, arrive_from, axis=0), states
    )
    moved_cache = jnp.where(
        arriving[:, None, None], jnp.take(got_cache, arrive_from, axis=0), cache
    )
    moved_conv = moved_states[:, :conv_rows]
    moved_lru = moved_states[:, conv_rows]
    arrive_anchor = anchor[arrive_rank]
    anchor_slot = arrive_anchor * req_rows + leaving[arrive_anchor, arrive_rank]
    source_slot = jnp.where(arriving, anchor_slot, own_group * req_rows + local_ids)
    position = lengths[source_slot]
    inputs = tokens.astype(jnp.float32)
    normed = rms_norm(inputs, gain_rec)
    branch_in = jnp.dot(normed, w_input, preferred_element_type=jnp.float32).astype(jnp.bfloat16)
    branch = jax.nn.gelu(
        jnp.dot(normed, w_branch, preferred_element_type=jnp.float32), approximate=True
    )
    history = moved_conv.astype(jnp.float32)
    conv_in = (
        jnp.sum(conv_weight[:-1][None] * history, axis=1)
        + conv_weight[-1] * branch_in.astype(jnp.float32)
        + conv_bias
    )
    channels = conv_in.shape[1]
    block_size = gate_weight.shape[2]
    blocks = channels // block_size
    gate_pre = (
        jnp.einsum(
            "snb,gnbc->gsnc",
            conv_in.reshape(req_rows, blocks, block_size),
            gate_weight.astype(jnp.float32),
        ).reshape(2, req_rows, channels)
        + gate_bias[:, None, :]
    )
    rate_gate = jax.nn.sigmoid(gate_pre[0])
    admit_gate = jax.nn.sigmoid(gate_pre[1])
    log_decay = -8.0 * rate_gate * jax.nn.softplus(-decay_param)
    new_state = (
        jnp.exp(log_decay) * moved_lru.astype(jnp.float32)
        + jnp.sqrt(-jnp.expm1(2.0 * log_decay)) * admit_gate * conv_in
    )
    lru_out = new_state.astype(jnp.bfloat16)
    conv_out = jnp.concatenate([moved_conv[:, 1:], branch_in[:, None, :]], axis=1)
    gated_rec = (new_state * branch).astype(jnp.bfloat16)
    resid_one = inputs + across_mlp(
        jnp.dot(gated_rec, w_rec_out, preferred_element_type=jnp.float32)
    )
    head_size = w_keyval.shape[1] // 2
    heads = width // head_size
    slice_rows = w_query.shape[0]
    normed_att = rms_norm(resid_one, gain_att)
    query_part = jnp.dot(
        lax.dynamic_slice_in_dim(normed_att, mlp_id * slice_rows, slice_rows, 1),
        w_query,
        preferred_element_type=jnp.float32,
    )
    query_full = across_mlp(query_part)
    where_pos = position.astype(jnp.float32)
    queries = rotate(query_full.reshape(req_rows, heads, head_size), where_pos).astype(jnp.bfloat16)
    key_value = jnp.dot(normed_att, w_keyval, preferred_element_type=jnp.float32)
    key_new = rotate(key_value[:, None, :head_size], where_pos)[:, 0].astype(jnp.bfloat16)
    value_new = key_value[:, head_size:].astype(jnp.bfloat16)
    window = page_rows * lax.axis_size("mlp")
    score_scale = 1.0 / math.sqrt(head_size)
    scores = (
        jnp.einsum(
            "shd,swd->shw",
            queries,
            moved_cache[..., :head_size],
            preferred_element_type=jnp.float32,
        )
        * score_scale
    )
    slot_ids = mlp_id * page_rows + jnp.arange(page_rows, dtype=jnp.int32)[None, :]
    current = position[:, None]
    held_pos = current - 1 - jnp.mod(current - 1 - slot_ids, window)
    usable = ((held_pos >= 0) & (held_pos != current - window))[:, None, :]
    local_top = jnp.max(jnp.where(usable, scores, -1e30), axis=-1)
    weights = jnp.where(usable, jnp.exp(scores - local_top[..., None]), 0.0)
    local_sum = jnp.sum(weights, axis=-1)
    local_acc = jnp.einsum(
        "shw,swd->shd",
        weights.astype(jnp.bfloat16),
        moved_cache[..., head_size:],
        preferred_element_type=jnp.float32,
    )
    merged_top, merged_sum, merged_acc = joined(
        (local_top, local_sum, local_acc), "mlp", combine_parts
    )
    own_score = (
        jnp.sum(queries.astype(jnp.float32) * key_new.astype(jnp.float32)[:, None, :], axis=-1)
        * score_scale
    )
    top_score = jnp.maximum(merged_top, own_score)
    rescale = jnp.exp(merged_top - top_score)
    own_weight = jnp.exp(own_score - top_score)
    own_rounded = lax.optimization_barrier(own_weight.astype(jnp.bfloat16)).astype(jnp.float32)
    denominator = merged_sum * rescale + own_weight
    numerator = (
        merged_acc * rescale[..., None]
        + own_rounded[..., None] * value_new.astype(jnp.float32)[:, None, :]
    )
    attended = (numerator / denominator[..., None]).reshape(req_rows, width).astype(jnp.bfloat16)
    attn_part = jnp.dot(
        lax.dynamic_slice_in_dim(attended, mlp_id * slice_rows, slice_rows, 1),
        w_attn_out,
        preferred_element_type=jnp.float32,
    )
    resid_two = resid_one + across_mlp(attn_part)
    normed_mlp = rms_norm(resid_two, gain_mlp)
    gate_act = jax.nn.gelu(
        jnp.dot(normed_mlp, w_gate, preferred_element_type=jnp.float32), approximate=True
    )
    hidden = (gate_act * jnp.dot(normed_mlp, w_up, preferred_element_type=jnp.float32)).astype(
        jnp.bfloat16
    )
    down_part = jnp.dot(hidden, w_down, preferred_element_type=jnp.float32)
    share = scatter_sum(down_part, "mlp")
    share_cols = share.shape[1]
    hidden_out = (
        lax.dynamic_slice_in_dim(resid_two, mlp_id * share_cols, share_cols, 1) + share
    ).astype(jnp.bfloat16)
    write_row = jnp.concatenate([key_new, value_new], axis=-1)
    row_hit = slot_ids == jnp.mod(current, window)
    cache_out = jnp.where(row_hit[:, :, None], write_row[:, None, :], moved_cache)
    return (hidden_out, cache_out, conv_out, lru_out)


def solution(mesh):
    placed = (
        P("req", None),
        P(),
        P(),
        P(),
        P("req", "mlp", None),
        P("req", None, "mlp"),
        P("req", "mlp"),
        P(),
        P(None, "mlp"),
        P(None, "mlp"),
        P(None, "mlp"),
        P("mlp"),
        P(None, "mlp", None, None),
        P(None, "mlp"),
        P("mlp"),
        P("mlp", None),
        P(),
        P("mlp", None),
        P(),
        P("mlp", None),
        P(),
        P(None, "mlp"),
        P(None, "mlp"),
        P("mlp", None),
    )
    return jax.shard_map(
        per_device,
        mesh=mesh,
        in_specs=placed,
        out_specs=(P("req", "mlp"), P("req", "mlp", None), P("req", None, "mlp"), P("req", "mlp")),
        check_vma=False,
    )
```

```python
import math

import jax
import jax.numpy as jnp
from jax import lax
from jax.sharding import PartitionSpec as P

epsilon = 1e-06


def partner_swap(value, axis, bit):
    size = lax.axis_size(axis)
    pairs = [(j, j ^ bit) for j in range(size)]
    return jax.tree.map(lambda part: lax.ppermute(part, axis, pairs), value)


def axis_bits(axis):
    size = lax.axis_size(axis)
    assert size & (size - 1) == 0
    bits = []
    bit = 1
    while bit < size:
        bits.append(bit)
        bit *= 2
    return bits


def axis_stages(axis):
    stages = []
    for bit in axis_bits(axis):
        mask = bit | (bit // 2) if bit == 2 else bit
        stages.append((mask, bit))
    return stages


def joined(value, axis, join):
    for mask, _ in axis_stages(axis):
        value = join(value, partner_swap(value, axis, mask))
    return value


def scatter_sum(value, axis):
    size = lax.axis_size(axis)
    rows, cols = value.shape
    me = lax.axis_index(axis)
    held = value.reshape(rows, size, cols // size)
    for mask, bit in reversed(axis_stages(axis)):
        half = held.shape[1] // 2
        lower, upper = held[:, :half], held[:, half:]
        mine_upper = (me & bit) != 0
        keep = jnp.where(mine_upper, upper, lower)
        send = jnp.where(mine_upper, lower, upper)
        held = keep + partner_swap(send, axis, mask)
    return held.reshape(rows, cols // size)


def rms_norm(values, gain_vec):
    mean_square = jnp.mean(values * values, axis=-1, keepdims=True)
    return (values * lax.rsqrt(mean_square + epsilon) * gain_vec).astype(jnp.bfloat16)


def rotate(vectors, positions):
    half_size = vectors.shape[-1] // 2
    frequency = 10000.0 ** (-2.0 * jnp.arange(half_size, dtype=jnp.float32) / vectors.shape[-1])
    angles = positions[:, None] * frequency[None, :]
    cos_part = jnp.cos(angles)[:, None, :]
    sin_part = jnp.sin(angles)[:, None, :]
    first_half = vectors[..., :half_size]
    second = vectors[..., half_size:]
    return jnp.concatenate(
        [first_half * cos_part - second * sin_part, second * cos_part + first_half * sin_part],
        axis=-1,
    )


def combine_parts(first_part, second_part):
    head_size = first_part.shape[-1] - 2
    first_top, first_sum = first_part[..., head_size], first_part[..., head_size + 1]
    second_top, second_sum = second_part[..., head_size], second_part[..., head_size + 1]
    larger = jnp.maximum(first_top, second_top)
    first_factor = jnp.exp(first_top - larger)
    second_factor = jnp.exp(second_top - larger)
    return jnp.concatenate(
        [
            first_part[..., :head_size] * first_factor[..., None]
            + second_part[..., :head_size] * second_factor[..., None],
            larger[..., None],
            (first_sum * first_factor + second_sum * second_factor)[..., None],
        ],
        axis=-1,
    )


def across_mlp(partial_value):
    return joined(partial_value, "mlp", lambda first, second: first + second)


def per_device(
    tokens,
    lengths,
    leaving,
    owner,
    cache,
    conv_state,
    lru_state,
    gain_rec,
    w_input,
    w_branch,
    conv_weight,
    conv_bias,
    gate_weight,
    gate_bias,
    decay_param,
    w_rec_out,
    gain_att,
    w_query,
    w_keyval,
    w_attn_out,
    gain_mlp,
    w_gate,
    w_up,
    w_down,
):
    req_rows = tokens.shape[0]
    width = tokens.shape[1]
    leavers = leaving.shape[1]
    groups = lax.axis_size("req")
    own_group = lax.axis_index("req")
    mlp_id = lax.axis_index("mlp")
    rank_ids = jnp.arange(leavers, dtype=jnp.int32)
    group_ids = jnp.arange(groups, dtype=jnp.int32)
    my_leave = leaving[own_group]
    anchor = jnp.sum(jnp.where(owner == own_group, group_ids[:, None], 0), axis=0)
    page_rows = cache.shape[1]
    conv_rows = conv_state.shape[1]
    states = jnp.concatenate([conv_state, lru_state[:, None, :]], axis=1)
    to_group = owner[own_group][None, :] == group_ids[:, None]
    send_slot = jnp.sum(jnp.where(to_group, my_leave[None, :], 0), axis=1)
    got_states = lax.all_to_all(jnp.take(states, send_slot, axis=0), "req", 0, 0, tiled=True)
    got_cache = lax.all_to_all(jnp.take(cache, send_slot, axis=0), "req", 0, 0, tiled=True)
    local_ids = jnp.arange(req_rows, dtype=jnp.int32)
    match_slot = my_leave[None, :] == local_ids[:, None]
    arrive_rank = jnp.sum(jnp.where(match_slot, rank_ids[None, :], 0), axis=1)
    arriving = jnp.any(match_slot, axis=1)
    arrive_from = anchor[arrive_rank]
    moved_states = jnp.where(
        arriving[:, None, None], jnp.take(got_states, arrive_from, axis=0), states
    )
    moved_cache = jnp.where(
        arriving[:, None, None], jnp.take(got_cache, arrive_from, axis=0), cache
    )
    moved_conv = moved_states[:, :conv_rows]
    moved_lru = moved_states[:, conv_rows]
    arrive_anchor = anchor[arrive_rank]
    anchor_slot = arrive_anchor * req_rows + leaving[arrive_anchor, arrive_rank]
    source_slot = jnp.where(arriving, anchor_slot, own_group * req_rows + local_ids)
    position = lengths[source_slot]
    inputs = tokens.astype(jnp.float32)
    normed = rms_norm(inputs, gain_rec)
    branch_in = jnp.dot(normed, w_input, preferred_element_type=jnp.float32).astype(jnp.bfloat16)
    branch = jax.nn.gelu(
        jnp.dot(normed, w_branch, preferred_element_type=jnp.float32), approximate=True
    )
    history = moved_conv.astype(jnp.float32)
    conv_in = (
        jnp.sum(conv_weight[:-1][None] * history, axis=1)
        + conv_weight[-1] * branch_in.astype(jnp.float32)
        + conv_bias
    )
    channels = conv_in.shape[1]
    block_size = gate_weight.shape[2]
    blocks = channels // block_size
    gate_pre = (
        jnp.einsum(
            "snb,gnbc->gsnc",
            conv_in.reshape(req_rows, blocks, block_size),
            gate_weight.astype(jnp.float32),
        ).reshape(2, req_rows, channels)
        + gate_bias[:, None, :]
    )
    rate_gate = jax.nn.sigmoid(gate_pre[0])
    admit_gate = jax.nn.sigmoid(gate_pre[1])
    log_decay = -8.0 * rate_gate * jax.nn.softplus(-decay_param)
    new_state = (
        jnp.exp(log_decay) * moved_lru.astype(jnp.float32)
        + jnp.sqrt(-jnp.expm1(2.0 * log_decay)) * admit_gate * conv_in
    )
    lru_out = new_state.astype(jnp.bfloat16)
    conv_out = jnp.concatenate([moved_conv[:, 1:], branch_in[:, None, :]], axis=1)
    gated_rec = (new_state * branch).astype(jnp.bfloat16)
    resid_one = inputs + across_mlp(
        jnp.dot(gated_rec, w_rec_out, preferred_element_type=jnp.float32)
    )
    head_size = w_keyval.shape[1] // 2
    heads = width // head_size
    slice_rows = w_query.shape[0]
    normed_att = rms_norm(resid_one, gain_att)
    query_part = jnp.dot(
        lax.dynamic_slice_in_dim(normed_att, mlp_id * slice_rows, slice_rows, 1),
        w_query,
        preferred_element_type=jnp.float32,
    )
    query_full = across_mlp(query_part)
    where_pos = position.astype(jnp.float32)
    queries = rotate(query_full.reshape(req_rows, heads, head_size), where_pos).astype(jnp.bfloat16)
    key_value = jnp.dot(normed_att, w_keyval, preferred_element_type=jnp.float32)
    key_new = rotate(key_value[:, None, :head_size], where_pos)[:, 0].astype(jnp.bfloat16)
    value_new = key_value[:, head_size:].astype(jnp.bfloat16)
    window = page_rows * lax.axis_size("mlp")
    score_scale = 1.0 / math.sqrt(head_size)
    scores = (
        jnp.einsum(
            "shd,swd->shw",
            queries,
            moved_cache[..., :head_size],
            preferred_element_type=jnp.float32,
        )
        * score_scale
    )
    slot_ids = mlp_id * page_rows + jnp.arange(page_rows, dtype=jnp.int32)[None, :]
    current = position[:, None]
    held_pos = current - 1 - jnp.mod(current - 1 - slot_ids, window)
    usable = ((held_pos >= 0) & (held_pos != current - window))[:, None, :]
    local_top = jnp.max(jnp.where(usable, scores, -1e30), axis=-1)
    weights = jnp.where(usable, jnp.exp(scores - local_top[..., None]), 0.0)
    local_sum = jnp.sum(weights, axis=-1)
    local_acc = jnp.einsum(
        "shw,swd->shd",
        weights.astype(jnp.bfloat16),
        moved_cache[..., head_size:],
        preferred_element_type=jnp.float32,
    )
    merged = joined(
        jnp.concatenate([local_acc, local_top[..., None], local_sum[..., None]], axis=-1),
        "mlp",
        combine_parts,
    )
    merged_acc = merged[..., :head_size]
    merged_top = merged[..., head_size]
    merged_sum = merged[..., head_size + 1]
    own_score = (
        jnp.sum(queries.astype(jnp.float32) * key_new.astype(jnp.float32)[:, None, :], axis=-1)
        * score_scale
    )
    top_score = jnp.maximum(merged_top, own_score)
    rescale = jnp.exp(merged_top - top_score)
    own_weight = jnp.exp(own_score - top_score)
    own_rounded = lax.optimization_barrier(own_weight.astype(jnp.bfloat16)).astype(jnp.float32)
    denominator = merged_sum * rescale + own_weight
    numerator = (
        merged_acc * rescale[..., None]
        + own_rounded[..., None] * value_new.astype(jnp.float32)[:, None, :]
    )
    attended = (numerator / denominator[..., None]).reshape(req_rows, width).astype(jnp.bfloat16)
    attn_part = jnp.dot(
        lax.dynamic_slice_in_dim(attended, mlp_id * slice_rows, slice_rows, 1),
        w_attn_out,
        preferred_element_type=jnp.float32,
    )
    resid_two = resid_one + across_mlp(attn_part)
    normed_mlp = rms_norm(resid_two, gain_mlp)
    gate_act = jax.nn.gelu(
        jnp.dot(normed_mlp, w_gate, preferred_element_type=jnp.float32), approximate=True
    )
    hidden = (gate_act * jnp.dot(normed_mlp, w_up, preferred_element_type=jnp.float32)).astype(
        jnp.bfloat16
    )
    down_part = jnp.dot(hidden, w_down, preferred_element_type=jnp.float32)
    share = scatter_sum(down_part, "mlp")
    share_cols = share.shape[1]
    hidden_out = (
        lax.dynamic_slice_in_dim(resid_two, mlp_id * share_cols, share_cols, 1) + share
    ).astype(jnp.bfloat16)
    write_row = jnp.concatenate([key_new, value_new], axis=-1)
    row_hit = slot_ids == jnp.mod(current, window)
    cache_out = jnp.where(row_hit[:, :, None], write_row[:, None, :], moved_cache)
    return (hidden_out, cache_out, conv_out, lru_out)


def solution(mesh):
    placed = (
        P("req", None),
        P(),
        P(),
        P(),
        P("req", "mlp", None),
        P("req", None, "mlp"),
        P("req", "mlp"),
        P(),
        P(None, "mlp"),
        P(None, "mlp"),
        P(None, "mlp"),
        P("mlp"),
        P(None, "mlp", None, None),
        P(None, "mlp"),
        P("mlp"),
        P("mlp", None),
        P(),
        P("mlp", None),
        P(),
        P("mlp", None),
        P(),
        P(None, "mlp"),
        P(None, "mlp"),
        P("mlp", None),
    )
    return jax.shard_map(
        per_device,
        mesh=mesh,
        in_specs=placed,
        out_specs=(P("req", "mlp"), P("req", "mlp", None), P("req", None, "mlp"), P("req", "mlp")),
        check_vma=False,
    )
```

```python
import math

import jax
import jax.numpy as jnp
from jax import lax
from jax.sharding import PartitionSpec as P

epsilon = 1e-06


def partner_swap(value, axis, bit):
    size = lax.axis_size(axis)
    pairs = [(j, j ^ bit) for j in range(size)]
    return jax.tree.map(lambda part: lax.ppermute(part, axis, pairs), value)


def axis_bits(axis):
    size = lax.axis_size(axis)
    assert size & (size - 1) == 0
    bits = []
    bit = 1
    while bit < size:
        bits.append(bit)
        bit *= 2
    return bits


def axis_stages(axis):
    stages = []
    for bit in axis_bits(axis):
        mask = bit | (bit // 2) if bit == 2 else bit
        stages.append((mask, bit))
    return stages


def joined(value, axis, join):
    for mask, _ in axis_stages(axis):
        value = join(value, partner_swap(value, axis, mask))
    return value


def scatter_sum(value, axis):
    size = lax.axis_size(axis)
    rows, cols = value.shape
    me = lax.axis_index(axis)
    held = value.reshape(rows, size, cols // size)
    for mask, bit in reversed(axis_stages(axis)):
        half = held.shape[1] // 2
        lower, upper = held[:, :half], held[:, half:]
        mine_upper = (me & bit) != 0
        keep = jnp.where(mine_upper, upper, lower)
        send = jnp.where(mine_upper, lower, upper)
        held = keep + partner_swap(send.astype(jnp.bfloat16), axis, mask).astype(jnp.float32)
    return held.reshape(rows, cols // size)


def rms_norm(values, gain_vec):
    mean_square = jnp.mean(values * values, axis=-1, keepdims=True)
    return (values * lax.rsqrt(mean_square + epsilon) * gain_vec).astype(jnp.bfloat16)


def rotate(vectors, positions):
    half_size = vectors.shape[-1] // 2
    frequency = 10000.0 ** (-2.0 * jnp.arange(half_size, dtype=jnp.float32) / vectors.shape[-1])
    angles = positions[:, None] * frequency[None, :]
    cos_part = jnp.cos(angles)[:, None, :]
    sin_part = jnp.sin(angles)[:, None, :]
    first_half = vectors[..., :half_size]
    second = vectors[..., half_size:]
    return jnp.concatenate(
        [first_half * cos_part - second * sin_part, second * cos_part + first_half * sin_part],
        axis=-1,
    )


def combine_parts(first_part, second_part):
    width = first_part.shape[-1] - 128
    heads = width // 128
    first_top, first_sum = first_part[:, width : width + heads], first_part[:, width + heads : width + 2 * heads]
    second_top = second_part[:, width : width + heads]
    second_sum = second_part[:, width + heads : width + 2 * heads]
    larger = jnp.maximum(first_top, second_top)
    first_factor = jnp.exp(first_top - larger)
    second_factor = jnp.exp(second_top - larger)
    rows = first_part.shape[0]
    head_size = width // heads
    acc = (
        first_part[:, :width].reshape(rows, heads, head_size) * first_factor[..., None]
        + second_part[:, :width].reshape(rows, heads, head_size) * second_factor[..., None]
    )
    stats = jnp.concatenate(
        [larger, first_sum * first_factor + second_sum * second_factor, first_part[:, width + 2 * heads :]],
        axis=-1,
    )
    return jnp.concatenate([acc.reshape(rows, width), stats], axis=-1)


def across_mlp(partial_value):
    return joined(partial_value, "mlp", lambda first, second: first + second)


def across_mlp_narrow(partial_value):
    for mask, _ in axis_stages("mlp"):
        sent = partner_swap(partial_value.astype(jnp.bfloat16), "mlp", mask)
        partial_value = partial_value + sent.astype(jnp.float32)
    return partial_value


def per_device(
    tokens,
    lengths,
    leaving,
    owner,
    cache,
    conv_state,
    lru_state,
    gain_rec,
    w_input,
    w_branch,
    conv_weight,
    conv_bias,
    gate_weight,
    gate_bias,
    decay_param,
    w_rec_out,
    gain_att,
    w_query,
    w_keyval,
    w_attn_out,
    gain_mlp,
    w_gate,
    w_up,
    w_down,
):
    req_rows = tokens.shape[0]
    width = tokens.shape[1]
    leavers = leaving.shape[1]
    groups = lax.axis_size("req")
    own_group = lax.axis_index("req")
    mlp_id = lax.axis_index("mlp")
    rank_ids = jnp.arange(leavers, dtype=jnp.int32)
    group_ids = jnp.arange(groups, dtype=jnp.int32)
    my_leave = leaving[own_group]
    anchor = jnp.sum(jnp.where(owner == own_group, group_ids[:, None], 0), axis=0)
    page_rows = cache.shape[1]
    conv_rows = conv_state.shape[1]
    states = jnp.concatenate([conv_state, lru_state[:, None, :]], axis=1)
    to_group = owner[own_group][None, :] == group_ids[:, None]
    send_slot = jnp.sum(jnp.where(to_group, my_leave[None, :], 0), axis=1)
    got_states = lax.all_to_all(jnp.take(states, send_slot, axis=0), "req", 0, 0, tiled=True)
    got_cache = lax.all_to_all(jnp.take(cache, send_slot, axis=0), "req", 0, 0, tiled=True)
    local_ids = jnp.arange(req_rows, dtype=jnp.int32)
    match_slot = my_leave[None, :] == local_ids[:, None]
    arrive_rank = jnp.sum(jnp.where(match_slot, rank_ids[None, :], 0), axis=1)
    arriving = jnp.any(match_slot, axis=1)
    arrive_from = anchor[arrive_rank]
    moved_states = jnp.where(
        arriving[:, None, None], jnp.take(got_states, arrive_from, axis=0), states
    )
    moved_cache = jnp.where(
        arriving[:, None, None], jnp.take(got_cache, arrive_from, axis=0), cache
    )
    moved_conv = moved_states[:, :conv_rows]
    moved_lru = moved_states[:, conv_rows]
    arrive_anchor = anchor[arrive_rank]
    anchor_slot = arrive_anchor * req_rows + leaving[arrive_anchor, arrive_rank]
    source_slot = jnp.where(arriving, anchor_slot, own_group * req_rows + local_ids)
    position = lengths[source_slot]
    inputs = tokens.astype(jnp.float32)
    normed = rms_norm(inputs, gain_rec)
    branch_in = jnp.dot(normed, w_input, preferred_element_type=jnp.float32).astype(jnp.bfloat16)
    branch = jax.nn.gelu(
        jnp.dot(normed, w_branch, preferred_element_type=jnp.float32), approximate=True
    )
    history = moved_conv.astype(jnp.float32)
    conv_in = (
        jnp.sum(conv_weight[:-1][None] * history, axis=1)
        + conv_weight[-1] * branch_in.astype(jnp.float32)
        + conv_bias
    )
    channels = conv_in.shape[1]
    block_size = gate_weight.shape[2]
    blocks = channels // block_size
    gate_pre = (
        jnp.einsum(
            "snb,gnbc->gsnc",
            conv_in.reshape(req_rows, blocks, block_size),
            gate_weight.astype(jnp.float32),
        ).reshape(2, req_rows, channels)
        + gate_bias[:, None, :]
    )
    rate_gate = jax.nn.sigmoid(gate_pre[0])
    admit_gate = jax.nn.sigmoid(gate_pre[1])
    log_decay = -8.0 * rate_gate * jax.nn.softplus(-decay_param)
    new_state = (
        jnp.exp(log_decay) * moved_lru.astype(jnp.float32)
        + jnp.sqrt(-jnp.expm1(2.0 * log_decay)) * admit_gate * conv_in
    )
    lru_out = new_state.astype(jnp.bfloat16)
    conv_out = jnp.concatenate([moved_conv[:, 1:], branch_in[:, None, :]], axis=1)
    gated_rec = (new_state * branch).astype(jnp.bfloat16)
    resid_one = inputs + across_mlp(
        jnp.dot(gated_rec, w_rec_out, preferred_element_type=jnp.float32)
    )
    head_size = w_keyval.shape[1] // 2
    heads = width // head_size
    slice_rows = w_query.shape[0]
    normed_att = rms_norm(resid_one, gain_att)
    query_part = jnp.dot(
        lax.dynamic_slice_in_dim(normed_att, mlp_id * slice_rows, slice_rows, 1),
        w_query,
        preferred_element_type=jnp.float32,
    )
    query_full = across_mlp(query_part)
    where_pos = position.astype(jnp.float32)
    queries = rotate(query_full.reshape(req_rows, heads, head_size), where_pos).astype(jnp.bfloat16)
    key_value = jnp.dot(normed_att, w_keyval, preferred_element_type=jnp.float32)
    key_new = rotate(key_value[:, None, :head_size], where_pos)[:, 0].astype(jnp.bfloat16)
    value_new = key_value[:, head_size:].astype(jnp.bfloat16)
    window = page_rows * lax.axis_size("mlp")
    score_scale = 1.0 / math.sqrt(head_size)
    scores = (
        jnp.einsum(
            "shd,swd->shw",
            queries,
            moved_cache[..., :head_size],
            preferred_element_type=jnp.float32,
        )
        * score_scale
    )
    slot_ids = mlp_id * page_rows + jnp.arange(page_rows, dtype=jnp.int32)[None, :]
    current = position[:, None]
    held_pos = current - 1 - jnp.mod(current - 1 - slot_ids, window)
    usable = ((held_pos >= 0) & (held_pos != current - window))[:, None, :]
    local_top = jnp.max(jnp.where(usable, scores, -1e30), axis=-1)
    weights = jnp.where(usable, jnp.exp(scores - local_top[..., None]), 0.0)
    local_sum = jnp.sum(weights, axis=-1)
    local_acc = jnp.einsum(
        "shw,swd->shd",
        weights.astype(jnp.bfloat16),
        moved_cache[..., head_size:],
        preferred_element_type=jnp.float32,
    )
    stat_pad = jnp.zeros((req_rows, 128 - 2 * heads), jnp.float32)
    merged = joined(
        jnp.concatenate(
            [local_acc.reshape(req_rows, width), local_top, local_sum, stat_pad], axis=-1
        ),
        "mlp",
        combine_parts,
    )
    merged_acc = merged[:, :width].reshape(req_rows, heads, head_size)
    merged_top = merged[:, width : width + heads]
    merged_sum = merged[:, width + heads : width + 2 * heads]
    own_score = (
        jnp.sum(queries.astype(jnp.float32) * key_new.astype(jnp.float32)[:, None, :], axis=-1)
        * score_scale
    )
    top_score = jnp.maximum(merged_top, own_score)
    rescale = jnp.exp(merged_top - top_score)
    own_weight = jnp.exp(own_score - top_score)
    own_rounded = lax.optimization_barrier(own_weight.astype(jnp.bfloat16)).astype(jnp.float32)
    denominator = merged_sum * rescale + own_weight
    numerator = (
        merged_acc * rescale[..., None]
        + own_rounded[..., None] * value_new.astype(jnp.float32)[:, None, :]
    )
    attended = (numerator / denominator[..., None]).reshape(req_rows, width).astype(jnp.bfloat16)
    attn_part = jnp.dot(
        lax.dynamic_slice_in_dim(attended, mlp_id * slice_rows, slice_rows, 1),
        w_attn_out,
        preferred_element_type=jnp.float32,
    )
    resid_two = resid_one + across_mlp_narrow(attn_part)
    normed_mlp = rms_norm(resid_two, gain_mlp)
    gate_act = jax.nn.gelu(
        jnp.dot(normed_mlp, w_gate, preferred_element_type=jnp.float32), approximate=True
    )
    hidden = (gate_act * jnp.dot(normed_mlp, w_up, preferred_element_type=jnp.float32)).astype(
        jnp.bfloat16
    )
    down_part = jnp.dot(hidden, w_down, preferred_element_type=jnp.float32)
    share = scatter_sum(down_part, "mlp")
    share_cols = share.shape[1]
    hidden_out = (
        lax.dynamic_slice_in_dim(resid_two, mlp_id * share_cols, share_cols, 1) + share
    ).astype(jnp.bfloat16)
    write_row = jnp.concatenate([key_new, value_new], axis=-1)
    row_hit = slot_ids == jnp.mod(current, window)
    cache_out = jnp.where(row_hit[:, :, None], write_row[:, None, :], moved_cache)
    return (hidden_out, cache_out, conv_out, lru_out)


def solution(mesh):
    placed = (
        P("req", None),
        P(),
        P(),
        P(),
        P("req", "mlp", None),
        P("req", None, "mlp"),
        P("req", "mlp"),
        P(),
        P(None, "mlp"),
        P(None, "mlp"),
        P(None, "mlp"),
        P("mlp"),
        P(None, "mlp", None, None),
        P(None, "mlp"),
        P("mlp"),
        P("mlp", None),
        P(),
        P("mlp", None),
        P(),
        P("mlp", None),
        P(),
        P(None, "mlp"),
        P(None, "mlp"),
        P("mlp", None),
    )
    return jax.shard_map(
        per_device,
        mesh=mesh,
        in_specs=placed,
        out_specs=(P("req", "mlp"), P("req", "mlp", None), P("req", None, "mlp"), P("req", "mlp")),
        check_vma=False,
    )
```

```python
import math

import jax
import jax.numpy as jnp
from jax import lax
from jax.sharding import PartitionSpec as P

epsilon = 1e-06


def partner_swap(value, axis, bit):
    size = lax.axis_size(axis)
    pairs = [(j, j ^ bit) for j in range(size)]
    return jax.tree.map(lambda part: lax.ppermute(part, axis, pairs), value)


def axis_bits(axis):
    size = lax.axis_size(axis)
    assert size & (size - 1) == 0
    bits = []
    bit = 1
    while bit < size:
        bits.append(bit)
        bit *= 2
    return bits


def axis_stages(axis):
    stages = []
    for bit in axis_bits(axis):
        mask = bit | (bit // 2) if bit == 2 else bit
        stages.append((mask, bit))
    return stages


def joined(value, axis, join):
    for mask, _ in axis_stages(axis):
        value = join(value, partner_swap(value, axis, mask))
    return value


def scatter_sum(value, axis):
    size = lax.axis_size(axis)
    rows, cols = value.shape
    me = lax.axis_index(axis)
    held = value.reshape(rows, size, cols // size)
    for mask, bit in reversed(axis_stages(axis)):
        half = held.shape[1] // 2
        lower, upper = held[:, :half], held[:, half:]
        mine_upper = (me & bit) != 0
        keep = jnp.where(mine_upper, upper, lower)
        send = jnp.where(mine_upper, lower, upper)
        held = keep + partner_swap(send.astype(jnp.bfloat16), axis, mask).astype(jnp.float32)
    return held.reshape(rows, cols // size)


def rms_norm(values, gain_vec):
    mean_square = jnp.mean(values * values, axis=-1, keepdims=True)
    return (values * lax.rsqrt(mean_square + epsilon) * gain_vec).astype(jnp.bfloat16)


def rotate(vectors, positions):
    half_size = vectors.shape[-1] // 2
    frequency = 10000.0 ** (-2.0 * jnp.arange(half_size, dtype=jnp.float32) / vectors.shape[-1])
    angles = positions[:, None] * frequency[None, :]
    cos_part = jnp.cos(angles)[:, None, :]
    sin_part = jnp.sin(angles)[:, None, :]
    first_half = vectors[..., :half_size]
    second = vectors[..., half_size:]
    return jnp.concatenate(
        [first_half * cos_part - second * sin_part, second * cos_part + first_half * sin_part],
        axis=-1,
    )


def combine_parts(first_part, second_part):
    width = first_part.shape[-1] - 128
    heads = width // 128
    first_top, first_sum = first_part[:, width : width + heads], first_part[:, width + heads : width + 2 * heads]
    second_top = second_part[:, width : width + heads]
    second_sum = second_part[:, width + heads : width + 2 * heads]
    larger = jnp.maximum(first_top, second_top)
    first_factor = jnp.exp(first_top - larger)
    second_factor = jnp.exp(second_top - larger)
    rows = first_part.shape[0]
    head_size = width // heads
    acc = (
        first_part[:, :width].reshape(rows, heads, head_size) * first_factor[..., None]
        + second_part[:, :width].reshape(rows, heads, head_size) * second_factor[..., None]
    )
    stats = jnp.concatenate(
        [larger, first_sum * first_factor + second_sum * second_factor, first_part[:, width + 2 * heads :]],
        axis=-1,
    )
    return jnp.concatenate([acc.reshape(rows, width), stats], axis=-1)


def across_mlp(partial_value):
    return joined(partial_value, "mlp", lambda first, second: first + second)


def across_mlp_narrow(partial_value):
    for mask, _ in axis_stages("mlp"):
        sent = partner_swap(partial_value.astype(jnp.bfloat16), "mlp", mask)
        partial_value = partial_value + sent.astype(jnp.float32)
    return partial_value


def per_device(
    tokens,
    lengths,
    leaving,
    owner,
    cache,
    conv_state,
    lru_state,
    gain_rec,
    w_input,
    w_branch,
    conv_weight,
    conv_bias,
    gate_weight,
    gate_bias,
    decay_param,
    w_rec_out,
    gain_att,
    w_query,
    w_keyval,
    w_attn_out,
    gain_mlp,
    w_gate,
    w_up,
    w_down,
):
    req_rows = tokens.shape[0]
    width = tokens.shape[1]
    leavers = leaving.shape[1]
    groups = lax.axis_size("req")
    own_group = lax.axis_index("req")
    mlp_id = lax.axis_index("mlp")
    rank_ids = jnp.arange(leavers, dtype=jnp.int32)
    group_ids = jnp.arange(groups, dtype=jnp.int32)
    my_leave = leaving[own_group]
    anchor = jnp.sum(jnp.where(owner == own_group, group_ids[:, None], 0), axis=0)
    page_rows = cache.shape[1]
    conv_rows = conv_state.shape[1]
    states = jnp.concatenate([conv_state, lru_state[:, None, :]], axis=1)
    to_group = owner[own_group][None, :] == group_ids[:, None]
    send_slot = jnp.sum(jnp.where(to_group, my_leave[None, :], 0), axis=1)
    got_states = lax.all_to_all(jnp.take(states, send_slot, axis=0), "req", 0, 0, tiled=True)
    got_cache = lax.all_to_all(jnp.take(cache, send_slot, axis=0), "req", 0, 0, tiled=True)
    local_ids = jnp.arange(req_rows, dtype=jnp.int32)
    match_slot = my_leave[None, :] == local_ids[:, None]
    arrive_rank = jnp.sum(jnp.where(match_slot, rank_ids[None, :], 0), axis=1)
    arriving = jnp.any(match_slot, axis=1)
    arrive_from = anchor[arrive_rank]
    moved_states = jnp.where(
        arriving[:, None, None], jnp.take(got_states, arrive_from, axis=0), states
    )
    moved_cache = jnp.where(
        arriving[:, None, None], jnp.take(got_cache, arrive_from, axis=0), cache
    )
    moved_conv = moved_states[:, :conv_rows]
    moved_lru = moved_states[:, conv_rows]
    arrive_anchor = anchor[arrive_rank]
    anchor_slot = arrive_anchor * req_rows + leaving[arrive_anchor, arrive_rank]
    source_slot = jnp.where(arriving, anchor_slot, own_group * req_rows + local_ids)
    position = lengths[source_slot]
    inputs = tokens.astype(jnp.float32)
    normed = rms_norm(inputs, gain_rec)
    branch_in = jnp.dot(normed, w_input, preferred_element_type=jnp.float32).astype(jnp.bfloat16)
    branch = jax.nn.gelu(
        jnp.dot(normed, w_branch, preferred_element_type=jnp.float32), approximate=True
    )
    history = moved_conv.astype(jnp.float32)
    conv_in = (
        jnp.sum(conv_weight[:-1][None] * history, axis=1)
        + conv_weight[-1] * branch_in.astype(jnp.float32)
        + conv_bias
    )
    channels = conv_in.shape[1]
    block_size = gate_weight.shape[2]
    blocks = channels // block_size
    gate_pre = (
        jnp.einsum(
            "snb,gnbc->gsnc",
            conv_in.reshape(req_rows, blocks, block_size),
            gate_weight.astype(jnp.float32),
        ).reshape(2, req_rows, channels)
        + gate_bias[:, None, :]
    )
    rate_gate = jax.nn.sigmoid(gate_pre[0])
    admit_gate = jax.nn.sigmoid(gate_pre[1])
    log_decay = -8.0 * rate_gate * jax.nn.softplus(-decay_param)
    new_state = (
        jnp.exp(log_decay) * moved_lru.astype(jnp.float32)
        + jnp.sqrt(-jnp.expm1(2.0 * log_decay)) * admit_gate * conv_in
    )
    lru_out = new_state.astype(jnp.bfloat16)
    conv_out = jnp.concatenate([moved_conv[:, 1:], branch_in[:, None, :]], axis=1)
    gated_rec = (new_state * branch).astype(jnp.bfloat16)
    resid_one = inputs + across_mlp_narrow(
        jnp.dot(gated_rec, w_rec_out, preferred_element_type=jnp.float32)
    )
    head_size = w_keyval.shape[1] // 2
    heads = width // head_size
    slice_rows = w_query.shape[0]
    normed_att = rms_norm(resid_one, gain_att)
    query_part = jnp.dot(
        lax.dynamic_slice_in_dim(normed_att, mlp_id * slice_rows, slice_rows, 1),
        w_query,
        preferred_element_type=jnp.float32,
    )
    query_full = across_mlp_narrow(query_part)
    where_pos = position.astype(jnp.float32)
    queries = rotate(query_full.reshape(req_rows, heads, head_size), where_pos).astype(jnp.bfloat16)
    key_value = jnp.dot(normed_att, w_keyval, preferred_element_type=jnp.float32)
    key_new = rotate(key_value[:, None, :head_size], where_pos)[:, 0].astype(jnp.bfloat16)
    value_new = key_value[:, head_size:].astype(jnp.bfloat16)
    window = page_rows * lax.axis_size("mlp")
    score_scale = 1.0 / math.sqrt(head_size)
    scores = (
        jnp.einsum(
            "shd,swd->shw",
            queries,
            moved_cache[..., :head_size],
            preferred_element_type=jnp.float32,
        )
        * score_scale
    )
    slot_ids = mlp_id * page_rows + jnp.arange(page_rows, dtype=jnp.int32)[None, :]
    current = position[:, None]
    held_pos = current - 1 - jnp.mod(current - 1 - slot_ids, window)
    usable = ((held_pos >= 0) & (held_pos != current - window))[:, None, :]
    local_top = jnp.max(jnp.where(usable, scores, -1e30), axis=-1)
    weights = jnp.where(usable, jnp.exp(scores - local_top[..., None]), 0.0)
    local_sum = jnp.sum(weights, axis=-1)
    local_acc = jnp.einsum(
        "shw,swd->shd",
        weights.astype(jnp.bfloat16),
        moved_cache[..., head_size:],
        preferred_element_type=jnp.float32,
    )
    stat_pad = jnp.zeros((req_rows, 128 - 2 * heads), jnp.float32)
    merged = joined(
        jnp.concatenate(
            [local_acc.reshape(req_rows, width), local_top, local_sum, stat_pad], axis=-1
        ),
        "mlp",
        combine_parts,
    )
    merged_acc = merged[:, :width].reshape(req_rows, heads, head_size)
    merged_top = merged[:, width : width + heads]
    merged_sum = merged[:, width + heads : width + 2 * heads]
    own_score = (
        jnp.sum(queries.astype(jnp.float32) * key_new.astype(jnp.float32)[:, None, :], axis=-1)
        * score_scale
    )
    top_score = jnp.maximum(merged_top, own_score)
    rescale = jnp.exp(merged_top - top_score)
    own_weight = jnp.exp(own_score - top_score)
    own_rounded = lax.optimization_barrier(own_weight.astype(jnp.bfloat16)).astype(jnp.float32)
    denominator = merged_sum * rescale + own_weight
    numerator = (
        merged_acc * rescale[..., None]
        + own_rounded[..., None] * value_new.astype(jnp.float32)[:, None, :]
    )
    attended = (numerator / denominator[..., None]).reshape(req_rows, width).astype(jnp.bfloat16)
    attn_part = jnp.dot(
        lax.dynamic_slice_in_dim(attended, mlp_id * slice_rows, slice_rows, 1),
        w_attn_out,
        preferred_element_type=jnp.float32,
    )
    resid_two = resid_one + across_mlp_narrow(attn_part)
    normed_mlp = rms_norm(resid_two, gain_mlp)
    gate_act = jax.nn.gelu(
        jnp.dot(normed_mlp, w_gate, preferred_element_type=jnp.float32), approximate=True
    )
    hidden = (gate_act * jnp.dot(normed_mlp, w_up, preferred_element_type=jnp.float32)).astype(
        jnp.bfloat16
    )
    down_part = jnp.dot(hidden, w_down, preferred_element_type=jnp.float32)
    share = scatter_sum(down_part, "mlp")
    share_cols = share.shape[1]
    hidden_out = (
        lax.dynamic_slice_in_dim(resid_two, mlp_id * share_cols, share_cols, 1) + share
    ).astype(jnp.bfloat16)
    write_row = jnp.concatenate([key_new, value_new], axis=-1)
    row_hit = slot_ids == jnp.mod(current, window)
    cache_out = jnp.where(row_hit[:, :, None], write_row[:, None, :], moved_cache)
    return (hidden_out, cache_out, conv_out, lru_out)


def solution(mesh):
    placed = (
        P("req", None),
        P(),
        P(),
        P(),
        P("req", "mlp", None),
        P("req", None, "mlp"),
        P("req", "mlp"),
        P(),
        P(None, "mlp"),
        P(None, "mlp"),
        P(None, "mlp"),
        P("mlp"),
        P(None, "mlp", None, None),
        P(None, "mlp"),
        P("mlp"),
        P("mlp", None),
        P(),
        P("mlp", None),
        P(),
        P("mlp", None),
        P(),
        P(None, "mlp"),
        P(None, "mlp"),
        P("mlp", None),
    )
    return jax.shard_map(
        per_device,
        mesh=mesh,
        in_specs=placed,
        out_specs=(P("req", "mlp"), P("req", "mlp", None), P("req", None, "mlp"), P("req", "mlp")),
        check_vma=False,
    )
```

```python
import math

import jax
import jax.numpy as jnp
from jax import lax
from jax.sharding import PartitionSpec as P

epsilon = 1e-06


def partner_swap(value, axis, bit):
    size = lax.axis_size(axis)
    pairs = [(j, j ^ bit) for j in range(size)]
    return jax.tree.map(lambda part: lax.ppermute(part, axis, pairs), value)


def axis_bits(axis):
    size = lax.axis_size(axis)
    assert size & (size - 1) == 0
    bits = []
    bit = 1
    while bit < size:
        bits.append(bit)
        bit *= 2
    return bits


def axis_stages(axis):
    stages = []
    for bit in axis_bits(axis):
        mask = bit | (bit // 2) if bit == 2 else bit
        stages.append((mask, bit))
    return stages


def joined(value, axis, join):
    for mask, _ in axis_stages(axis):
        value = join(value, partner_swap(value, axis, mask))
    return value


def scatter_sum(value, axis):
    size = lax.axis_size(axis)
    rows, cols = value.shape
    me = lax.axis_index(axis)
    held = value.reshape(rows, size, cols // size)
    for mask, bit in reversed(axis_stages(axis)):
        half = held.shape[1] // 2
        lower, upper = held[:, :half], held[:, half:]
        mine_upper = (me & bit) != 0
        keep = jnp.where(mine_upper, upper, lower)
        send = jnp.where(mine_upper, lower, upper)
        held = keep + partner_swap(send.astype(jnp.bfloat16), axis, mask).astype(jnp.float32)
    return held.reshape(rows, cols // size)


def rms_norm(values, gain_vec):
    mean_square = jnp.mean(values * values, axis=-1, keepdims=True)
    return (values * lax.rsqrt(mean_square + epsilon) * gain_vec).astype(jnp.bfloat16)


def rotate(vectors, positions):
    half_size = vectors.shape[-1] // 2
    frequency = 10000.0 ** (-2.0 * jnp.arange(half_size, dtype=jnp.float32) / vectors.shape[-1])
    angles = positions[:, None] * frequency[None, :]
    cos_part = jnp.cos(angles)[:, None, :]
    sin_part = jnp.sin(angles)[:, None, :]
    first_half = vectors[..., :half_size]
    second = vectors[..., half_size:]
    return jnp.concatenate(
        [first_half * cos_part - second * sin_part, second * cos_part + first_half * sin_part],
        axis=-1,
    )


def combine_parts(first_part, second_part):
    width = first_part.shape[-1] - 128
    heads = width // 128
    first_top, first_sum = first_part[:, width : width + heads], first_part[:, width + heads : width + 2 * heads]
    second_top = second_part[:, width : width + heads]
    second_sum = second_part[:, width + heads : width + 2 * heads]
    larger = jnp.maximum(first_top, second_top)
    first_factor = jnp.exp(first_top - larger)
    second_factor = jnp.exp(second_top - larger)
    rows = first_part.shape[0]
    head_size = width // heads
    acc = (
        first_part[:, :width].reshape(rows, heads, head_size) * first_factor[..., None]
        + second_part[:, :width].reshape(rows, heads, head_size) * second_factor[..., None]
    )
    stats = jnp.concatenate(
        [larger, first_sum * first_factor + second_sum * second_factor, first_part[:, width + 2 * heads :]],
        axis=-1,
    )
    return jnp.concatenate([acc.reshape(rows, width), stats], axis=-1)


def across_mlp(partial_value):
    return joined(partial_value, "mlp", lambda first, second: first + second)


def across_mlp_narrow(partial_value):
    for mask, _ in axis_stages("mlp"):
        sent = partner_swap(partial_value.astype(jnp.bfloat16), "mlp", mask)
        partial_value = partial_value + sent.astype(jnp.float32)
    return partial_value


def per_device(
    tokens,
    lengths,
    leaving,
    owner,
    cache,
    conv_state,
    lru_state,
    gain_rec,
    w_input,
    w_branch,
    conv_weight,
    conv_bias,
    gate_weight,
    gate_bias,
    decay_param,
    w_rec_out,
    gain_att,
    w_query,
    w_keyval,
    w_attn_out,
    gain_mlp,
    w_gate,
    w_up,
    w_down,
):
    req_rows = tokens.shape[0]
    width = tokens.shape[1]
    leavers = leaving.shape[1]
    groups = lax.axis_size("req")
    own_group = lax.axis_index("req")
    mlp_id = lax.axis_index("mlp")
    rank_ids = jnp.arange(leavers, dtype=jnp.int32)
    group_ids = jnp.arange(groups, dtype=jnp.int32)
    my_leave = leaving[own_group]
    anchor = jnp.sum(jnp.where(owner == own_group, group_ids[:, None], 0), axis=0)
    page_rows = cache.shape[1]
    conv_rows = conv_state.shape[1]
    states = jnp.concatenate([conv_state, lru_state[:, None, :]], axis=1)
    to_group = owner[own_group][None, :] == group_ids[:, None]
    rank_of_me = jnp.sum(jnp.where(owner == own_group, rank_ids[None, :], 0), axis=1)
    send_slot = jnp.sum(jnp.where(to_group, my_leave[None, :], 0), axis=1)
    leave_states = jnp.take(states, my_leave, axis=0)
    leave_states = jnp.concatenate([leave_states, jnp.zeros_like(leave_states)], axis=1)
    all_states = lax.all_gather(leave_states, "req", axis=0, tiled=True)[:, : conv_rows + 1]
    got_states = jnp.take(all_states, group_ids * leavers + rank_of_me, axis=0)
    got_cache = lax.all_to_all(jnp.take(cache, send_slot, axis=0), "req", 0, 0, tiled=True)
    local_ids = jnp.arange(req_rows, dtype=jnp.int32)
    match_slot = my_leave[None, :] == local_ids[:, None]
    arrive_rank = jnp.sum(jnp.where(match_slot, rank_ids[None, :], 0), axis=1)
    arriving = jnp.any(match_slot, axis=1)
    arrive_from = anchor[arrive_rank]
    moved_states = jnp.where(
        arriving[:, None, None], jnp.take(got_states, arrive_from, axis=0), states
    )
    moved_cache = jnp.where(
        arriving[:, None, None], jnp.take(got_cache, arrive_from, axis=0), cache
    )
    moved_conv = moved_states[:, :conv_rows]
    moved_lru = moved_states[:, conv_rows]
    arrive_anchor = anchor[arrive_rank]
    anchor_slot = arrive_anchor * req_rows + leaving[arrive_anchor, arrive_rank]
    source_slot = jnp.where(arriving, anchor_slot, own_group * req_rows + local_ids)
    position = lengths[source_slot]
    inputs = tokens.astype(jnp.float32)
    normed = rms_norm(inputs, gain_rec)
    branch_in = jnp.dot(normed, w_input, preferred_element_type=jnp.float32).astype(jnp.bfloat16)
    branch = jax.nn.gelu(
        jnp.dot(normed, w_branch, preferred_element_type=jnp.float32), approximate=True
    )
    history = moved_conv.astype(jnp.float32)
    conv_in = (
        jnp.sum(conv_weight[:-1][None] * history, axis=1)
        + conv_weight[-1] * branch_in.astype(jnp.float32)
        + conv_bias
    )
    channels = conv_in.shape[1]
    block_size = gate_weight.shape[2]
    blocks = channels // block_size
    gate_pre = (
        jnp.einsum(
            "snb,gnbc->gsnc",
            conv_in.reshape(req_rows, blocks, block_size),
            gate_weight.astype(jnp.float32),
        ).reshape(2, req_rows, channels)
        + gate_bias[:, None, :]
    )
    rate_gate = jax.nn.sigmoid(gate_pre[0])
    admit_gate = jax.nn.sigmoid(gate_pre[1])
    log_decay = -8.0 * rate_gate * jax.nn.softplus(-decay_param)
    new_state = (
        jnp.exp(log_decay) * moved_lru.astype(jnp.float32)
        + jnp.sqrt(-jnp.expm1(2.0 * log_decay)) * admit_gate * conv_in
    )
    lru_out = new_state.astype(jnp.bfloat16)
    conv_out = jnp.concatenate([moved_conv[:, 1:], branch_in[:, None, :]], axis=1)
    gated_rec = (new_state * branch).astype(jnp.bfloat16)
    resid_one = inputs + across_mlp_narrow(
        jnp.dot(gated_rec, w_rec_out, preferred_element_type=jnp.float32)
    )
    head_size = w_keyval.shape[1] // 2
    heads = width // head_size
    slice_rows = w_query.shape[0]
    normed_att = rms_norm(resid_one, gain_att)
    query_part = jnp.dot(
        lax.dynamic_slice_in_dim(normed_att, mlp_id * slice_rows, slice_rows, 1),
        w_query,
        preferred_element_type=jnp.float32,
    )
    query_full = across_mlp_narrow(query_part)
    where_pos = position.astype(jnp.float32)
    queries = rotate(query_full.reshape(req_rows, heads, head_size), where_pos).astype(jnp.bfloat16)
    key_value = jnp.dot(normed_att, w_keyval, preferred_element_type=jnp.float32)
    key_new = rotate(key_value[:, None, :head_size], where_pos)[:, 0].astype(jnp.bfloat16)
    value_new = key_value[:, head_size:].astype(jnp.bfloat16)
    window = page_rows * lax.axis_size("mlp")
    score_scale = 1.0 / math.sqrt(head_size)
    scores = (
        jnp.einsum(
            "shd,swd->shw",
            queries,
            moved_cache[..., :head_size],
            preferred_element_type=jnp.float32,
        )
        * score_scale
    )
    slot_ids = mlp_id * page_rows + jnp.arange(page_rows, dtype=jnp.int32)[None, :]
    current = position[:, None]
    held_pos = current - 1 - jnp.mod(current - 1 - slot_ids, window)
    usable = ((held_pos >= 0) & (held_pos != current - window))[:, None, :]
    local_top = jnp.max(jnp.where(usable, scores, -1e30), axis=-1)
    weights = jnp.where(usable, jnp.exp(scores - local_top[..., None]), 0.0)
    local_sum = jnp.sum(weights, axis=-1)
    local_acc = jnp.einsum(
        "shw,swd->shd",
        weights.astype(jnp.bfloat16),
        moved_cache[..., head_size:],
        preferred_element_type=jnp.float32,
    )
    stat_pad = jnp.zeros((req_rows, 128 - 2 * heads), jnp.float32)
    merged = joined(
        jnp.concatenate(
            [local_acc.reshape(req_rows, width), local_top, local_sum, stat_pad], axis=-1
        ),
        "mlp",
        combine_parts,
    )
    merged_acc = merged[:, :width].reshape(req_rows, heads, head_size)
    merged_top = merged[:, width : width + heads]
    merged_sum = merged[:, width + heads : width + 2 * heads]
    own_score = (
        jnp.sum(queries.astype(jnp.float32) * key_new.astype(jnp.float32)[:, None, :], axis=-1)
        * score_scale
    )
    top_score = jnp.maximum(merged_top, own_score)
    rescale = jnp.exp(merged_top - top_score)
    own_weight = jnp.exp(own_score - top_score)
    own_rounded = lax.optimization_barrier(own_weight.astype(jnp.bfloat16)).astype(jnp.float32)
    denominator = merged_sum * rescale + own_weight
    numerator = (
        merged_acc * rescale[..., None]
        + own_rounded[..., None] * value_new.astype(jnp.float32)[:, None, :]
    )
    attended = (numerator / denominator[..., None]).reshape(req_rows, width).astype(jnp.bfloat16)
    attn_part = jnp.dot(
        lax.dynamic_slice_in_dim(attended, mlp_id * slice_rows, slice_rows, 1),
        w_attn_out,
        preferred_element_type=jnp.float32,
    )
    resid_two = resid_one + across_mlp_narrow(attn_part)
    normed_mlp = rms_norm(resid_two, gain_mlp)
    gate_act = jax.nn.gelu(
        jnp.dot(normed_mlp, w_gate, preferred_element_type=jnp.float32), approximate=True
    )
    hidden = (gate_act * jnp.dot(normed_mlp, w_up, preferred_element_type=jnp.float32)).astype(
        jnp.bfloat16
    )
    down_part = jnp.dot(hidden, w_down, preferred_element_type=jnp.float32)
    share = scatter_sum(down_part, "mlp")
    share_cols = share.shape[1]
    hidden_out = (
        lax.dynamic_slice_in_dim(resid_two, mlp_id * share_cols, share_cols, 1) + share
    ).astype(jnp.bfloat16)
    write_row = jnp.concatenate([key_new, value_new], axis=-1)
    row_hit = slot_ids == jnp.mod(current, window)
    cache_out = jnp.where(row_hit[:, :, None], write_row[:, None, :], moved_cache)
    return (hidden_out, cache_out, conv_out, lru_out)


def solution(mesh):
    placed = (
        P("req", None),
        P(),
        P(),
        P(),
        P("req", "mlp", None),
        P("req", None, "mlp"),
        P("req", "mlp"),
        P(),
        P(None, "mlp"),
        P(None, "mlp"),
        P(None, "mlp"),
        P("mlp"),
        P(None, "mlp", None, None),
        P(None, "mlp"),
        P("mlp"),
        P("mlp", None),
        P(),
        P("mlp", None),
        P(),
        P("mlp", None),
        P(),
        P(None, "mlp"),
        P(None, "mlp"),
        P("mlp", None),
    )
    return jax.shard_map(
        per_device,
        mesh=mesh,
        in_specs=placed,
        out_specs=(P("req", "mlp"), P("req", "mlp", None), P("req", None, "mlp"), P("req", "mlp")),
        check_vma=False,
    )
```

```python
import math

import jax
import jax.numpy as jnp
from jax import lax
from jax.sharding import PartitionSpec as P

epsilon = 1e-06


def partner_swap(value, axis, bit):
    size = lax.axis_size(axis)
    pairs = [(j, j ^ bit) for j in range(size)]
    return jax.tree.map(lambda part: lax.ppermute(part, axis, pairs), value)


def axis_bits(axis):
    size = lax.axis_size(axis)
    assert size & (size - 1) == 0
    bits = []
    bit = 1
    while bit < size:
        bits.append(bit)
        bit *= 2
    return bits


def axis_stages(axis):
    stages = []
    for bit in axis_bits(axis):
        mask = bit | (bit // 2) if bit == 2 else bit
        stages.append((mask, bit))
    return stages


def joined(value, axis, join):
    for mask, _ in axis_stages(axis):
        value = join(value, partner_swap(value, axis, mask))
    return value


def scatter_sum(value, axis):
    size = lax.axis_size(axis)
    rows, cols = value.shape
    me = lax.axis_index(axis)
    held = value.reshape(rows, size, cols // size)
    for mask, bit in reversed(axis_stages(axis)):
        half = held.shape[1] // 2
        lower, upper = held[:, :half], held[:, half:]
        mine_upper = (me & bit) != 0
        keep = jnp.where(mine_upper, upper, lower)
        send = jnp.where(mine_upper, lower, upper)
        held = keep + partner_swap(send.astype(jnp.bfloat16), axis, mask).astype(jnp.float32)
    return held.reshape(rows, cols // size)


def rms_norm(values, gain_vec):
    mean_square = jnp.mean(values * values, axis=-1, keepdims=True)
    return (values * lax.rsqrt(mean_square + epsilon) * gain_vec).astype(jnp.bfloat16)


def rotate(vectors, positions):
    half_size = vectors.shape[-1] // 2
    frequency = 10000.0 ** (-2.0 * jnp.arange(half_size, dtype=jnp.float32) / vectors.shape[-1])
    angles = positions[:, None] * frequency[None, :]
    cos_part = jnp.cos(angles)[:, None, :]
    sin_part = jnp.sin(angles)[:, None, :]
    first_half = vectors[..., :half_size]
    second = vectors[..., half_size:]
    return jnp.concatenate(
        [first_half * cos_part - second * sin_part, second * cos_part + first_half * sin_part],
        axis=-1,
    )


def combine_parts(first_part, second_part):
    width = first_part.shape[-1] - 128
    heads = width // 128
    first_top, first_sum = first_part[:, width : width + heads], first_part[:, width + heads : width + 2 * heads]
    second_top = second_part[:, width : width + heads]
    second_sum = second_part[:, width + heads : width + 2 * heads]
    larger = jnp.maximum(first_top, second_top)
    first_factor = jnp.exp(first_top - larger)
    second_factor = jnp.exp(second_top - larger)
    rows = first_part.shape[0]
    head_size = width // heads
    acc = (
        first_part[:, :width].reshape(rows, heads, head_size) * first_factor[..., None]
        + second_part[:, :width].reshape(rows, heads, head_size) * second_factor[..., None]
    )
    stats = jnp.concatenate(
        [larger, first_sum * first_factor + second_sum * second_factor, first_part[:, width + 2 * heads :]],
        axis=-1,
    )
    return jnp.concatenate([acc.reshape(rows, width), stats], axis=-1)


def across_mlp(partial_value):
    return joined(partial_value, "mlp", lambda first, second: first + second)


def across_mlp_narrow(partial_value):
    for mask, _ in axis_stages("mlp"):
        sent = partner_swap(partial_value.astype(jnp.bfloat16), "mlp", mask)
        partial_value = partial_value + sent.astype(jnp.float32)
    return partial_value


def per_device(
    tokens,
    lengths,
    leaving,
    owner,
    cache,
    conv_state,
    lru_state,
    gain_rec,
    w_input,
    w_branch,
    conv_weight,
    conv_bias,
    gate_weight,
    gate_bias,
    decay_param,
    w_rec_out,
    gain_att,
    w_query,
    w_keyval,
    w_attn_out,
    gain_mlp,
    w_gate,
    w_up,
    w_down,
):
    req_rows = tokens.shape[0]
    width = tokens.shape[1]
    leavers = leaving.shape[1]
    groups = lax.axis_size("req")
    own_group = lax.axis_index("req")
    mlp_id = lax.axis_index("mlp")
    rank_ids = jnp.arange(leavers, dtype=jnp.int32)
    group_ids = jnp.arange(groups, dtype=jnp.int32)
    my_leave = leaving[own_group]
    my_owner = owner[own_group]
    to_me = owner == own_group
    anchor = jnp.sum(jnp.where(to_me, group_ids[:, None], 0), axis=0)
    anchor_leave = jnp.sum(jnp.where(to_me, leaving, 0), axis=0)
    page_rows = cache.shape[1]
    conv_rows = conv_state.shape[1]
    states = jnp.concatenate([conv_state, lru_state[:, None, :]], axis=1)
    to_group = my_owner[None, :] == group_ids[:, None]
    send_slot = jnp.sum(jnp.where(to_group, my_leave[None, :], 0), axis=1)
    got_states = lax.all_to_all(
        jnp.take(states, send_slot, axis=0, mode="clip"), "req", 0, 0, tiled=True
    )
    got_cache = lax.all_to_all(
        jnp.take(cache, send_slot, axis=0, mode="clip"), "req", 0, 0, tiled=True
    )
    local_ids = jnp.arange(req_rows, dtype=jnp.int32)
    match_slot = my_leave[None, :] == local_ids[:, None]
    arriving = jnp.any(match_slot, axis=1)
    arrive_from = jnp.sum(jnp.where(match_slot, anchor[None, :], 0), axis=1)
    anchor_slot = jnp.sum(
        jnp.where(match_slot, (anchor * req_rows + anchor_leave)[None, :], 0), axis=1
    )
    moved_states = jnp.where(
        arriving[:, None, None], jnp.take(got_states, arrive_from, axis=0, mode="clip"), states
    )
    moved_cache = jnp.where(
        arriving[:, None, None], jnp.take(got_cache, arrive_from, axis=0, mode="clip"), cache
    )
    moved_conv = moved_states[:, :conv_rows]
    moved_lru = moved_states[:, conv_rows]
    source_slot = jnp.where(arriving, anchor_slot, own_group * req_rows + local_ids)
    position = jnp.take(lengths, source_slot, mode="clip")
    inputs = tokens.astype(jnp.float32)
    normed = rms_norm(inputs, gain_rec)
    branch_in = jnp.dot(normed, w_input, preferred_element_type=jnp.float32).astype(jnp.bfloat16)
    branch = jax.nn.gelu(
        jnp.dot(normed, w_branch, preferred_element_type=jnp.float32), approximate=True
    )
    history = moved_conv.astype(jnp.float32)
    conv_in = (
        jnp.sum(conv_weight[:-1][None] * history, axis=1)
        + conv_weight[-1] * branch_in.astype(jnp.float32)
        + conv_bias
    )
    channels = conv_in.shape[1]
    block_size = gate_weight.shape[2]
    blocks = channels // block_size
    gate_pre = (
        jnp.einsum(
            "snb,gnbc->gsnc",
            conv_in.reshape(req_rows, blocks, block_size),
            gate_weight.astype(jnp.float32),
        ).reshape(2, req_rows, channels)
        + gate_bias[:, None, :]
    )
    rate_gate = jax.nn.sigmoid(gate_pre[0])
    admit_gate = jax.nn.sigmoid(gate_pre[1])
    log_decay = -8.0 * rate_gate * jax.nn.softplus(-decay_param)
    new_state = (
        jnp.exp(log_decay) * moved_lru.astype(jnp.float32)
        + jnp.sqrt(-jnp.expm1(2.0 * log_decay)) * admit_gate * conv_in
    )
    lru_out = new_state.astype(jnp.bfloat16)
    conv_out = jnp.concatenate([moved_conv[:, 1:], branch_in[:, None, :]], axis=1)
    gated_rec = (new_state * branch).astype(jnp.bfloat16)
    resid_one = inputs + across_mlp_narrow(
        jnp.dot(gated_rec, w_rec_out, preferred_element_type=jnp.float32)
    )
    head_size = w_keyval.shape[1] // 2
    heads = width // head_size
    slice_rows = w_query.shape[0]
    normed_att = rms_norm(resid_one, gain_att)
    query_part = jnp.dot(
        lax.dynamic_slice_in_dim(normed_att, mlp_id * slice_rows, slice_rows, 1),
        w_query,
        preferred_element_type=jnp.float32,
    )
    query_full = across_mlp_narrow(query_part)
    where_pos = position.astype(jnp.float32)
    queries = rotate(query_full.reshape(req_rows, heads, head_size), where_pos).astype(jnp.bfloat16)
    key_value = jnp.dot(normed_att, w_keyval, preferred_element_type=jnp.float32)
    key_new = rotate(key_value[:, None, :head_size], where_pos)[:, 0].astype(jnp.bfloat16)
    value_new = key_value[:, head_size:].astype(jnp.bfloat16)
    window = page_rows * lax.axis_size("mlp")
    score_scale = 1.0 / math.sqrt(head_size)
    scores = (
        jnp.einsum(
            "shd,swd->shw",
            queries,
            moved_cache[..., :head_size],
            preferred_element_type=jnp.float32,
        )
        * score_scale
    )
    slot_ids = mlp_id * page_rows + jnp.arange(page_rows, dtype=jnp.int32)[None, :]
    current = position[:, None]
    held_pos = current - 1 - jnp.mod(current - 1 - slot_ids, window)
    usable = ((held_pos >= 0) & (held_pos != current - window))[:, None, :]
    local_top = jnp.max(jnp.where(usable, scores, -1e30), axis=-1)
    weights = jnp.where(usable, jnp.exp(scores - local_top[..., None]), 0.0)
    local_sum = jnp.sum(weights, axis=-1)
    local_acc = jnp.einsum(
        "shw,swd->shd",
        weights.astype(jnp.bfloat16),
        moved_cache[..., head_size:],
        preferred_element_type=jnp.float32,
    )
    stat_pad = jnp.zeros((req_rows, 128 - 2 * heads), jnp.float32)
    merged = joined(
        jnp.concatenate(
            [local_acc.reshape(req_rows, width), local_top, local_sum, stat_pad], axis=-1
        ),
        "mlp",
        combine_parts,
    )
    merged_acc = merged[:, :width].reshape(req_rows, heads, head_size)
    merged_top = merged[:, width : width + heads]
    merged_sum = merged[:, width + heads : width + 2 * heads]
    own_score = (
        jnp.sum(queries.astype(jnp.float32) * key_new.astype(jnp.float32)[:, None, :], axis=-1)
        * score_scale
    )
    top_score = jnp.maximum(merged_top, own_score)
    rescale = jnp.exp(merged_top - top_score)
    own_weight = jnp.exp(own_score - top_score)
    own_rounded = lax.optimization_barrier(own_weight.astype(jnp.bfloat16)).astype(jnp.float32)
    denominator = merged_sum * rescale + own_weight
    numerator = (
        merged_acc * rescale[..., None]
        + own_rounded[..., None] * value_new.astype(jnp.float32)[:, None, :]
    )
    attended = (numerator / denominator[..., None]).reshape(req_rows, width).astype(jnp.bfloat16)
    attn_part = jnp.dot(
        lax.dynamic_slice_in_dim(attended, mlp_id * slice_rows, slice_rows, 1),
        w_attn_out,
        preferred_element_type=jnp.float32,
    )
    resid_two = resid_one + across_mlp_narrow(attn_part)
    normed_mlp = rms_norm(resid_two, gain_mlp)
    gate_act = jax.nn.gelu(
        jnp.dot(normed_mlp, w_gate, preferred_element_type=jnp.float32), approximate=True
    )
    hidden = (gate_act * jnp.dot(normed_mlp, w_up, preferred_element_type=jnp.float32)).astype(
        jnp.bfloat16
    )
    down_part = jnp.dot(hidden, w_down, preferred_element_type=jnp.float32)
    share = scatter_sum(down_part, "mlp")
    share_cols = share.shape[1]
    hidden_out = (
        lax.dynamic_slice_in_dim(resid_two, mlp_id * share_cols, share_cols, 1) + share
    ).astype(jnp.bfloat16)
    write_row = jnp.concatenate([key_new, value_new], axis=-1)
    row_hit = slot_ids == jnp.mod(current, window)
    cache_out = jnp.where(row_hit[:, :, None], write_row[:, None, :], moved_cache)
    return (hidden_out, cache_out, conv_out, lru_out)


def solution(mesh):
    placed = (
        P("req", None),
        P(),
        P(),
        P(),
        P("req", "mlp", None),
        P("req", None, "mlp"),
        P("req", "mlp"),
        P(),
        P(None, "mlp"),
        P(None, "mlp"),
        P(None, "mlp"),
        P("mlp"),
        P(None, "mlp", None, None),
        P(None, "mlp"),
        P("mlp"),
        P("mlp", None),
        P(),
        P("mlp", None),
        P(),
        P("mlp", None),
        P(),
        P(None, "mlp"),
        P(None, "mlp"),
        P("mlp", None),
    )
    return jax.shard_map(
        per_device,
        mesh=mesh,
        in_specs=placed,
        out_specs=(P("req", "mlp"), P("req", "mlp", None), P("req", None, "mlp"), P("req", "mlp")),
        check_vma=False,
    )
```

```python
import math

import jax
import jax.numpy as jnp
from jax import lax
from jax.sharding import PartitionSpec as P

epsilon = 1e-06


def partner_swap(value, axis, bit):
    size = lax.axis_size(axis)
    pairs = [(j, j ^ bit) for j in range(size)]
    return jax.tree.map(lambda part: lax.ppermute(part, axis, pairs), value)


def axis_bits(axis):
    size = lax.axis_size(axis)
    assert size & (size - 1) == 0
    bits = []
    bit = 1
    while bit < size:
        bits.append(bit)
        bit *= 2
    return bits


def axis_stages(axis):
    stages = []
    for bit in axis_bits(axis):
        mask = bit | (bit // 2) if bit == 2 else bit
        stages.append((mask, bit))
    return stages


def joined(value, axis, join):
    for mask, _ in axis_stages(axis):
        value = join(value, partner_swap(value, axis, mask))
    return value


def scatter_sum(value, axis):
    size = lax.axis_size(axis)
    rows, cols = value.shape
    me = lax.axis_index(axis)
    held = value.reshape(rows, size, cols // size)
    for mask, bit in reversed(axis_stages(axis)):
        half = held.shape[1] // 2
        lower, upper = held[:, :half], held[:, half:]
        mine_upper = (me & bit) != 0
        keep = jnp.where(mine_upper, upper, lower)
        send = jnp.where(mine_upper, lower, upper)
        held = keep + partner_swap(send.astype(jnp.bfloat16), axis, mask).astype(jnp.float32)
    return held.reshape(rows, cols // size)


def rms_norm(values, gain_vec):
    mean_square = jnp.mean(values * values, axis=-1, keepdims=True)
    return (values * lax.rsqrt(mean_square + epsilon) * gain_vec).astype(jnp.bfloat16)


def rotate(vectors, positions):
    half_size = vectors.shape[-1] // 2
    frequency = 10000.0 ** (-2.0 * jnp.arange(half_size, dtype=jnp.float32) / vectors.shape[-1])
    angles = positions[:, None] * frequency[None, :]
    cos_part = jnp.cos(angles)[:, None, :]
    sin_part = jnp.sin(angles)[:, None, :]
    first_half = vectors[..., :half_size]
    second = vectors[..., half_size:]
    return jnp.concatenate(
        [first_half * cos_part - second * sin_part, second * cos_part + first_half * sin_part],
        axis=-1,
    )


def combine_parts(first_part, second_part):
    width = first_part.shape[-1] - 128
    heads = width // 128
    first_top, first_sum = first_part[:, width : width + heads], first_part[:, width + heads : width + 2 * heads]
    second_top = second_part[:, width : width + heads]
    second_sum = second_part[:, width + heads : width + 2 * heads]
    larger = jnp.maximum(first_top, second_top)
    first_factor = jnp.exp(first_top - larger)
    second_factor = jnp.exp(second_top - larger)
    rows = first_part.shape[0]
    head_size = width // heads
    acc = (
        first_part[:, :width].reshape(rows, heads, head_size) * first_factor[..., None]
        + second_part[:, :width].reshape(rows, heads, head_size) * second_factor[..., None]
    )
    stats = jnp.concatenate(
        [larger, first_sum * first_factor + second_sum * second_factor, first_part[:, width + 2 * heads :]],
        axis=-1,
    )
    return jnp.concatenate([acc.reshape(rows, width), stats], axis=-1)


def across_mlp(partial_value):
    return joined(partial_value, "mlp", lambda first, second: first + second)


def across_mlp_narrow(partial_value):
    for mask, _ in axis_stages("mlp"):
        sent = partner_swap(partial_value.astype(jnp.bfloat16), "mlp", mask)
        partial_value = partial_value + sent.astype(jnp.float32)
    return partial_value


def per_device(
    tokens,
    lengths,
    leaving,
    owner,
    cache,
    conv_state,
    lru_state,
    gain_rec,
    w_input,
    w_branch,
    conv_weight,
    conv_bias,
    gate_weight,
    gate_bias,
    decay_param,
    w_rec_out,
    gain_att,
    w_query,
    w_keyval,
    w_attn_out,
    gain_mlp,
    w_gate,
    w_up,
    w_down,
):
    req_rows = tokens.shape[0]
    width = tokens.shape[1]
    leavers = leaving.shape[1]
    groups = lax.axis_size("req")
    own_group = lax.axis_index("req")
    mlp_id = lax.axis_index("mlp")
    rank_ids = jnp.arange(leavers, dtype=jnp.int32)
    group_ids = jnp.arange(groups, dtype=jnp.int32)
    my_leave = leaving[own_group]
    my_owner = owner[own_group]
    to_me = owner == own_group
    anchor = jnp.sum(jnp.where(to_me, group_ids[:, None], 0), axis=0)
    anchor_leave = jnp.sum(jnp.where(to_me, leaving, 0), axis=0)
    page_rows = cache.shape[1]
    conv_rows = conv_state.shape[1]
    states = jnp.concatenate([conv_state, lru_state[:, None, :]], axis=1)
    to_group = my_owner[None, :] == group_ids[:, None]
    send_slot = jnp.sum(jnp.where(to_group, my_leave[None, :], 0), axis=1)
    got_states = lax.all_to_all(
        jnp.take(states, send_slot, axis=0, mode="clip"), "req", 0, 0, tiled=True
    )
    got_cache = lax.all_to_all(
        jnp.take(cache, send_slot, axis=0, mode="clip"), "req", 0, 0, tiled=True
    )
    local_ids = jnp.arange(req_rows, dtype=jnp.int32)
    match_slot = my_leave[None, :] == local_ids[:, None]
    arriving = jnp.any(match_slot, axis=1)
    arrive_from = jnp.sum(jnp.where(match_slot, anchor[None, :], 0), axis=1)
    anchor_slot = jnp.sum(
        jnp.where(match_slot, (anchor * req_rows + anchor_leave)[None, :], 0), axis=1
    )
    moved_states = jnp.where(
        arriving[:, None, None], jnp.take(got_states, arrive_from, axis=0, mode="clip"), states
    )
    moved_cache = jnp.where(
        arriving[:, None, None], jnp.take(got_cache, arrive_from, axis=0, mode="clip"), cache
    )
    moved_conv = moved_states[:, :conv_rows]
    moved_lru = moved_states[:, conv_rows]
    source_slot = jnp.where(arriving, anchor_slot, own_group * req_rows + local_ids)
    position = jnp.take(lengths, source_slot, mode="clip")
    inputs = tokens.astype(jnp.float32)
    normed = rms_norm(inputs, gain_rec)
    branch_in = jnp.dot(normed, w_input, preferred_element_type=jnp.float32).astype(jnp.bfloat16)
    branch = jax.nn.gelu(
        jnp.dot(normed, w_branch, preferred_element_type=jnp.float32), approximate=True
    )
    history = moved_conv.astype(jnp.float32)
    conv_in = (
        jnp.sum(conv_weight[:-1][None] * history, axis=1)
        + conv_weight[-1] * branch_in.astype(jnp.float32)
        + conv_bias
    )
    channels = conv_in.shape[1]
    block_size = gate_weight.shape[2]
    blocks = channels // block_size
    gate_pre = (
        jnp.einsum(
            "snb,gnbc->gsnc",
            conv_in.reshape(req_rows, blocks, block_size),
            gate_weight.astype(jnp.float32),
        ).reshape(2, req_rows, channels)
        + gate_bias[:, None, :]
    )
    rate_gate = jax.nn.sigmoid(gate_pre[0])
    admit_gate = jax.nn.sigmoid(gate_pre[1])
    log_decay = -8.0 * rate_gate * jax.nn.softplus(-decay_param)
    new_state = (
        jnp.exp(log_decay) * moved_lru.astype(jnp.float32)
        + jnp.sqrt(-jnp.expm1(2.0 * log_decay)) * admit_gate * conv_in
    )
    lru_out = new_state.astype(jnp.bfloat16)
    conv_out = jnp.concatenate([moved_conv[:, 1:], branch_in[:, None, :]], axis=1)
    gated_rec = (new_state * branch).astype(jnp.bfloat16)
    resid_one = inputs + across_mlp_narrow(
        jnp.dot(gated_rec, w_rec_out, preferred_element_type=jnp.float32)
    )
    head_size = w_keyval.shape[1] // 2
    heads = width // head_size
    slice_rows = w_query.shape[0]
    normed_att = rms_norm(resid_one, gain_att)
    query_part = jnp.dot(
        lax.dynamic_slice_in_dim(normed_att, mlp_id * slice_rows, slice_rows, 1),
        w_query,
        preferred_element_type=jnp.float32,
    )
    query_full = across_mlp_narrow(query_part)
    where_pos = position.astype(jnp.float32)
    queries = rotate(query_full.reshape(req_rows, heads, head_size), where_pos).astype(jnp.bfloat16)
    key_value = jnp.dot(normed_att, w_keyval, preferred_element_type=jnp.float32)
    key_new = rotate(key_value[:, None, :head_size], where_pos)[:, 0].astype(jnp.bfloat16)
    value_new = key_value[:, head_size:].astype(jnp.bfloat16)
    window = page_rows * lax.axis_size("mlp")
    score_scale = 1.0 / math.sqrt(head_size)
    slot_ids = mlp_id * page_rows + jnp.arange(page_rows, dtype=jnp.int32)[None, :]
    current = position[:, None]
    held_pos = current - 1 - jnp.mod(current - 1 - slot_ids, window)
    usable = ((held_pos >= 0) & (held_pos != current - window))[:, None, :]

    def window_part(query_rows, rows, usable_rows):
        scores = (
            jnp.einsum(
                "shd,swd->shw",
                query_rows,
                rows[..., :head_size],
                preferred_element_type=jnp.float32,
            )
            * score_scale
        )
        top = jnp.max(jnp.where(usable_rows, scores, -1e30), axis=-1)
        weights = jnp.where(usable_rows, jnp.exp(scores - top[..., None]), 0.0)
        acc = jnp.einsum(
            "shw,swd->shd",
            weights.astype(jnp.bfloat16),
            rows[..., head_size:],
            preferred_element_type=jnp.float32,
        )
        return top, jnp.sum(weights, axis=-1), acc

    stay_top, stay_sum, stay_acc = window_part(queries, cache, usable)
    came_top, came_sum, came_acc = window_part(
        jnp.take(queries, my_leave, axis=0, mode="clip"),
        jnp.take(got_cache, anchor, axis=0, mode="clip"),
        jnp.take(usable, my_leave, axis=0, mode="clip"),
    )
    arrive_rank = jnp.sum(jnp.where(match_slot, rank_ids[None, :], 0), axis=1)
    local_top = jnp.where(
        arriving[:, None], jnp.take(came_top, arrive_rank, axis=0, mode="clip"), stay_top
    )
    local_sum = jnp.where(
        arriving[:, None], jnp.take(came_sum, arrive_rank, axis=0, mode="clip"), stay_sum
    )
    local_acc = jnp.where(
        arriving[:, None, None], jnp.take(came_acc, arrive_rank, axis=0, mode="clip"), stay_acc
    )
    stat_pad = jnp.zeros((req_rows, 128 - 2 * heads), jnp.float32)
    merged = joined(
        jnp.concatenate(
            [local_acc.reshape(req_rows, width), local_top, local_sum, stat_pad], axis=-1
        ),
        "mlp",
        combine_parts,
    )
    merged_acc = merged[:, :width].reshape(req_rows, heads, head_size)
    merged_top = merged[:, width : width + heads]
    merged_sum = merged[:, width + heads : width + 2 * heads]
    own_score = (
        jnp.sum(queries.astype(jnp.float32) * key_new.astype(jnp.float32)[:, None, :], axis=-1)
        * score_scale
    )
    top_score = jnp.maximum(merged_top, own_score)
    rescale = jnp.exp(merged_top - top_score)
    own_weight = jnp.exp(own_score - top_score)
    own_rounded = lax.optimization_barrier(own_weight.astype(jnp.bfloat16)).astype(jnp.float32)
    denominator = merged_sum * rescale + own_weight
    numerator = (
        merged_acc * rescale[..., None]
        + own_rounded[..., None] * value_new.astype(jnp.float32)[:, None, :]
    )
    attended = (numerator / denominator[..., None]).reshape(req_rows, width).astype(jnp.bfloat16)
    attn_part = jnp.dot(
        lax.dynamic_slice_in_dim(attended, mlp_id * slice_rows, slice_rows, 1),
        w_attn_out,
        preferred_element_type=jnp.float32,
    )
    resid_two = resid_one + across_mlp_narrow(attn_part)
    normed_mlp = rms_norm(resid_two, gain_mlp)
    gate_act = jax.nn.gelu(
        jnp.dot(normed_mlp, w_gate, preferred_element_type=jnp.float32), approximate=True
    )
    hidden = (gate_act * jnp.dot(normed_mlp, w_up, preferred_element_type=jnp.float32)).astype(
        jnp.bfloat16
    )
    down_part = jnp.dot(hidden, w_down, preferred_element_type=jnp.float32)
    share = scatter_sum(down_part, "mlp")
    share_cols = share.shape[1]
    hidden_out = (
        lax.dynamic_slice_in_dim(resid_two, mlp_id * share_cols, share_cols, 1) + share
    ).astype(jnp.bfloat16)
    write_row = jnp.concatenate([key_new, value_new], axis=-1)
    row_hit = slot_ids == jnp.mod(current, window)
    cache_out = jnp.where(row_hit[:, :, None], write_row[:, None, :], moved_cache)
    return (hidden_out, cache_out, conv_out, lru_out)


def solution(mesh):
    placed = (
        P("req", None),
        P(),
        P(),
        P(),
        P("req", "mlp", None),
        P("req", None, "mlp"),
        P("req", "mlp"),
        P(),
        P(None, "mlp"),
        P(None, "mlp"),
        P(None, "mlp"),
        P("mlp"),
        P(None, "mlp", None, None),
        P(None, "mlp"),
        P("mlp"),
        P("mlp", None),
        P(),
        P("mlp", None),
        P(),
        P("mlp", None),
        P(),
        P(None, "mlp"),
        P(None, "mlp"),
        P("mlp", None),
    )
    return jax.shard_map(
        per_device,
        mesh=mesh,
        in_specs=placed,
        out_specs=(P("req", "mlp"), P("req", "mlp", None), P("req", None, "mlp"), P("req", "mlp")),
        check_vma=False,
    )
```

```python
import math

import jax
import jax.numpy as jnp
from jax import lax
from jax.sharding import PartitionSpec as P

epsilon = 1e-06


def partner_swap(value, axis, bit):
    size = lax.axis_size(axis)
    pairs = [(j, j ^ bit) for j in range(size)]
    return jax.tree.map(lambda part: lax.ppermute(part, axis, pairs), value)


def axis_bits(axis):
    size = lax.axis_size(axis)
    assert size & (size - 1) == 0
    bits = []
    bit = 1
    while bit < size:
        bits.append(bit)
        bit *= 2
    return bits


def axis_stages(axis):
    stages = []
    for bit in axis_bits(axis):
        mask = bit | (bit // 2) if bit == 2 else bit
        stages.append((mask, bit))
    return stages


def joined(value, axis, join):
    for mask, _ in axis_stages(axis):
        value = join(value, partner_swap(value, axis, mask))
    return value


def scatter_sum(value, axis):
    size = lax.axis_size(axis)
    rows, cols = value.shape
    me = lax.axis_index(axis)
    held = value.reshape(rows, size, cols // size)
    for mask, bit in reversed(axis_stages(axis)):
        half = held.shape[1] // 2
        lower, upper = held[:, :half], held[:, half:]
        mine_upper = (me & bit) != 0
        keep = jnp.where(mine_upper, upper, lower)
        send = jnp.where(mine_upper, lower, upper)
        held = keep + partner_swap(send.astype(jnp.bfloat16), axis, mask).astype(jnp.float32)
    return held.reshape(rows, cols // size)


def rms_norm(values, gain_vec):
    mean_square = jnp.mean(values * values, axis=-1, keepdims=True)
    return (values * lax.rsqrt(mean_square + epsilon) * gain_vec).astype(jnp.bfloat16)


def rotate(vectors, positions):
    half_size = vectors.shape[-1] // 2
    frequency = 10000.0 ** (-2.0 * jnp.arange(half_size, dtype=jnp.float32) / vectors.shape[-1])
    angles = positions[:, None] * frequency[None, :]
    cos_part = jnp.cos(angles)[:, None, :]
    sin_part = jnp.sin(angles)[:, None, :]
    first_half = vectors[..., :half_size]
    second = vectors[..., half_size:]
    return jnp.concatenate(
        [first_half * cos_part - second * sin_part, second * cos_part + first_half * sin_part],
        axis=-1,
    )


def combine_parts(first_part, second_part):
    width = first_part.shape[-1] - 128
    heads = width // 128
    first_top, first_sum = first_part[:, width : width + heads], first_part[:, width + heads : width + 2 * heads]
    second_top = second_part[:, width : width + heads]
    second_sum = second_part[:, width + heads : width + 2 * heads]
    larger = jnp.maximum(first_top, second_top)
    first_factor = jnp.exp(first_top - larger)
    second_factor = jnp.exp(second_top - larger)
    rows = first_part.shape[0]
    head_size = width // heads
    acc = (
        first_part[:, :width].reshape(rows, heads, head_size) * first_factor[..., None]
        + second_part[:, :width].reshape(rows, heads, head_size) * second_factor[..., None]
    )
    stats = jnp.concatenate(
        [larger, first_sum * first_factor + second_sum * second_factor, first_part[:, width + 2 * heads :]],
        axis=-1,
    )
    return jnp.concatenate([acc.reshape(rows, width), stats], axis=-1)


def across_mlp(partial_value):
    return joined(partial_value, "mlp", lambda first, second: first + second)


def across_mlp_narrow(partial_value):
    for mask, _ in axis_stages("mlp"):
        sent = partner_swap(partial_value.astype(jnp.bfloat16), "mlp", mask)
        partial_value = partial_value + sent.astype(jnp.float32)
    return partial_value


def per_device(
    tokens,
    lengths,
    leaving,
    owner,
    cache,
    conv_state,
    lru_state,
    gain_rec,
    w_input,
    w_branch,
    conv_weight,
    conv_bias,
    gate_weight,
    gate_bias,
    decay_param,
    w_rec_out,
    gain_att,
    w_query,
    w_keyval,
    w_attn_out,
    gain_mlp,
    w_gate,
    w_up,
    w_down,
):
    req_rows = tokens.shape[0]
    width = tokens.shape[1]
    leavers = leaving.shape[1]
    groups = lax.axis_size("req")
    own_group = lax.axis_index("req")
    mlp_id = lax.axis_index("mlp")
    rank_ids = jnp.arange(leavers, dtype=jnp.int32)
    group_ids = jnp.arange(groups, dtype=jnp.int32)
    my_leave = leaving[own_group]
    my_owner = owner[own_group]
    to_me = owner == own_group
    anchor = jnp.sum(jnp.where(to_me, group_ids[:, None], 0), axis=0)
    anchor_leave = jnp.sum(jnp.where(to_me, leaving, 0), axis=0)
    page_rows = cache.shape[1]
    conv_rows = conv_state.shape[1]
    states = jnp.concatenate([conv_state, lru_state[:, None, :]], axis=1)
    to_group = my_owner[None, :] == group_ids[:, None]
    send_slot = jnp.sum(jnp.where(to_group, my_leave[None, :], 0), axis=1)
    states_send, cache_send = lax.optimization_barrier(
        (
            jnp.take(states, send_slot, axis=0, mode="clip"),
            jnp.take(cache, send_slot, axis=0, mode="clip"),
        )
    )
    got_states = lax.all_to_all(states_send, "req", 0, 0, tiled=True)
    got_cache = lax.all_to_all(cache_send, "req", 0, 0, tiled=True)
    got_states, tokens, lengths = lax.optimization_barrier((got_states, tokens, lengths))
    local_ids = jnp.arange(req_rows, dtype=jnp.int32)
    match_slot = my_leave[None, :] == local_ids[:, None]
    arriving = jnp.any(match_slot, axis=1)
    arrive_from = jnp.sum(jnp.where(match_slot, anchor[None, :], 0), axis=1)
    anchor_slot = jnp.sum(
        jnp.where(match_slot, (anchor * req_rows + anchor_leave)[None, :], 0), axis=1
    )
    moved_states = jnp.where(
        arriving[:, None, None], jnp.take(got_states, arrive_from, axis=0, mode="clip"), states
    )
    moved_cache = jnp.where(
        arriving[:, None, None], jnp.take(got_cache, arrive_from, axis=0, mode="clip"), cache
    )
    moved_conv = moved_states[:, :conv_rows]
    moved_lru = moved_states[:, conv_rows]
    source_slot = jnp.where(arriving, anchor_slot, own_group * req_rows + local_ids)
    position = jnp.take(lengths, source_slot, mode="clip")
    inputs = tokens.astype(jnp.float32)
    normed = rms_norm(inputs, gain_rec)
    branch_in = jnp.dot(normed, w_input, preferred_element_type=jnp.float32).astype(jnp.bfloat16)
    branch = jax.nn.gelu(
        jnp.dot(normed, w_branch, preferred_element_type=jnp.float32), approximate=True
    )
    history = moved_conv.astype(jnp.float32)
    conv_in = (
        jnp.sum(conv_weight[:-1][None] * history, axis=1)
        + conv_weight[-1] * branch_in.astype(jnp.float32)
        + conv_bias
    )
    channels = conv_in.shape[1]
    block_size = gate_weight.shape[2]
    blocks = channels // block_size
    gate_pre = (
        jnp.einsum(
            "snb,gnbc->gsnc",
            conv_in.reshape(req_rows, blocks, block_size),
            gate_weight.astype(jnp.float32),
        ).reshape(2, req_rows, channels)
        + gate_bias[:, None, :]
    )
    rate_gate = jax.nn.sigmoid(gate_pre[0])
    admit_gate = jax.nn.sigmoid(gate_pre[1])
    log_decay = -8.0 * rate_gate * jax.nn.softplus(-decay_param)
    new_state = (
        jnp.exp(log_decay) * moved_lru.astype(jnp.float32)
        + jnp.sqrt(-jnp.expm1(2.0 * log_decay)) * admit_gate * conv_in
    )
    lru_out = new_state.astype(jnp.bfloat16)
    conv_out = jnp.concatenate([moved_conv[:, 1:], branch_in[:, None, :]], axis=1)
    gated_rec = (new_state * branch).astype(jnp.bfloat16)
    resid_one = inputs + across_mlp_narrow(
        jnp.dot(gated_rec, w_rec_out, preferred_element_type=jnp.float32)
    )
    head_size = w_keyval.shape[1] // 2
    heads = width // head_size
    slice_rows = w_query.shape[0]
    normed_att = rms_norm(resid_one, gain_att)
    query_part = jnp.dot(
        lax.dynamic_slice_in_dim(normed_att, mlp_id * slice_rows, slice_rows, 1),
        w_query,
        preferred_element_type=jnp.float32,
    )
    query_full = across_mlp_narrow(query_part)
    where_pos = position.astype(jnp.float32)
    queries = rotate(query_full.reshape(req_rows, heads, head_size), where_pos).astype(jnp.bfloat16)
    key_value = jnp.dot(normed_att, w_keyval, preferred_element_type=jnp.float32)
    key_new = rotate(key_value[:, None, :head_size], where_pos)[:, 0].astype(jnp.bfloat16)
    value_new = key_value[:, head_size:].astype(jnp.bfloat16)
    window = page_rows * lax.axis_size("mlp")
    score_scale = 1.0 / math.sqrt(head_size)
    scores = (
        jnp.einsum(
            "shd,swd->shw",
            queries,
            moved_cache[..., :head_size],
            preferred_element_type=jnp.float32,
        )
        * score_scale
    )
    slot_ids = mlp_id * page_rows + jnp.arange(page_rows, dtype=jnp.int32)[None, :]
    current = position[:, None]
    held_pos = current - 1 - jnp.mod(current - 1 - slot_ids, window)
    usable = ((held_pos >= 0) & (held_pos != current - window))[:, None, :]
    local_top = jnp.max(jnp.where(usable, scores, -1e30), axis=-1)
    weights = jnp.where(usable, jnp.exp(scores - local_top[..., None]), 0.0)
    local_sum = jnp.sum(weights, axis=-1)
    local_acc = jnp.einsum(
        "shw,swd->shd",
        weights.astype(jnp.bfloat16),
        moved_cache[..., head_size:],
        preferred_element_type=jnp.float32,
    )
    stat_pad = jnp.zeros((req_rows, 128 - 2 * heads), jnp.float32)
    merged = joined(
        jnp.concatenate(
            [local_acc.reshape(req_rows, width), local_top, local_sum, stat_pad], axis=-1
        ),
        "mlp",
        combine_parts,
    )
    merged_acc = merged[:, :width].reshape(req_rows, heads, head_size)
    merged_top = merged[:, width : width + heads]
    merged_sum = merged[:, width + heads : width + 2 * heads]
    own_score = (
        jnp.sum(queries.astype(jnp.float32) * key_new.astype(jnp.float32)[:, None, :], axis=-1)
        * score_scale
    )
    top_score = jnp.maximum(merged_top, own_score)
    rescale = jnp.exp(merged_top - top_score)
    own_weight = jnp.exp(own_score - top_score)
    own_rounded = lax.optimization_barrier(own_weight.astype(jnp.bfloat16)).astype(jnp.float32)
    denominator = merged_sum * rescale + own_weight
    numerator = (
        merged_acc * rescale[..., None]
        + own_rounded[..., None] * value_new.astype(jnp.float32)[:, None, :]
    )
    attended = (numerator / denominator[..., None]).reshape(req_rows, width).astype(jnp.bfloat16)
    attn_part = jnp.dot(
        lax.dynamic_slice_in_dim(attended, mlp_id * slice_rows, slice_rows, 1),
        w_attn_out,
        preferred_element_type=jnp.float32,
    )
    resid_two = resid_one + across_mlp_narrow(attn_part)
    normed_mlp = rms_norm(resid_two, gain_mlp)
    gate_act = jax.nn.gelu(
        jnp.dot(normed_mlp, w_gate, preferred_element_type=jnp.float32), approximate=True
    )
    hidden = (gate_act * jnp.dot(normed_mlp, w_up, preferred_element_type=jnp.float32)).astype(
        jnp.bfloat16
    )
    down_part = jnp.dot(hidden, w_down, preferred_element_type=jnp.float32)
    share = scatter_sum(down_part, "mlp")
    share_cols = share.shape[1]
    hidden_out = (
        lax.dynamic_slice_in_dim(resid_two, mlp_id * share_cols, share_cols, 1) + share
    ).astype(jnp.bfloat16)
    write_row = jnp.concatenate([key_new, value_new], axis=-1)
    row_hit = slot_ids == jnp.mod(current, window)
    cache_out = jnp.where(row_hit[:, :, None], write_row[:, None, :], moved_cache)
    return (hidden_out, cache_out, conv_out, lru_out)


def solution(mesh):
    placed = (
        P("req", None),
        P(),
        P(),
        P(),
        P("req", "mlp", None),
        P("req", None, "mlp"),
        P("req", "mlp"),
        P(),
        P(None, "mlp"),
        P(None, "mlp"),
        P(None, "mlp"),
        P("mlp"),
        P(None, "mlp", None, None),
        P(None, "mlp"),
        P("mlp"),
        P("mlp", None),
        P(),
        P("mlp", None),
        P(),
        P("mlp", None),
        P(),
        P(None, "mlp"),
        P(None, "mlp"),
        P("mlp", None),
    )
    return jax.shard_map(
        per_device,
        mesh=mesh,
        in_specs=placed,
        out_specs=(P("req", "mlp"), P("req", "mlp", None), P("req", None, "mlp"), P("req", "mlp")),
        check_vma=False,
    )
```

```python
import math

import jax
import jax.numpy as jnp
from jax import lax
from jax.sharding import PartitionSpec as P

epsilon = 1e-06


def partner_swap(value, axis, bit):
    size = lax.axis_size(axis)
    pairs = [(j, j ^ bit) for j in range(size)]
    return jax.tree.map(lambda part: lax.ppermute(part, axis, pairs), value)


def axis_bits(axis):
    size = lax.axis_size(axis)
    assert size & (size - 1) == 0
    bits = []
    bit = 1
    while bit < size:
        bits.append(bit)
        bit *= 2
    return bits


def axis_stages(axis):
    stages = []
    for bit in axis_bits(axis):
        mask = bit | (bit // 2) if bit == 2 else bit
        stages.append((mask, bit))
    return stages


def joined(value, axis, join):
    for mask, _ in axis_stages(axis):
        value = join(value, partner_swap(value, axis, mask))
    return value


def scatter_sum(value, axis):
    size = lax.axis_size(axis)
    rows, cols = value.shape
    me = lax.axis_index(axis)
    held = value.reshape(rows, size, cols // size)
    for mask, bit in reversed(axis_stages(axis)):
        half = held.shape[1] // 2
        lower, upper = held[:, :half], held[:, half:]
        mine_upper = (me & bit) != 0
        keep = jnp.where(mine_upper, upper, lower)
        send = jnp.where(mine_upper, lower, upper)
        held = keep + partner_swap(send.astype(jnp.bfloat16), axis, mask).astype(jnp.float32)
    return held.reshape(rows, cols // size)


def rms_norm(values, gain_vec):
    mean_square = jnp.mean(values * values, axis=-1, keepdims=True)
    return (values * lax.rsqrt(mean_square + epsilon) * gain_vec).astype(jnp.bfloat16)


def rotate(vectors, positions):
    half_size = vectors.shape[-1] // 2
    frequency = 10000.0 ** (-2.0 * jnp.arange(half_size, dtype=jnp.float32) / vectors.shape[-1])
    angles = positions[:, None] * frequency[None, :]
    cos_part = jnp.cos(angles)[:, None, :]
    sin_part = jnp.sin(angles)[:, None, :]
    first_half = vectors[..., :half_size]
    second = vectors[..., half_size:]
    return jnp.concatenate(
        [first_half * cos_part - second * sin_part, second * cos_part + first_half * sin_part],
        axis=-1,
    )


def combine_parts(first_part, second_part):
    width = first_part.shape[-1] - 128
    heads = width // 128
    first_top, first_sum = first_part[:, width : width + heads], first_part[:, width + heads : width + 2 * heads]
    second_top = second_part[:, width : width + heads]
    second_sum = second_part[:, width + heads : width + 2 * heads]
    larger = jnp.maximum(first_top, second_top)
    first_factor = jnp.exp(first_top - larger)
    second_factor = jnp.exp(second_top - larger)
    rows = first_part.shape[0]
    head_size = width // heads
    acc = (
        first_part[:, :width].reshape(rows, heads, head_size) * first_factor[..., None]
        + second_part[:, :width].reshape(rows, heads, head_size) * second_factor[..., None]
    )
    stats = jnp.concatenate(
        [larger, first_sum * first_factor + second_sum * second_factor, first_part[:, width + 2 * heads :]],
        axis=-1,
    )
    return jnp.concatenate([acc.reshape(rows, width), stats], axis=-1)


def across_mlp(partial_value):
    return joined(partial_value, "mlp", lambda first, second: first + second)


def across_mlp_narrow(partial_value):
    for mask, _ in axis_stages("mlp"):
        sent = partner_swap(partial_value.astype(jnp.bfloat16), "mlp", mask)
        partial_value = partial_value + sent.astype(jnp.float32)
    return partial_value


def per_device(
    tokens,
    lengths,
    leaving,
    owner,
    cache,
    conv_state,
    lru_state,
    gain_rec,
    w_input,
    w_branch,
    conv_weight,
    conv_bias,
    gate_weight,
    gate_bias,
    decay_param,
    w_rec_out,
    gain_att,
    w_query,
    w_keyval,
    w_attn_out,
    gain_mlp,
    w_gate,
    w_up,
    w_down,
):
    req_rows = tokens.shape[0]
    width = tokens.shape[1]
    leavers = leaving.shape[1]
    groups = lax.axis_size("req")
    own_group = lax.axis_index("req")
    mlp_id = lax.axis_index("mlp")
    rank_ids = jnp.arange(leavers, dtype=jnp.int32)
    group_ids = jnp.arange(groups, dtype=jnp.int32)
    my_leave = leaving[own_group]
    my_owner = owner[own_group]
    to_me = owner == own_group
    anchor = jnp.sum(jnp.where(to_me, group_ids[:, None], 0), axis=0)
    anchor_leave = jnp.sum(jnp.where(to_me, leaving, 0), axis=0)
    page_rows = cache.shape[1]
    conv_rows = conv_state.shape[1]
    states = jnp.concatenate([conv_state, lru_state[:, None, :]], axis=1)
    to_group = my_owner[None, :] == group_ids[:, None]
    send_slot = jnp.sum(jnp.where(to_group, my_leave[None, :], 0), axis=1)
    states_send, cache_send = lax.optimization_barrier(
        (
            jnp.take(states, send_slot, axis=0, mode="clip"),
            jnp.take(cache, send_slot, axis=0, mode="clip"),
        )
    )
    got_states = lax.all_to_all(states_send, "req", 0, 0, tiled=True)
    got_cache = lax.all_to_all(cache_send, "req", 0, 0, tiled=True)
    got_states, tokens, lengths = lax.optimization_barrier((got_states, tokens, lengths))
    local_ids = jnp.arange(req_rows, dtype=jnp.int32)
    match_slot = my_leave[None, :] == local_ids[:, None]
    arriving = jnp.any(match_slot, axis=1)
    arrive_from = jnp.sum(jnp.where(match_slot, anchor[None, :], 0), axis=1)
    anchor_slot = jnp.sum(
        jnp.where(match_slot, (anchor * req_rows + anchor_leave)[None, :], 0), axis=1
    )
    moved_states = jnp.where(
        arriving[:, None, None], jnp.take(got_states, arrive_from, axis=0, mode="clip"), states
    )
    moved_cache = jnp.where(
        arriving[:, None, None], jnp.take(got_cache, arrive_from, axis=0, mode="clip"), cache
    )
    moved_conv = moved_states[:, :conv_rows]
    moved_lru = moved_states[:, conv_rows]
    source_slot = jnp.where(arriving, anchor_slot, own_group * req_rows + local_ids)
    position = jnp.take(lengths, source_slot, mode="clip")
    inputs = tokens.astype(jnp.float32)
    normed = rms_norm(inputs, gain_rec)
    branch_in = jnp.dot(normed, w_input, preferred_element_type=jnp.float32).astype(jnp.bfloat16)
    branch = jax.nn.gelu(
        jnp.dot(normed, w_branch, preferred_element_type=jnp.float32), approximate=True
    )
    history = moved_conv.astype(jnp.float32)
    conv_in = (
        jnp.sum(conv_weight[:-1][None] * history, axis=1)
        + conv_weight[-1] * branch_in.astype(jnp.float32)
        + conv_bias
    )
    channels = conv_in.shape[1]
    block_size = gate_weight.shape[2]
    blocks = channels // block_size
    gate_pre = (
        jnp.einsum(
            "snb,gnbc->gsnc",
            conv_in.reshape(req_rows, blocks, block_size),
            gate_weight.astype(jnp.float32),
        ).reshape(2, req_rows, channels)
        + gate_bias[:, None, :]
    )
    rate_gate = jax.nn.sigmoid(gate_pre[0])
    admit_gate = jax.nn.sigmoid(gate_pre[1])
    log_decay = -8.0 * rate_gate * jax.nn.softplus(-decay_param)
    new_state = (
        jnp.exp(log_decay) * moved_lru.astype(jnp.float32)
        + jnp.sqrt(-jnp.expm1(2.0 * log_decay)) * admit_gate * conv_in
    )
    lru_out = new_state.astype(jnp.bfloat16)
    conv_out = jnp.concatenate([moved_conv[:, 1:], branch_in[:, None, :]], axis=1)
    gated_rec = (new_state * branch).astype(jnp.bfloat16)
    resid_one = inputs + across_mlp_narrow(
        jnp.dot(gated_rec, w_rec_out, preferred_element_type=jnp.float32)
    )
    head_size = w_keyval.shape[1] // 2
    heads = width // head_size
    slice_rows = w_query.shape[0]
    normed_att = rms_norm(resid_one, gain_att)
    query_part = jnp.dot(
        lax.dynamic_slice_in_dim(normed_att, mlp_id * slice_rows, slice_rows, 1),
        w_query,
        preferred_element_type=jnp.float32,
    )
    query_full = across_mlp_narrow(query_part)
    where_pos = position.astype(jnp.float32)
    queries = rotate(query_full.reshape(req_rows, heads, head_size), where_pos).astype(jnp.bfloat16)
    key_value = jnp.dot(normed_att, w_keyval, preferred_element_type=jnp.float32)
    key_new = rotate(key_value[:, None, :head_size], where_pos)[:, 0].astype(jnp.bfloat16)
    value_new = key_value[:, head_size:].astype(jnp.bfloat16)
    window = page_rows * lax.axis_size("mlp")
    score_scale = 1.0 / math.sqrt(head_size)
    scores = (
        jnp.einsum(
            "shd,swd->shw",
            queries,
            moved_cache[..., :head_size],
            preferred_element_type=jnp.float32,
        )
        * score_scale
    )
    slot_ids = mlp_id * page_rows + jnp.arange(page_rows, dtype=jnp.int32)[None, :]
    current = position[:, None]
    held_pos = current - 1 - jnp.mod(current - 1 - slot_ids, window)
    usable = ((held_pos >= 0) & (held_pos != current - window))[:, None, :]
    local_top = (
        jnp.max(jnp.where(usable, scores, -1e30), axis=-1).astype(jnp.bfloat16).astype(jnp.float32)
    )
    weights = jnp.where(usable, jnp.exp(scores - local_top[..., None]), 0.0)
    local_sum = jnp.sum(weights, axis=-1)
    local_acc = jnp.einsum(
        "shw,swd->shd",
        weights.astype(jnp.bfloat16),
        moved_cache[..., head_size:],
        preferred_element_type=jnp.float32,
    )
    stat_pad = jnp.zeros((req_rows, 128 - 2 * heads), jnp.float32)
    merged = jnp.concatenate(
        [local_acc.reshape(req_rows, width), local_top, local_sum, stat_pad], axis=-1
    )
    for mask, _ in axis_stages("mlp"):
        sent = partner_swap(merged.astype(jnp.bfloat16), "mlp", mask)
        merged = combine_parts(merged, sent.astype(jnp.float32))
    merged_acc = merged[:, :width].reshape(req_rows, heads, head_size)
    merged_top = merged[:, width : width + heads]
    merged_sum = merged[:, width + heads : width + 2 * heads]
    own_score = (
        jnp.sum(queries.astype(jnp.float32) * key_new.astype(jnp.float32)[:, None, :], axis=-1)
        * score_scale
    )
    top_score = jnp.maximum(merged_top, own_score)
    rescale = jnp.exp(merged_top - top_score)
    own_weight = jnp.exp(own_score - top_score)
    own_rounded = lax.optimization_barrier(own_weight.astype(jnp.bfloat16)).astype(jnp.float32)
    denominator = merged_sum * rescale + own_weight
    numerator = (
        merged_acc * rescale[..., None]
        + own_rounded[..., None] * value_new.astype(jnp.float32)[:, None, :]
    )
    attended = (numerator / denominator[..., None]).reshape(req_rows, width).astype(jnp.bfloat16)
    attn_part = jnp.dot(
        lax.dynamic_slice_in_dim(attended, mlp_id * slice_rows, slice_rows, 1),
        w_attn_out,
        preferred_element_type=jnp.float32,
    )
    resid_two = resid_one + across_mlp_narrow(attn_part)
    normed_mlp = rms_norm(resid_two, gain_mlp)
    gate_act = jax.nn.gelu(
        jnp.dot(normed_mlp, w_gate, preferred_element_type=jnp.float32), approximate=True
    )
    hidden = (gate_act * jnp.dot(normed_mlp, w_up, preferred_element_type=jnp.float32)).astype(
        jnp.bfloat16
    )
    down_part = jnp.dot(hidden, w_down, preferred_element_type=jnp.float32)
    share = scatter_sum(down_part, "mlp")
    share_cols = share.shape[1]
    hidden_out = (
        lax.dynamic_slice_in_dim(resid_two, mlp_id * share_cols, share_cols, 1) + share
    ).astype(jnp.bfloat16)
    write_row = jnp.concatenate([key_new, value_new], axis=-1)
    row_hit = slot_ids == jnp.mod(current, window)
    cache_out = jnp.where(row_hit[:, :, None], write_row[:, None, :], moved_cache)
    return (hidden_out, cache_out, conv_out, lru_out)


def solution(mesh):
    placed = (
        P("req", None),
        P(),
        P(),
        P(),
        P("req", "mlp", None),
        P("req", None, "mlp"),
        P("req", "mlp"),
        P(),
        P(None, "mlp"),
        P(None, "mlp"),
        P(None, "mlp"),
        P("mlp"),
        P(None, "mlp", None, None),
        P(None, "mlp"),
        P("mlp"),
        P("mlp", None),
        P(),
        P("mlp", None),
        P(),
        P("mlp", None),
        P(),
        P(None, "mlp"),
        P(None, "mlp"),
        P("mlp", None),
    )
    return jax.shard_map(
        per_device,
        mesh=mesh,
        in_specs=placed,
        out_specs=(P("req", "mlp"), P("req", "mlp", None), P("req", None, "mlp"), P("req", "mlp")),
        check_vma=False,
    )
```

```python
import math

import jax
import jax.numpy as jnp
from jax import lax
from jax.sharding import PartitionSpec as P

epsilon = 1e-06


def partner_swap(value, axis, bit):
    size = lax.axis_size(axis)
    pairs = [(j, j ^ bit) for j in range(size)]
    return jax.tree.map(lambda part: lax.ppermute(part, axis, pairs), value)


def axis_bits(axis):
    size = lax.axis_size(axis)
    assert size & (size - 1) == 0
    bits = []
    bit = 1
    while bit < size:
        bits.append(bit)
        bit *= 2
    return bits


def axis_stages(axis):
    stages = []
    for bit in axis_bits(axis):
        mask = bit | (bit // 2) if bit == 2 else bit
        stages.append((mask, bit))
    return stages


def joined(value, axis, join):
    for mask, _ in axis_stages(axis):
        value = join(value, partner_swap(value, axis, mask))
    return value


def scatter_sum(value, axis):
    me = lax.axis_index(axis)
    held = value
    for mask, bit in reversed(axis_stages(axis)):
        half = held.shape[1] // 2
        lower, upper = held[:, :half], held[:, half:]
        mine_upper = (me & bit) != 0
        keep = jnp.where(mine_upper, upper, lower)
        send = jnp.where(mine_upper, lower, upper)
        held = keep + partner_swap(send.astype(jnp.bfloat16), axis, mask).astype(jnp.float32)
    return held


def rms_norm(values, gain_vec):
    mean_square = jnp.mean(values * values, axis=-1, keepdims=True)
    return (values * lax.rsqrt(mean_square + epsilon) * gain_vec).astype(jnp.bfloat16)


def rotate(vectors, positions):
    half_size = vectors.shape[-1] // 2
    frequency = 10000.0 ** (-2.0 * jnp.arange(half_size, dtype=jnp.float32) / vectors.shape[-1])
    angles = positions[:, None] * frequency[None, :]
    cos_part = jnp.cos(angles)[:, None, :]
    sin_part = jnp.sin(angles)[:, None, :]
    first_half = vectors[..., :half_size]
    second = vectors[..., half_size:]
    return jnp.concatenate(
        [first_half * cos_part - second * sin_part, second * cos_part + first_half * sin_part],
        axis=-1,
    )


def combine_parts(first_part, second_part):
    width = first_part.shape[-1] - 128
    heads = width // 128
    first_top, first_sum = first_part[:, width : width + heads], first_part[:, width + heads : width + 2 * heads]
    second_top = second_part[:, width : width + heads]
    second_sum = second_part[:, width + heads : width + 2 * heads]
    larger = jnp.maximum(first_top, second_top)
    first_factor = jnp.exp(first_top - larger)
    second_factor = jnp.exp(second_top - larger)
    rows = first_part.shape[0]
    head_size = width // heads
    acc = (
        first_part[:, :width].reshape(rows, heads, head_size) * first_factor[..., None]
        + second_part[:, :width].reshape(rows, heads, head_size) * second_factor[..., None]
    )
    stats = jnp.concatenate(
        [larger, first_sum * first_factor + second_sum * second_factor, first_part[:, width + 2 * heads :]],
        axis=-1,
    )
    return jnp.concatenate([acc.reshape(rows, width), stats], axis=-1)


def across_mlp(partial_value):
    return joined(partial_value, "mlp", lambda first, second: first + second)


def across_mlp_narrow(partial_value):
    for mask, _ in axis_stages("mlp"):
        sent = partner_swap(partial_value.astype(jnp.bfloat16), "mlp", mask)
        partial_value = partial_value + sent.astype(jnp.float32)
    return partial_value


def per_device(
    tokens,
    lengths,
    leaving,
    owner,
    cache,
    conv_state,
    lru_state,
    gain_rec,
    w_input,
    w_branch,
    conv_weight,
    conv_bias,
    gate_weight,
    gate_bias,
    decay_param,
    w_rec_out,
    gain_att,
    w_query,
    w_keyval,
    w_attn_out,
    gain_mlp,
    w_gate,
    w_up,
    w_down,
):
    req_rows = tokens.shape[0]
    width = tokens.shape[1]
    leavers = leaving.shape[1]
    groups = lax.axis_size("req")
    own_group = lax.axis_index("req")
    mlp_id = lax.axis_index("mlp")
    rank_ids = jnp.arange(leavers, dtype=jnp.int32)
    group_ids = jnp.arange(groups, dtype=jnp.int32)
    my_leave = leaving[own_group]
    my_owner = owner[own_group]
    to_me = owner == own_group
    anchor = jnp.sum(jnp.where(to_me, group_ids[:, None], 0), axis=0)
    anchor_leave = jnp.sum(jnp.where(to_me, leaving, 0), axis=0)
    page_rows = cache.shape[1]
    conv_rows = conv_state.shape[1]
    states = jnp.concatenate([conv_state, lru_state[:, None, :]], axis=1)
    to_group = my_owner[None, :] == group_ids[:, None]
    send_slot = jnp.sum(jnp.where(to_group, my_leave[None, :], 0), axis=1)
    states_send, cache_send = lax.optimization_barrier(
        (
            jnp.take(states, send_slot, axis=0, mode="clip"),
            jnp.take(cache, send_slot, axis=0, mode="clip"),
        )
    )
    got_states = lax.all_to_all(states_send, "req", 0, 0, tiled=True)
    got_cache = lax.all_to_all(cache_send, "req", 0, 0, tiled=True)
    got_states, tokens, lengths = lax.optimization_barrier((got_states, tokens, lengths))
    local_ids = jnp.arange(req_rows, dtype=jnp.int32)
    match_slot = my_leave[None, :] == local_ids[:, None]
    arriving = jnp.any(match_slot, axis=1)
    arrive_from = jnp.sum(jnp.where(match_slot, anchor[None, :], 0), axis=1)
    anchor_slot = jnp.sum(
        jnp.where(match_slot, (anchor * req_rows + anchor_leave)[None, :], 0), axis=1
    )
    moved_states = jnp.where(
        arriving[:, None, None], jnp.take(got_states, arrive_from, axis=0, mode="clip"), states
    )
    moved_cache = jnp.where(
        arriving[:, None, None], jnp.take(got_cache, arrive_from, axis=0, mode="clip"), cache
    )
    moved_conv = moved_states[:, :conv_rows]
    moved_lru = moved_states[:, conv_rows]
    source_slot = jnp.where(arriving, anchor_slot, own_group * req_rows + local_ids)
    position = jnp.take(lengths, source_slot, mode="clip")
    inputs = tokens.astype(jnp.float32)
    normed = rms_norm(inputs, gain_rec)
    branch_in = jnp.dot(normed, w_input, preferred_element_type=jnp.float32).astype(jnp.bfloat16)
    branch = jax.nn.gelu(
        jnp.dot(normed, w_branch, preferred_element_type=jnp.float32), approximate=True
    )
    history = moved_conv.astype(jnp.float32)
    conv_in = (
        jnp.sum(conv_weight[:-1][None] * history, axis=1)
        + conv_weight[-1] * branch_in.astype(jnp.float32)
        + conv_bias
    )
    channels = conv_in.shape[1]
    block_size = gate_weight.shape[2]
    blocks = channels // block_size
    gate_pre = (
        jnp.einsum(
            "snb,gnbc->gsnc",
            conv_in.reshape(req_rows, blocks, block_size),
            gate_weight.astype(jnp.float32),
        ).reshape(2, req_rows, channels)
        + gate_bias[:, None, :]
    )
    rate_gate = jax.nn.sigmoid(gate_pre[0])
    admit_gate = jax.nn.sigmoid(gate_pre[1])
    log_decay = -8.0 * rate_gate * jax.nn.softplus(-decay_param)
    new_state = (
        jnp.exp(log_decay) * moved_lru.astype(jnp.float32)
        + jnp.sqrt(-jnp.expm1(2.0 * log_decay)) * admit_gate * conv_in
    )
    lru_out = new_state.astype(jnp.bfloat16)
    conv_out = jnp.concatenate([moved_conv[:, 1:], branch_in[:, None, :]], axis=1)
    gated_rec = (new_state * branch).astype(jnp.bfloat16)
    resid_one = inputs + across_mlp_narrow(
        jnp.dot(gated_rec, w_rec_out, preferred_element_type=jnp.float32)
    )
    head_size = w_keyval.shape[1] // 2
    heads = width // head_size
    slice_rows = w_query.shape[0]
    normed_att = rms_norm(resid_one, gain_att)
    query_part = jnp.dot(
        lax.dynamic_slice_in_dim(normed_att, mlp_id * slice_rows, slice_rows, 1),
        w_query,
        preferred_element_type=jnp.float32,
    )
    query_full = across_mlp_narrow(query_part)
    where_pos = position.astype(jnp.float32)
    queries = rotate(query_full.reshape(req_rows, heads, head_size), where_pos).astype(jnp.bfloat16)
    key_value = jnp.dot(normed_att, w_keyval, preferred_element_type=jnp.float32)
    key_new = rotate(key_value[:, None, :head_size], where_pos)[:, 0].astype(jnp.bfloat16)
    value_new = key_value[:, head_size:].astype(jnp.bfloat16)
    window = page_rows * lax.axis_size("mlp")
    score_scale = 1.0 / math.sqrt(head_size)
    scores = (
        jnp.einsum(
            "shd,swd->shw",
            queries,
            moved_cache[..., :head_size],
            preferred_element_type=jnp.float32,
        )
        * score_scale
    )
    slot_ids = mlp_id * page_rows + jnp.arange(page_rows, dtype=jnp.int32)[None, :]
    current = position[:, None]
    held_pos = current - 1 - jnp.mod(current - 1 - slot_ids, window)
    usable = ((held_pos >= 0) & (held_pos != current - window))[:, None, :]
    local_top = jnp.max(jnp.where(usable, scores, -1e30), axis=-1)
    weights = jnp.where(usable, jnp.exp(scores - local_top[..., None]), 0.0)
    local_sum = jnp.sum(weights, axis=-1)
    local_acc = jnp.einsum(
        "shw,swd->shd",
        weights.astype(jnp.bfloat16),
        moved_cache[..., head_size:],
        preferred_element_type=jnp.float32,
    )
    stat_pad = jnp.zeros((req_rows, 128 - 2 * heads), jnp.float32)
    merged = joined(
        jnp.concatenate(
            [local_acc.reshape(req_rows, width), local_top, local_sum, stat_pad], axis=-1
        ),
        "mlp",
        combine_parts,
    )
    merged_acc = merged[:, :width].reshape(req_rows, heads, head_size)
    merged_top = merged[:, width : width + heads]
    merged_sum = merged[:, width + heads : width + 2 * heads]
    own_score = (
        jnp.sum(queries.astype(jnp.float32) * key_new.astype(jnp.float32)[:, None, :], axis=-1)
        * score_scale
    )
    top_score = jnp.maximum(merged_top, own_score)
    rescale = jnp.exp(merged_top - top_score)
    own_weight = jnp.exp(own_score - top_score)
    own_rounded = lax.optimization_barrier(own_weight.astype(jnp.bfloat16)).astype(jnp.float32)
    denominator = merged_sum * rescale + own_weight
    numerator = (
        merged_acc * rescale[..., None]
        + own_rounded[..., None] * value_new.astype(jnp.float32)[:, None, :]
    )
    attended = (numerator / denominator[..., None]).reshape(req_rows, width).astype(jnp.bfloat16)
    attn_part = jnp.dot(
        lax.dynamic_slice_in_dim(attended, mlp_id * slice_rows, slice_rows, 1),
        w_attn_out,
        preferred_element_type=jnp.float32,
    )
    resid_two = resid_one + across_mlp_narrow(attn_part)
    normed_mlp = rms_norm(resid_two, gain_mlp)
    gate_act = jax.nn.gelu(
        jnp.dot(normed_mlp, w_gate, preferred_element_type=jnp.float32), approximate=True
    )
    hidden = (gate_act * jnp.dot(normed_mlp, w_up, preferred_element_type=jnp.float32)).astype(
        jnp.bfloat16
    )
    down_part = jnp.dot(hidden, w_down, preferred_element_type=jnp.float32)
    share = scatter_sum(down_part, "mlp")
    share_cols = share.shape[1]
    hidden_out = (
        lax.dynamic_slice_in_dim(resid_two, mlp_id * share_cols, share_cols, 1) + share
    ).astype(jnp.bfloat16)
    write_row = jnp.concatenate([key_new, value_new], axis=-1)
    row_hit = slot_ids == jnp.mod(current, window)
    cache_out = jnp.where(row_hit[:, :, None], write_row[:, None, :], moved_cache)
    return (hidden_out, cache_out, conv_out, lru_out)


def solution(mesh):
    placed = (
        P("req", None),
        P(),
        P(),
        P(),
        P("req", "mlp", None),
        P("req", None, "mlp"),
        P("req", "mlp"),
        P(),
        P(None, "mlp"),
        P(None, "mlp"),
        P(None, "mlp"),
        P("mlp"),
        P(None, "mlp", None, None),
        P(None, "mlp"),
        P("mlp"),
        P("mlp", None),
        P(),
        P("mlp", None),
        P(),
        P("mlp", None),
        P(),
        P(None, "mlp"),
        P(None, "mlp"),
        P("mlp", None),
    )
    return jax.shard_map(
        per_device,
        mesh=mesh,
        in_specs=placed,
        out_specs=(P("req", "mlp"), P("req", "mlp", None), P("req", None, "mlp"), P("req", "mlp")),
        check_vma=False,
    )
```

```python
import math

import jax
import jax.numpy as jnp
from jax import lax
from jax.sharding import PartitionSpec as P

epsilon = 1e-06


def partner_swap(value, axis, bit):
    size = lax.axis_size(axis)
    pairs = [(j, j ^ bit) for j in range(size)]
    return jax.tree.map(lambda part: lax.ppermute(part, axis, pairs), value)


def axis_bits(axis):
    size = lax.axis_size(axis)
    assert size & (size - 1) == 0
    bits = []
    bit = 1
    while bit < size:
        bits.append(bit)
        bit *= 2
    return bits


def axis_stages(axis):
    stages = []
    for bit in axis_bits(axis):
        mask = bit | (bit // 2) if bit == 2 else bit
        stages.append((mask, bit))
    return stages


def joined(value, axis, join):
    for mask, _ in axis_stages(axis):
        value = join(value, partner_swap(value, axis, mask))
    return value


def scatter_sum(value, axis):
    me = lax.axis_index(axis)
    held = value
    for mask, bit in reversed(axis_stages(axis)):
        half = held.shape[1] // 2
        lower, upper = held[:, :half], held[:, half:]
        mine_upper = (me & bit) != 0
        keep = jnp.where(mine_upper, upper, lower)
        send = jnp.where(mine_upper, lower, upper)
        held = keep + partner_swap(send.astype(jnp.bfloat16), axis, mask).astype(jnp.float32)
    return held


def rms_norm(values, gain_vec):
    mean_square = jnp.mean(values * values, axis=-1, keepdims=True)
    return (values * lax.rsqrt(mean_square + epsilon) * gain_vec).astype(jnp.bfloat16)


def rotate(vectors, positions):
    half_size = vectors.shape[-1] // 2
    frequency = 10000.0 ** (-2.0 * jnp.arange(half_size, dtype=jnp.float32) / vectors.shape[-1])
    angles = positions[:, None] * frequency[None, :]
    cos_part = jnp.cos(angles)[:, None, :]
    sin_part = jnp.sin(angles)[:, None, :]
    first_half = vectors[..., :half_size]
    second = vectors[..., half_size:]
    return jnp.concatenate(
        [first_half * cos_part - second * sin_part, second * cos_part + first_half * sin_part],
        axis=-1,
    )


def combine_parts(first_part, second_part):
    width = first_part.shape[-1] - 128
    heads = width // 128
    first_top, first_sum = first_part[:, width : width + heads], first_part[:, width + heads : width + 2 * heads]
    second_top = second_part[:, width : width + heads]
    second_sum = second_part[:, width + heads : width + 2 * heads]
    larger = jnp.maximum(first_top, second_top)
    first_factor = jnp.exp(first_top - larger)
    second_factor = jnp.exp(second_top - larger)
    rows = first_part.shape[0]
    head_size = width // heads
    acc = (
        first_part[:, :width].reshape(rows, heads, head_size) * first_factor[..., None]
        + second_part[:, :width].reshape(rows, heads, head_size) * second_factor[..., None]
    )
    stats = jnp.concatenate(
        [larger, first_sum * first_factor + second_sum * second_factor, first_part[:, width + 2 * heads :]],
        axis=-1,
    )
    return jnp.concatenate([acc.reshape(rows, width), stats], axis=-1)


def across_mlp(partial_value):
    return joined(partial_value, "mlp", lambda first, second: first + second)


def across_mlp_narrow(partial_value):
    for mask, _ in axis_stages("mlp"):
        sent = partner_swap(partial_value.astype(jnp.bfloat16), "mlp", mask)
        partial_value = partial_value + sent.astype(jnp.float32)
    return partial_value


def per_device(
    tokens,
    lengths,
    leaving,
    owner,
    cache,
    conv_state,
    lru_state,
    gain_rec,
    w_input,
    w_branch,
    conv_weight,
    conv_bias,
    gate_weight,
    gate_bias,
    decay_param,
    w_rec_out,
    gain_att,
    w_query,
    w_keyval,
    w_attn_out,
    gain_mlp,
    w_gate,
    w_up,
    w_down,
):
    req_rows = tokens.shape[0]
    width = tokens.shape[1]
    leavers = leaving.shape[1]
    groups = lax.axis_size("req")
    own_group = lax.axis_index("req")
    mlp_id = lax.axis_index("mlp")
    rank_ids = jnp.arange(leavers, dtype=jnp.int32)
    group_ids = jnp.arange(groups, dtype=jnp.int32)
    my_leave = leaving[own_group]
    my_owner = owner[own_group]
    to_me = owner == own_group
    anchor = jnp.sum(jnp.where(to_me, group_ids[:, None], 0), axis=0)
    anchor_leave = jnp.sum(jnp.where(to_me, leaving, 0), axis=0)
    page_rows = cache.shape[1]
    conv_rows = conv_state.shape[1]
    states = jnp.concatenate([conv_state, lru_state[:, None, :]], axis=1)
    to_group = my_owner[None, :] == group_ids[:, None]
    send_slot = jnp.sum(jnp.where(to_group, my_leave[None, :], 0), axis=1)
    states_send, cache_send = lax.optimization_barrier(
        (
            jnp.take(states, send_slot, axis=0, mode="clip"),
            jnp.take(cache, send_slot, axis=0, mode="clip"),
        )
    )
    got_states = lax.all_to_all(states_send, "req", 0, 0, tiled=True)
    got_cache = lax.all_to_all(cache_send, "req", 0, 0, tiled=True)
    got_states, tokens, lengths = lax.optimization_barrier((got_states, tokens, lengths))
    local_ids = jnp.arange(req_rows, dtype=jnp.int32)
    match_slot = my_leave[None, :] == local_ids[:, None]
    arriving = jnp.any(match_slot, axis=1)
    arrive_from = jnp.sum(jnp.where(match_slot, anchor[None, :], 0), axis=1)
    anchor_slot = jnp.sum(
        jnp.where(match_slot, (anchor * req_rows + anchor_leave)[None, :], 0), axis=1
    )
    moved_states = jnp.where(
        arriving[:, None, None], jnp.take(got_states, arrive_from, axis=0, mode="clip"), states
    )
    moved_cache = jnp.where(
        arriving[:, None, None], jnp.take(got_cache, arrive_from, axis=0, mode="clip"), cache
    )
    moved_conv = moved_states[:, :conv_rows]
    moved_lru = moved_states[:, conv_rows]
    source_slot = jnp.where(arriving, anchor_slot, own_group * req_rows + local_ids)
    position = jnp.take(lengths, source_slot, mode="clip")
    inputs = tokens.astype(jnp.float32)
    normed = rms_norm(inputs, gain_rec)
    branch_in = jnp.dot(normed, w_input, preferred_element_type=jnp.float32).astype(jnp.bfloat16)
    branch = jax.nn.gelu(
        jnp.dot(normed, w_branch, preferred_element_type=jnp.float32), approximate=True
    )
    history = moved_conv.astype(jnp.float32)
    conv_in = (
        jnp.sum(conv_weight[:-1][None] * history, axis=1)
        + conv_weight[-1] * branch_in.astype(jnp.float32)
        + conv_bias
    )
    channels = conv_in.shape[1]
    block_size = gate_weight.shape[2]
    blocks = channels // block_size
    gate_pre = (
        jnp.einsum(
            "snb,gnbc->gsnc",
            conv_in.reshape(req_rows, blocks, block_size),
            gate_weight.astype(jnp.float32),
        ).reshape(2, req_rows, channels)
        + gate_bias[:, None, :]
    )
    rate_gate = jax.nn.sigmoid(gate_pre[0])
    admit_gate = jax.nn.sigmoid(gate_pre[1])
    log_decay = -8.0 * rate_gate * jax.nn.softplus(-decay_param)
    new_state = (
        jnp.exp(log_decay) * moved_lru.astype(jnp.float32)
        + jnp.sqrt(-jnp.expm1(2.0 * log_decay)) * admit_gate * conv_in
    )
    lru_out = new_state.astype(jnp.bfloat16)
    conv_out = jnp.concatenate([moved_conv[:, 1:], branch_in[:, None, :]], axis=1)
    gated_rec = (new_state * branch).astype(jnp.bfloat16)
    resid_one = inputs + across_mlp_narrow(
        jnp.dot(gated_rec, w_rec_out, preferred_element_type=jnp.float32)
    )
    head_size = w_keyval.shape[1] // 2
    heads = width // head_size
    slice_rows = w_query.shape[0]
    normed_att = rms_norm(resid_one, gain_att)
    query_part = jnp.dot(
        lax.dynamic_slice_in_dim(normed_att, mlp_id * slice_rows, slice_rows, 1),
        w_query,
        preferred_element_type=jnp.float32,
    )
    query_full = across_mlp_narrow(query_part)
    where_pos = position.astype(jnp.float32)
    queries = rotate(query_full.reshape(req_rows, heads, head_size), where_pos).astype(jnp.bfloat16)
    key_value = jnp.dot(normed_att, w_keyval, preferred_element_type=jnp.float32)
    key_new = rotate(key_value[:, None, :head_size], where_pos)[:, 0].astype(jnp.bfloat16)
    value_new = key_value[:, head_size:].astype(jnp.bfloat16)
    window = page_rows * lax.axis_size("mlp")
    score_scale = 1.0 / math.sqrt(head_size)
    scores = (
        jnp.einsum(
            "shd,swd->shw",
            queries,
            moved_cache[..., :head_size],
            preferred_element_type=jnp.float32,
        )
        * score_scale
    )
    slot_ids = mlp_id * page_rows + jnp.arange(page_rows, dtype=jnp.int32)[None, :]
    current = position[:, None]
    held_pos = current - 1 - jnp.mod(current - 1 - slot_ids, window)
    usable = ((held_pos >= 0) & (held_pos != current - window))[:, None, :]
    local_top = jnp.max(jnp.where(usable, scores, -1e30), axis=-1)
    weights = jnp.where(usable, jnp.exp(scores - local_top[..., None]), 0.0)
    local_sum = jnp.sum(weights, axis=-1)
    local_acc = jnp.einsum(
        "shw,swd->shd",
        weights.astype(jnp.bfloat16),
        moved_cache[..., head_size:],
        preferred_element_type=jnp.float32,
    )
    acc = local_acc.reshape(req_rows, width)
    top, total = local_top, local_sum
    held = heads
    head_base = jnp.zeros((), jnp.int32)
    for mask, bit in reversed(axis_stages("mlp")):
        if held % 2 == 0 and (held // 2) * head_size >= 2 * slice_rows:
            held = held // 2
            upper = (mlp_id & bit) != 0
            cut = held * head_size
            keep_acc = jnp.where(upper, acc[:, cut:], acc[:, :cut])
            send_acc = jnp.where(upper, acc[:, :cut], acc[:, cut:])
            keep_top = jnp.where(upper, top[:, held:], top[:, :held])
            send_top = jnp.where(upper, top[:, :held], top[:, held:])
            keep_total = jnp.where(upper, total[:, held:], total[:, :held])
            send_total = jnp.where(upper, total[:, :held], total[:, held:])
            head_base = head_base + jnp.where(upper, held, 0)
        else:
            keep_acc = send_acc = acc
            keep_top = send_top = top
            keep_total = send_total = total
        cut = held * head_size
        stat_pad = jnp.zeros((req_rows, head_size - 2 * held), jnp.float32)
        got = partner_swap(
            jnp.concatenate([send_acc, send_top, send_total, stat_pad], axis=1), "mlp", mask
        )
        got_top = got[:, cut : cut + held]
        got_total = got[:, cut + held : cut + 2 * held]
        top = jnp.maximum(keep_top, got_top)
        keep_factor = jnp.exp(keep_top - top)
        got_factor = jnp.exp(got_top - top)
        acc = keep_acc * jnp.repeat(keep_factor, head_size, axis=1) + got[:, :cut] * jnp.repeat(
            got_factor, head_size, axis=1
        )
        total = keep_total * keep_factor + got_total * got_factor
    own_score = (
        jnp.sum(queries.astype(jnp.float32) * key_new.astype(jnp.float32)[:, None, :], axis=-1)
        * score_scale
    )
    own_score = lax.dynamic_slice_in_dim(own_score, head_base, held, 1)
    top_score = jnp.maximum(top, own_score)
    rescale = jnp.exp(top - top_score)
    own_weight = jnp.exp(own_score - top_score)
    own_rounded = lax.optimization_barrier(own_weight.astype(jnp.bfloat16)).astype(jnp.float32)
    denominator = total * rescale + own_weight
    numerator = acc * jnp.repeat(rescale, head_size, axis=1) + jnp.repeat(
        own_rounded, head_size, axis=1
    ) * jnp.tile(value_new.astype(jnp.float32), (1, held))
    attended = (numerator / jnp.repeat(denominator, head_size, axis=1)).astype(jnp.bfloat16)
    attn_part = jnp.dot(
        lax.dynamic_slice_in_dim(
            attended, mlp_id * slice_rows - head_base * head_size, slice_rows, 1
        ),
        w_attn_out,
        preferred_element_type=jnp.float32,
    )
    resid_two = resid_one + across_mlp_narrow(attn_part)
    normed_mlp = rms_norm(resid_two, gain_mlp)
    gate_act = jax.nn.gelu(
        jnp.dot(normed_mlp, w_gate, preferred_element_type=jnp.float32), approximate=True
    )
    hidden = (gate_act * jnp.dot(normed_mlp, w_up, preferred_element_type=jnp.float32)).astype(
        jnp.bfloat16
    )
    down_part = jnp.dot(hidden, w_down, preferred_element_type=jnp.float32)
    share = scatter_sum(down_part, "mlp")
    share_cols = share.shape[1]
    hidden_out = (
        lax.dynamic_slice_in_dim(resid_two, mlp_id * share_cols, share_cols, 1) + share
    ).astype(jnp.bfloat16)
    write_row = jnp.concatenate([key_new, value_new], axis=-1)
    row_hit = slot_ids == jnp.mod(current, window)
    cache_out = jnp.where(row_hit[:, :, None], write_row[:, None, :], moved_cache)
    return (hidden_out, cache_out, conv_out, lru_out)


def solution(mesh):
    placed = (
        P("req", None),
        P(),
        P(),
        P(),
        P("req", "mlp", None),
        P("req", None, "mlp"),
        P("req", "mlp"),
        P(),
        P(None, "mlp"),
        P(None, "mlp"),
        P(None, "mlp"),
        P("mlp"),
        P(None, "mlp", None, None),
        P(None, "mlp"),
        P("mlp"),
        P("mlp", None),
        P(),
        P("mlp", None),
        P(),
        P("mlp", None),
        P(),
        P(None, "mlp"),
        P(None, "mlp"),
        P("mlp", None),
    )
    return jax.shard_map(
        per_device,
        mesh=mesh,
        in_specs=placed,
        out_specs=(P("req", "mlp"), P("req", "mlp", None), P("req", None, "mlp"), P("req", "mlp")),
        check_vma=False,
    )
```

```python
import math

import jax
import jax.numpy as jnp
from jax import lax
from jax.sharding import PartitionSpec as P

epsilon = 1e-06


def partner_swap(value, axis, bit):
    size = lax.axis_size(axis)
    pairs = [(j, j ^ bit) for j in range(size)]
    return jax.tree.map(lambda part: lax.ppermute(part, axis, pairs), value)


def axis_bits(axis):
    size = lax.axis_size(axis)
    assert size & (size - 1) == 0
    bits = []
    bit = 1
    while bit < size:
        bits.append(bit)
        bit *= 2
    return bits


def axis_stages(axis):
    stages = []
    for bit in axis_bits(axis):
        mask = bit | (bit // 2) if bit == 2 else bit
        stages.append((mask, bit))
    return stages


def joined(value, axis, join):
    for mask, _ in axis_stages(axis):
        value = join(value, partner_swap(value, axis, mask))
    return value


def scatter_sum(value, axis):
    me = lax.axis_index(axis)
    held = value
    for mask, bit in reversed(axis_stages(axis)):
        half = held.shape[1] // 2
        lower, upper = held[:, :half], held[:, half:]
        mine_upper = (me & bit) != 0
        keep = jnp.where(mine_upper, upper, lower)
        send = jnp.where(mine_upper, lower, upper)
        held = keep + partner_swap(send.astype(jnp.bfloat16), axis, mask).astype(jnp.float32)
    return held


def rms_norm(values, gain_vec):
    mean_square = jnp.mean(values * values, axis=-1, keepdims=True)
    return (values * lax.rsqrt(mean_square + epsilon) * gain_vec).astype(jnp.bfloat16)


def rotate(vectors, positions):
    half_size = vectors.shape[-1] // 2
    frequency = 10000.0 ** (-2.0 * jnp.arange(half_size, dtype=jnp.float32) / vectors.shape[-1])
    angles = positions[:, None] * frequency[None, :]
    cos_part = jnp.cos(angles)[:, None, :]
    sin_part = jnp.sin(angles)[:, None, :]
    first_half = vectors[..., :half_size]
    second = vectors[..., half_size:]
    return jnp.concatenate(
        [first_half * cos_part - second * sin_part, second * cos_part + first_half * sin_part],
        axis=-1,
    )


def combine_parts(first_part, second_part):
    width = first_part.shape[-1] - 128
    heads = width // 128
    first_top, first_sum = first_part[:, width : width + heads], first_part[:, width + heads : width + 2 * heads]
    second_top = second_part[:, width : width + heads]
    second_sum = second_part[:, width + heads : width + 2 * heads]
    larger = jnp.maximum(first_top, second_top)
    first_factor = jnp.exp(first_top - larger)
    second_factor = jnp.exp(second_top - larger)
    rows = first_part.shape[0]
    head_size = width // heads
    acc = (
        first_part[:, :width].reshape(rows, heads, head_size) * first_factor[..., None]
        + second_part[:, :width].reshape(rows, heads, head_size) * second_factor[..., None]
    )
    stats = jnp.concatenate(
        [larger, first_sum * first_factor + second_sum * second_factor, first_part[:, width + 2 * heads :]],
        axis=-1,
    )
    return jnp.concatenate([acc.reshape(rows, width), stats], axis=-1)


def across_mlp(partial_value):
    return joined(partial_value, "mlp", lambda first, second: first + second)


def across_mlp_narrow(partial_value):
    for mask, _ in axis_stages("mlp"):
        sent = partner_swap(partial_value.astype(jnp.bfloat16), "mlp", mask)
        partial_value = partial_value + sent.astype(jnp.float32)
    return partial_value


def per_device(
    tokens,
    lengths,
    leaving,
    owner,
    cache,
    conv_state,
    lru_state,
    gain_rec,
    w_input,
    w_branch,
    conv_weight,
    conv_bias,
    gate_weight,
    gate_bias,
    decay_param,
    w_rec_out,
    gain_att,
    w_query,
    w_keyval,
    w_attn_out,
    gain_mlp,
    w_gate,
    w_up,
    w_down,
):
    req_rows = tokens.shape[0]
    width = tokens.shape[1]
    leavers = leaving.shape[1]
    groups = lax.axis_size("req")
    own_group = lax.axis_index("req")
    mlp_id = lax.axis_index("mlp")
    rank_ids = jnp.arange(leavers, dtype=jnp.int32)
    group_ids = jnp.arange(groups, dtype=jnp.int32)
    my_leave = leaving[own_group]
    my_owner = owner[own_group]
    to_me = owner == own_group
    anchor = jnp.sum(jnp.where(to_me, group_ids[:, None], 0), axis=0)
    anchor_leave = jnp.sum(jnp.where(to_me, leaving, 0), axis=0)
    page_rows = cache.shape[1]
    conv_rows = conv_state.shape[1]
    states = jnp.concatenate([conv_state, lru_state[:, None, :]], axis=1)
    to_group = my_owner[None, :] == group_ids[:, None]
    send_slot = jnp.sum(jnp.where(to_group, my_leave[None, :], 0), axis=1)
    got_states = lax.all_to_all(
        jnp.take(states, send_slot, axis=0, mode="clip"), "req", 0, 0, tiled=True
    )
    got_cache = lax.all_to_all(
        jnp.take(cache, send_slot, axis=0, mode="clip"), "req", 0, 0, tiled=True
    )
    got_states, tokens, lengths = lax.optimization_barrier((got_states, tokens, lengths))
    local_ids = jnp.arange(req_rows, dtype=jnp.int32)
    match_slot = my_leave[None, :] == local_ids[:, None]
    arriving = jnp.any(match_slot, axis=1)
    arrive_from = jnp.sum(jnp.where(match_slot, anchor[None, :], 0), axis=1)
    anchor_slot = jnp.sum(
        jnp.where(match_slot, (anchor * req_rows + anchor_leave)[None, :], 0), axis=1
    )
    moved_states = jnp.where(
        arriving[:, None, None], jnp.take(got_states, arrive_from, axis=0, mode="clip"), states
    )
    moved_cache = jnp.where(
        arriving[:, None, None], jnp.take(got_cache, arrive_from, axis=0, mode="clip"), cache
    )
    moved_conv = moved_states[:, :conv_rows]
    moved_lru = moved_states[:, conv_rows]
    source_slot = jnp.where(arriving, anchor_slot, own_group * req_rows + local_ids)
    position = jnp.take(lengths, source_slot, mode="clip")
    inputs = tokens.astype(jnp.float32)
    normed = rms_norm(inputs, gain_rec)
    branch_in = jnp.dot(normed, w_input, preferred_element_type=jnp.float32).astype(jnp.bfloat16)
    branch = jax.nn.gelu(
        jnp.dot(normed, w_branch, preferred_element_type=jnp.float32), approximate=True
    )
    history = moved_conv.astype(jnp.float32)
    conv_in = (
        jnp.sum(conv_weight[:-1][None] * history, axis=1)
        + conv_weight[-1] * branch_in.astype(jnp.float32)
        + conv_bias
    )
    channels = conv_in.shape[1]
    block_size = gate_weight.shape[2]
    blocks = channels // block_size
    gate_pre = (
        jnp.einsum(
            "snb,gnbc->gsnc",
            conv_in.reshape(req_rows, blocks, block_size),
            gate_weight.astype(jnp.float32),
        ).reshape(2, req_rows, channels)
        + gate_bias[:, None, :]
    )
    rate_gate = jax.nn.sigmoid(gate_pre[0])
    admit_gate = jax.nn.sigmoid(gate_pre[1])
    log_decay = -8.0 * rate_gate * jax.nn.softplus(-decay_param)
    new_state = (
        jnp.exp(log_decay) * moved_lru.astype(jnp.float32)
        + jnp.sqrt(-jnp.expm1(2.0 * log_decay)) * admit_gate * conv_in
    )
    lru_out = new_state.astype(jnp.bfloat16)
    conv_out = jnp.concatenate([moved_conv[:, 1:], branch_in[:, None, :]], axis=1)
    gated_rec = (new_state * branch).astype(jnp.bfloat16)
    resid_one = inputs + across_mlp_narrow(
        jnp.dot(gated_rec, w_rec_out, preferred_element_type=jnp.float32)
    )
    head_size = w_keyval.shape[1] // 2
    heads = width // head_size
    slice_rows = w_query.shape[0]
    normed_att = rms_norm(resid_one, gain_att)
    query_part = jnp.dot(
        lax.dynamic_slice_in_dim(normed_att, mlp_id * slice_rows, slice_rows, 1),
        w_query,
        preferred_element_type=jnp.float32,
    )
    query_full = across_mlp_narrow(query_part)
    where_pos = position.astype(jnp.float32)
    queries = rotate(query_full.reshape(req_rows, heads, head_size), where_pos).astype(jnp.bfloat16)
    key_value = jnp.dot(normed_att, w_keyval, preferred_element_type=jnp.float32)
    key_new = rotate(key_value[:, None, :head_size], where_pos)[:, 0].astype(jnp.bfloat16)
    value_new = key_value[:, head_size:].astype(jnp.bfloat16)
    window = page_rows * lax.axis_size("mlp")
    score_scale = 1.0 / math.sqrt(head_size)
    scores = (
        jnp.einsum(
            "shd,swd->shw",
            queries,
            moved_cache[..., :head_size],
            preferred_element_type=jnp.float32,
        )
        * score_scale
    )
    slot_ids = mlp_id * page_rows + jnp.arange(page_rows, dtype=jnp.int32)[None, :]
    current = position[:, None]
    held_pos = current - 1 - jnp.mod(current - 1 - slot_ids, window)
    usable = ((held_pos >= 0) & (held_pos != current - window))[:, None, :]
    local_top = jnp.max(jnp.where(usable, scores, -1e30), axis=-1)
    weights = jnp.where(usable, jnp.exp(scores - local_top[..., None]), 0.0)
    local_sum = jnp.sum(weights, axis=-1)
    local_acc = jnp.einsum(
        "shw,swd->shd",
        weights.astype(jnp.bfloat16),
        moved_cache[..., head_size:],
        preferred_element_type=jnp.float32,
    )
    acc = local_acc.reshape(req_rows, width)
    top, total = local_top, local_sum
    held = heads
    head_base = jnp.zeros((), jnp.int32)
    for mask, bit in reversed(axis_stages("mlp")):
        if held % 2 == 0 and (held // 2) * head_size >= 2 * slice_rows:
            held = held // 2
            upper = (mlp_id & bit) != 0
            cut = held * head_size
            keep_acc = jnp.where(upper, acc[:, cut:], acc[:, :cut])
            send_acc = jnp.where(upper, acc[:, :cut], acc[:, cut:])
            keep_top = jnp.where(upper, top[:, held:], top[:, :held])
            send_top = jnp.where(upper, top[:, :held], top[:, held:])
            keep_total = jnp.where(upper, total[:, held:], total[:, :held])
            send_total = jnp.where(upper, total[:, :held], total[:, held:])
            head_base = head_base + jnp.where(upper, held, 0)
        else:
            keep_acc = send_acc = acc
            keep_top = send_top = top
            keep_total = send_total = total
        cut = held * head_size
        stat_pad = jnp.zeros((req_rows, head_size - 2 * held), jnp.float32)
        got = partner_swap(
            jnp.concatenate([send_acc, send_top, send_total, stat_pad], axis=1), "mlp", mask
        )
        got_top = got[:, cut : cut + held]
        got_total = got[:, cut + held : cut + 2 * held]
        top = jnp.maximum(keep_top, got_top)
        keep_factor = jnp.exp(keep_top - top)
        got_factor = jnp.exp(got_top - top)
        acc = keep_acc * jnp.repeat(keep_factor, head_size, axis=1) + got[:, :cut] * jnp.repeat(
            got_factor, head_size, axis=1
        )
        total = keep_total * keep_factor + got_total * got_factor
    own_score = (
        jnp.sum(queries.astype(jnp.float32) * key_new.astype(jnp.float32)[:, None, :], axis=-1)
        * score_scale
    )
    own_score = lax.dynamic_slice_in_dim(own_score, head_base, held, 1)
    top_score = jnp.maximum(top, own_score)
    rescale = jnp.exp(top - top_score)
    own_weight = jnp.exp(own_score - top_score)
    own_rounded = lax.optimization_barrier(own_weight.astype(jnp.bfloat16)).astype(jnp.float32)
    denominator = total * rescale + own_weight
    numerator = acc * jnp.repeat(rescale, head_size, axis=1) + jnp.repeat(
        own_rounded, head_size, axis=1
    ) * jnp.tile(value_new.astype(jnp.float32), (1, held))
    attended = (numerator / jnp.repeat(denominator, head_size, axis=1)).astype(jnp.bfloat16)
    attn_part = jnp.dot(
        lax.dynamic_slice_in_dim(
            attended, mlp_id * slice_rows - head_base * head_size, slice_rows, 1
        ),
        w_attn_out,
        preferred_element_type=jnp.float32,
    )
    resid_two = resid_one + across_mlp_narrow(attn_part)
    normed_mlp = rms_norm(resid_two, gain_mlp)
    gate_act = jax.nn.gelu(
        jnp.dot(normed_mlp, w_gate, preferred_element_type=jnp.float32), approximate=True
    )
    hidden = (gate_act * jnp.dot(normed_mlp, w_up, preferred_element_type=jnp.float32)).astype(
        jnp.bfloat16
    )
    down_part = jnp.dot(hidden, w_down, preferred_element_type=jnp.float32)
    share = scatter_sum(down_part, "mlp")
    share_cols = share.shape[1]
    hidden_out = (
        lax.dynamic_slice_in_dim(resid_two, mlp_id * share_cols, share_cols, 1) + share
    ).astype(jnp.bfloat16)
    write_row = jnp.concatenate([key_new, value_new], axis=-1)
    row_hit = slot_ids == jnp.mod(current, window)
    cache_out = jnp.where(row_hit[:, :, None], write_row[:, None, :], moved_cache)
    return (hidden_out, cache_out, conv_out, lru_out)


def solution(mesh):
    placed = (
        P("req", None),
        P(),
        P(),
        P(),
        P("req", "mlp", None),
        P("req", None, "mlp"),
        P("req", "mlp"),
        P(),
        P(None, "mlp"),
        P(None, "mlp"),
        P(None, "mlp"),
        P("mlp"),
        P(None, "mlp", None, None),
        P(None, "mlp"),
        P("mlp"),
        P("mlp", None),
        P(),
        P("mlp", None),
        P(),
        P("mlp", None),
        P(),
        P(None, "mlp"),
        P(None, "mlp"),
        P("mlp", None),
    )
    return jax.shard_map(
        per_device,
        mesh=mesh,
        in_specs=placed,
        out_specs=(P("req", "mlp"), P("req", "mlp", None), P("req", None, "mlp"), P("req", "mlp")),
        check_vma=False,
    )
```

```python
import math

import jax
import jax.numpy as jnp
from jax import lax
from jax.sharding import PartitionSpec as P

epsilon = 1e-06


def partner_swap(value, axis, bit):
    size = lax.axis_size(axis)
    pairs = [(j, j ^ bit) for j in range(size)]
    return jax.tree.map(lambda part: lax.ppermute(part, axis, pairs), value)


def axis_bits(axis):
    size = lax.axis_size(axis)
    assert size & (size - 1) == 0
    bits = []
    bit = 1
    while bit < size:
        bits.append(bit)
        bit *= 2
    return bits


def axis_stages(axis):
    stages = []
    for bit in axis_bits(axis):
        mask = bit | (bit // 2) if bit == 2 else bit
        stages.append((mask, bit))
    return stages


def joined(value, axis, join):
    for mask, _ in axis_stages(axis):
        value = join(value, partner_swap(value, axis, mask))
    return value


def scatter_sum(value, axis):
    me = lax.axis_index(axis)
    held = value
    for mask, bit in reversed(axis_stages(axis)):
        half = held.shape[1] // 2
        lower, upper = held[:, :half], held[:, half:]
        mine_upper = (me & bit) != 0
        keep = jnp.where(mine_upper, upper, lower)
        send = jnp.where(mine_upper, lower, upper)
        held = keep + partner_swap(send.astype(jnp.bfloat16), axis, mask).astype(jnp.float32)
    return held


def rms_norm(values, gain_vec):
    mean_square = jnp.mean(values * values, axis=-1, keepdims=True)
    return (values * lax.rsqrt(mean_square + epsilon) * gain_vec).astype(jnp.bfloat16)


def rotate(vectors, positions):
    half_size = vectors.shape[-1] // 2
    frequency = 10000.0 ** (-2.0 * jnp.arange(half_size, dtype=jnp.float32) / vectors.shape[-1])
    angles = positions[:, None] * frequency[None, :]
    cos_part = jnp.cos(angles)[:, None, :]
    sin_part = jnp.sin(angles)[:, None, :]
    first_half = vectors[..., :half_size]
    second = vectors[..., half_size:]
    return jnp.concatenate(
        [first_half * cos_part - second * sin_part, second * cos_part + first_half * sin_part],
        axis=-1,
    )


def combine_parts(first_part, second_part):
    width = first_part.shape[-1] - 128
    heads = width // 128
    first_top, first_sum = first_part[:, width : width + heads], first_part[:, width + heads : width + 2 * heads]
    second_top = second_part[:, width : width + heads]
    second_sum = second_part[:, width + heads : width + 2 * heads]
    larger = jnp.maximum(first_top, second_top)
    first_factor = jnp.exp(first_top - larger)
    second_factor = jnp.exp(second_top - larger)
    rows = first_part.shape[0]
    head_size = width // heads
    acc = (
        first_part[:, :width].reshape(rows, heads, head_size) * first_factor[..., None]
        + second_part[:, :width].reshape(rows, heads, head_size) * second_factor[..., None]
    )
    stats = jnp.concatenate(
        [larger, first_sum * first_factor + second_sum * second_factor, first_part[:, width + 2 * heads :]],
        axis=-1,
    )
    return jnp.concatenate([acc.reshape(rows, width), stats], axis=-1)


def across_mlp(partial_value):
    return joined(partial_value, "mlp", lambda first, second: first + second)


def across_mlp_narrow(partial_value):
    for mask, _ in axis_stages("mlp"):
        sent = partner_swap(partial_value.astype(jnp.bfloat16), "mlp", mask)
        partial_value = partial_value + sent.astype(jnp.float32)
    return partial_value


def per_device(
    tokens,
    lengths,
    leaving,
    owner,
    cache,
    conv_state,
    lru_state,
    gain_rec,
    w_input,
    w_branch,
    conv_weight,
    conv_bias,
    gate_weight,
    gate_bias,
    decay_param,
    w_rec_out,
    gain_att,
    w_query,
    w_keyval,
    w_attn_out,
    gain_mlp,
    w_gate,
    w_up,
    w_down,
):
    req_rows = tokens.shape[0]
    width = tokens.shape[1]
    leavers = leaving.shape[1]
    groups = lax.axis_size("req")
    own_group = lax.axis_index("req")
    mlp_id = lax.axis_index("mlp")
    rank_ids = jnp.arange(leavers, dtype=jnp.int32)
    group_ids = jnp.arange(groups, dtype=jnp.int32)
    my_leave = leaving[own_group]
    my_owner = owner[own_group]
    to_me = owner == own_group
    anchor = jnp.sum(jnp.where(to_me, group_ids[:, None], 0), axis=0)
    anchor_leave = jnp.sum(jnp.where(to_me, leaving, 0), axis=0)
    page_rows = cache.shape[1]
    conv_rows = conv_state.shape[1]
    states = jnp.concatenate([conv_state, lru_state[:, None, :]], axis=1)
    to_group = my_owner[None, :] == group_ids[:, None]
    send_slot = jnp.sum(jnp.where(to_group, my_leave[None, :], 0), axis=1)
    got_states = lax.all_to_all(
        jnp.take(states, send_slot, axis=0, mode="clip"), "req", 0, 0, tiled=True
    )
    got_cache = lax.all_to_all(
        jnp.take(cache, send_slot, axis=0, mode="clip"), "req", 0, 0, tiled=True
    )
    got_states, tokens, lengths = lax.optimization_barrier((got_states, tokens, lengths))
    local_ids = jnp.arange(req_rows, dtype=jnp.int32)
    match_slot = my_leave[None, :] == local_ids[:, None]
    arriving = jnp.any(match_slot, axis=1)
    arrive_from = jnp.sum(jnp.where(match_slot, anchor[None, :], 0), axis=1)
    anchor_slot = jnp.sum(
        jnp.where(match_slot, (anchor * req_rows + anchor_leave)[None, :], 0), axis=1
    )
    moved_states = jnp.where(
        arriving[:, None, None], jnp.take(got_states, arrive_from, axis=0, mode="clip"), states
    )
    moved_cache = jnp.where(
        arriving[:, None, None], jnp.take(got_cache, arrive_from, axis=0, mode="clip"), cache
    )
    moved_conv = moved_states[:, :conv_rows]
    moved_lru = moved_states[:, conv_rows]
    source_slot = jnp.where(arriving, anchor_slot, own_group * req_rows + local_ids)
    position = jnp.take(lengths, source_slot, mode="clip")
    inputs = tokens.astype(jnp.float32)
    normed = rms_norm(inputs, gain_rec)
    branch_in = jnp.dot(normed, w_input, preferred_element_type=jnp.float32).astype(jnp.bfloat16)
    branch = jax.nn.gelu(
        jnp.dot(normed, w_branch, preferred_element_type=jnp.float32), approximate=True
    )
    history = moved_conv.astype(jnp.float32)
    conv_in = (
        jnp.sum(conv_weight[:-1][None] * history, axis=1)
        + conv_weight[-1] * branch_in.astype(jnp.float32)
        + conv_bias
    )
    channels = conv_in.shape[1]
    block_size = gate_weight.shape[2]
    blocks = channels // block_size
    gate_pre = (
        jnp.einsum(
            "snb,gnbc->gsnc",
            conv_in.reshape(req_rows, blocks, block_size),
            gate_weight.astype(jnp.float32),
        ).reshape(2, req_rows, channels)
        + gate_bias[:, None, :]
    )
    rate_gate = jax.nn.sigmoid(gate_pre[0])
    admit_gate = jax.nn.sigmoid(gate_pre[1])
    log_decay = -8.0 * rate_gate * jax.nn.softplus(-decay_param)
    new_state = (
        jnp.exp(log_decay) * moved_lru.astype(jnp.float32)
        + jnp.sqrt(-jnp.expm1(2.0 * log_decay)) * admit_gate * conv_in
    )
    lru_out = new_state.astype(jnp.bfloat16)
    conv_out = jnp.concatenate([moved_conv[:, 1:], branch_in[:, None, :]], axis=1)
    gated_rec = (new_state * branch).astype(jnp.bfloat16)
    resid_one = inputs + across_mlp_narrow(
        jnp.dot(gated_rec, w_rec_out, preferred_element_type=jnp.float32)
    )
    head_size = w_keyval.shape[1] // 2
    heads = width // head_size
    slice_rows = w_query.shape[0]
    normed_att = rms_norm(resid_one, gain_att)
    query_part = jnp.dot(
        lax.dynamic_slice_in_dim(normed_att, mlp_id * slice_rows, slice_rows, 1),
        w_query,
        preferred_element_type=jnp.float32,
    )
    query_full = across_mlp_narrow(query_part)
    where_pos = position.astype(jnp.float32)
    queries = rotate(query_full.reshape(req_rows, heads, head_size), where_pos).astype(jnp.bfloat16)
    key_value = jnp.dot(normed_att, w_keyval, preferred_element_type=jnp.float32)
    key_new = rotate(key_value[:, None, :head_size], where_pos)[:, 0].astype(jnp.bfloat16)
    value_new = key_value[:, head_size:].astype(jnp.bfloat16)
    window = page_rows * lax.axis_size("mlp")
    score_scale = 1.0 / math.sqrt(head_size)
    scores = (
        jnp.einsum(
            "shd,swd->shw",
            queries,
            moved_cache[..., :head_size],
            preferred_element_type=jnp.float32,
        )
        * score_scale
    )
    slot_ids = mlp_id * page_rows + jnp.arange(page_rows, dtype=jnp.int32)[None, :]
    current = position[:, None]
    held_pos = current - 1 - jnp.mod(current - 1 - slot_ids, window)
    usable = ((held_pos >= 0) & (held_pos != current - window))[:, None, :]
    local_top = jnp.max(jnp.where(usable, scores, -1e30), axis=-1)
    weights = jnp.where(usable, jnp.exp(scores - local_top[..., None]), 0.0)
    local_sum = jnp.sum(weights, axis=-1)
    local_acc = jnp.einsum(
        "shw,swd->shd",
        weights.astype(jnp.bfloat16),
        moved_cache[..., head_size:],
        preferred_element_type=jnp.float32,
    )
    acc = local_acc.reshape(req_rows, width)
    top, total = local_top, local_sum
    held = heads
    head_base = jnp.zeros((), jnp.int32)
    column_half = None

    def spread(per_head):
        cols = jnp.repeat(per_head, head_size, axis=1)
        if column_half is None:
            return cols
        return jnp.where(column_half, cols[:, slice_rows:], cols[:, :slice_rows])

    for mask, bit in reversed(axis_stages("mlp")):
        if held % 2 == 0 and (held // 2) * head_size >= 2 * slice_rows:
            held = held // 2
            upper = (mlp_id & bit) != 0
            cut = held * head_size
            keep_acc = jnp.where(upper, acc[:, cut:], acc[:, :cut])
            send_acc = jnp.where(upper, acc[:, :cut], acc[:, cut:])
            keep_top = jnp.where(upper, top[:, held:], top[:, :held])
            send_top = jnp.where(upper, top[:, :held], top[:, held:])
            keep_total = jnp.where(upper, total[:, held:], total[:, :held])
            send_total = jnp.where(upper, total[:, :held], total[:, held:])
            head_base = head_base + jnp.where(upper, held, 0)
        else:
            keep_top = send_top = top
            keep_total = send_total = total
            if column_half is None and acc.shape[1] == 2 * slice_rows:
                column_half = (mlp_id & bit) != 0
                keep_acc = jnp.where(column_half, acc[:, slice_rows:], acc[:, :slice_rows])
                send_acc = jnp.where(column_half, acc[:, :slice_rows], acc[:, slice_rows:])
            else:
                keep_acc = send_acc = acc
        cut = keep_acc.shape[1]
        stat_pad = jnp.zeros((req_rows, head_size - 2 * held), jnp.float32)
        got = partner_swap(
            jnp.concatenate([send_acc, send_top, send_total, stat_pad], axis=1), "mlp", mask
        )
        got_top = got[:, cut : cut + held]
        got_total = got[:, cut + held : cut + 2 * held]
        top = jnp.maximum(keep_top, got_top)
        keep_factor = jnp.exp(keep_top - top)
        got_factor = jnp.exp(got_top - top)
        acc = keep_acc * spread(keep_factor) + got[:, :cut] * spread(got_factor)
        total = keep_total * keep_factor + got_total * got_factor
    own_score = (
        jnp.sum(queries.astype(jnp.float32) * key_new.astype(jnp.float32)[:, None, :], axis=-1)
        * score_scale
    )
    own_score = lax.dynamic_slice_in_dim(own_score, head_base, held, 1)
    top_score = jnp.maximum(top, own_score)
    rescale = jnp.exp(top - top_score)
    own_weight = jnp.exp(own_score - top_score)
    own_rounded = lax.optimization_barrier(own_weight.astype(jnp.bfloat16)).astype(jnp.float32)
    denominator = total * rescale + own_weight
    values_tiled = jnp.tile(value_new.astype(jnp.float32), (1, held))
    values_tiled = jnp.where(
        column_half, values_tiled[:, slice_rows:], values_tiled[:, :slice_rows]
    )
    numerator = acc * spread(rescale) + spread(own_rounded) * values_tiled
    attended = (numerator / spread(denominator)).astype(jnp.bfloat16)
    attn_part = jnp.dot(attended, w_attn_out, preferred_element_type=jnp.float32)
    resid_two = resid_one + across_mlp_narrow(attn_part)
    normed_mlp = rms_norm(resid_two, gain_mlp)
    gate_act = jax.nn.gelu(
        jnp.dot(normed_mlp, w_gate, preferred_element_type=jnp.float32), approximate=True
    )
    hidden = (gate_act * jnp.dot(normed_mlp, w_up, preferred_element_type=jnp.float32)).astype(
        jnp.bfloat16
    )
    down_part = jnp.dot(hidden, w_down, preferred_element_type=jnp.float32)
    share = scatter_sum(down_part, "mlp")
    share_cols = share.shape[1]
    hidden_out = (
        lax.dynamic_slice_in_dim(resid_two, mlp_id * share_cols, share_cols, 1) + share
    ).astype(jnp.bfloat16)
    write_row = jnp.concatenate([key_new, value_new], axis=-1)
    row_hit = slot_ids == jnp.mod(current, window)
    cache_out = jnp.where(row_hit[:, :, None], write_row[:, None, :], moved_cache)
    return (hidden_out, cache_out, conv_out, lru_out)


def solution(mesh):
    placed = (
        P("req", None),
        P(),
        P(),
        P(),
        P("req", "mlp", None),
        P("req", None, "mlp"),
        P("req", "mlp"),
        P(),
        P(None, "mlp"),
        P(None, "mlp"),
        P(None, "mlp"),
        P("mlp"),
        P(None, "mlp", None, None),
        P(None, "mlp"),
        P("mlp"),
        P("mlp", None),
        P(),
        P("mlp", None),
        P(),
        P("mlp", None),
        P(),
        P(None, "mlp"),
        P(None, "mlp"),
        P("mlp", None),
    )
    return jax.shard_map(
        per_device,
        mesh=mesh,
        in_specs=placed,
        out_specs=(P("req", "mlp"), P("req", "mlp", None), P("req", None, "mlp"), P("req", "mlp")),
        check_vma=False,
    )
```
